32 devices in a mesh: groups: 2 (over x), seq: 4 (over y, core), pair: 4 (over z).
Axes of the slice: x: 2, y: 2, z: 4, core: 2. Of those that a mesh axis runs over, the one named last changes fastest.
Arguments:
- sequence: bfloat16 [4096, 1536], P(('groups', 'seq', 'pair')), parts along dimension 0, may hold values from -12 to 12
- gain_conv: float32 [1536], replicated, may hold values from 0.25 to 1.75
- conv_weight: bfloat16 [5, 1536, 1536], P(None, 'pair'), may hold values from -0.0625 to 0.0625
- gain_attn: float32 [1536], replicated, may hold values from 0.25 to 1.75
- w_qkv: bfloat16 [1536, 3072], P(None, 'pair'), may hold values from -1 to 1
- w_out: bfloat16 [1024, 1536], P('pair'), may hold values from -0.75 to 0.75
- gain_pool: float32 [1536], replicated, may hold values from 0.25 to 1.75
- w_pair: bfloat16 [1536, 256], replicated, may hold values from -0.15625 to 0.15625
- w_up: bfloat16 [128, 256], replicated, may hold values from -0.5 to 0.5
- w_down: bfloat16 [256, 128], replicated, may hold values from -0.375 to 0.375
Outputs:
- seq_out: bfloat16 [4096, 1536], P(('groups', 'seq', 'pair')), parts along dimension 0
- pair_map: bfloat16 [256, 128, 128], P(('groups', 'seq'), 'pair'), parts along dimension 0
The draws below stay inside these ranges and needn't reach their ends.
There are 2 independent parts, one for each index of `groups`. The reference program is written for one: setup_inputs(seed, part) draws one part's arguments, and reference() takes and returns one part's arrays. A program takes and returns all parts, laid end to end along the dimension named above; an argument that names none is the same for every part. Nothing has to cross between parts.
All inputs are finite; a program needn't handle non-finite values.
Results may differ from the reference program's by a relative error of at most 0.024.
Values may be sent and summed in bfloat16 or wider, within the bound.
No kernel may reach another device: no remote copies, remote signals or barrier semaphores. Data moves between devices by JAX's collectives and lax.ppermute only.
A program may use at most 64 MiB of HBM per device.

```python
import math
import jax
import jax.numpy as jnp
from jax import lax

CHANNELS = 1536
HEADS = 8
KEY_SIZE = 128
VALUE_SIZE = 128
TAPS = 5
DILATION = 4
POOL = 16
PAIR_CH = 128
PAIR_HIDDEN = 256
SEQ_LEN = 2048
BINS = 128
RIM = 8


def draw_sequence(key, part):
    first_key = jax.random.fold_in(jax.random.fold_in(key, 11), 0)
    drawn = jnp.clip(jax.random.normal(first_key, (SEQ_LEN, CHANNELS), jnp.float32), -6.0, 6.0)
    return drawn.astype(jnp.bfloat16)


def draw_w_qkv(key, part):
    first_key, second_key, third_key = jax.random.split(jax.random.fold_in(key, 23), 3)
    inverse = 1.0 / math.sqrt(CHANNELS)
    query_w = jax.random.normal(first_key, (CHANNELS, HEADS, KEY_SIZE), jnp.float32) * (1.5 * inverse)
    key_w = jax.random.normal(second_key, (CHANNELS, HEADS, KEY_SIZE), jnp.float32) * (1.5 * inverse)
    value_w = jax.random.normal(third_key, (CHANNELS, HEADS, VALUE_SIZE), jnp.float32) * inverse
    joined = jnp.concatenate([query_w, key_w, value_w], axis=-1)
    joined = jnp.clip(joined, -1.0, 1.0)
    return joined.reshape(CHANNELS, HEADS * (2 * KEY_SIZE + VALUE_SIZE)).astype(jnp.bfloat16)


def steps_of(key, extent, cuts, low, top_value):
    factor_of = 1.0
    for dim, blocks in cuts:
        steps = jax.random.uniform(jax.random.fold_in(jax.random.fold_in(key, 6), dim), (blocks,), jnp.float32, low / len(cuts), top_value / len(cuts))
        factor_of = factor_of * jnp.repeat(jnp.exp(steps), extent[dim] // blocks).reshape((-1,) + (1,) * (len(extent) - 1 - dim))
    return factor_of


def bell_draw(rng, shape, spread, reach, cuts=(), kind=jnp.bfloat16):
    values = jax.random.normal(rng, shape, jnp.float32) * spread
    if len(cuts) > 0:
        values = steps_of(rng, shape, cuts, -0.22, 0.18) * values
    return jnp.clip(values, min=-reach, max=reach).astype(kind)


def setup_inputs(seed: int = 0, part: int = 0) -> dict:
    streams_of = jax.random.split(jax.random.key(seed), 11)
    own_keys = jax.random.split(jax.random.fold_in(streams_of[10], part), 11)
    sequence = draw_sequence(jax.random.fold_in(jax.random.fold_in(streams_of[10], part), 71), part)
    gain_conv = jnp.clip(1.0 + 0.15 * jax.random.normal(streams_of[1], (CHANNELS,), jnp.float32), 0.25, 1.75)
    conv_weight = bell_draw(streams_of[2], (TAPS, CHANNELS, CHANNELS), (TAPS * CHANNELS) ** -0.5, 0.0625, ((1, 4),))
    gain_attn = jnp.clip(1.0 + 0.15 * jax.random.normal(streams_of[3], (CHANNELS,), jnp.float32), 0.25, 1.75)
    w_qkv = draw_w_qkv(jax.random.fold_in(streams_of[10], 71), part)
    w_out = bell_draw(streams_of[5], (HEADS * VALUE_SIZE, CHANNELS), (HEADS * VALUE_SIZE // 16) ** -0.5, 0.75, ((0, 4),))
    gain_pool = jnp.clip(1.0 + 0.15 * jax.random.normal(streams_of[6], (CHANNELS,), jnp.float32), 0.25, 1.75)
    w_pair = bell_draw(streams_of[7], (CHANNELS, 2 * PAIR_CH), CHANNELS ** -0.5, 0.15625)
    w_up = bell_draw(streams_of[8], (PAIR_CH, PAIR_HIDDEN), PAIR_CH ** -0.5, 0.5)
    w_down = bell_draw(streams_of[9], (PAIR_HIDDEN, PAIR_CH), PAIR_HIDDEN ** -0.5, 0.375)
    return dict(sequence=sequence, gain_conv=gain_conv, conv_weight=conv_weight, gain_attn=gain_attn, w_qkv=w_qkv, w_out=w_out, gain_pool=gain_pool, w_pair=w_pair, w_up=w_up, w_down=w_down)


EPS = 1e-06

def norm_rows(values, gain):
    return values * lax.rsqrt(lax.optimization_barrier(jnp.mean(values * values, axis=-1, keepdims=True)) + EPS) * gain

def attend_head(operands):
    queries, key_rows, value_rows = operands
    block_rows = math.gcd(SEQ_LEN, 512)
    scale = 1.0 / math.sqrt(KEY_SIZE)

    def one_block(query_block):
        scores = jnp.dot(query_block, key_rows.T, preferred_element_type=jnp.float32) * scale
        peak = lax.optimization_barrier(jnp.max(scores, axis=-1))
        weights = jnp.exp(scores - peak[:, None])
        summed = lax.optimization_barrier(jnp.sum(weights, axis=-1))
        mixed = jnp.dot(weights.astype(jnp.bfloat16), value_rows, preferred_element_type=jnp.float32)
        return (mixed / summed[:, None]).astype(jnp.bfloat16)
    blocks = lax.map(one_block, queries.reshape(SEQ_LEN // block_rows, block_rows, KEY_SIZE))
    return blocks.reshape(SEQ_LEN, VALUE_SIZE)

def reference(sequence, gain_conv, conv_weight, gain_attn, w_qkv, w_out, gain_pool, w_pair, w_up, w_down):
    inputs = sequence.astype(jnp.float32)
    normed = norm_rows(inputs, gain_conv).astype(jnp.bfloat16)
    padded = jnp.pad(normed, ((RIM, RIM), (0, 0)))
    conv = jnp.zeros((SEQ_LEN, CHANNELS), jnp.float32)
    for offset in range(TAPS):
        conv = conv + jnp.dot(padded[offset * DILATION:offset * DILATION + SEQ_LEN], conv_weight[offset], preferred_element_type=jnp.float32)
    first_out = (inputs + conv).astype(jnp.bfloat16)
    attn_in = norm_rows(first_out.astype(jnp.float32), gain_attn).astype(jnp.bfloat16)
    projected = jnp.dot(attn_in, w_qkv, preferred_element_type=jnp.float32).astype(jnp.bfloat16)
    grouped = projected.reshape(SEQ_LEN, HEADS, 2 * KEY_SIZE + VALUE_SIZE).transpose(1, 0, 2)
    queries = grouped[:, :, :KEY_SIZE]
    key_rows = grouped[:, :, KEY_SIZE:2 * KEY_SIZE]
    value_rows = grouped[:, :, 2 * KEY_SIZE:]
    attended = lax.map(attend_head, (queries, key_rows, value_rows))
    attended = attended.transpose(1, 0, 2).reshape(SEQ_LEN, HEADS * VALUE_SIZE)
    mixed = jnp.dot(attended, w_out, preferred_element_type=jnp.float32)
    seq_out = (first_out.astype(jnp.float32) + mixed).astype(jnp.bfloat16)
    pooled = lax.optimization_barrier(jnp.mean(seq_out.astype(jnp.float32).reshape(BINS, POOL, CHANNELS), axis=1))
    bin_norm = norm_rows(pooled, gain_pool).astype(jnp.bfloat16)
    sides = jnp.dot(bin_norm, w_pair, preferred_element_type=jnp.float32).astype(jnp.bfloat16)
    left_side = sides[:, :PAIR_CH].astype(jnp.float32)
    right_side = sides[:, PAIR_CH:].astype(jnp.float32)

    def pair_row(left_row):
        pair_tile = (left_row[None, :] * right_side).astype(jnp.bfloat16)
        hidden = jax.nn.relu(jnp.dot(pair_tile, w_up, preferred_element_type=jnp.float32)).astype(jnp.bfloat16)
        return (pair_tile.astype(jnp.float32) + jnp.dot(hidden, w_down, preferred_element_type=jnp.float32)).astype(jnp.bfloat16)
    pair_map = lax.map(pair_row, left_side)
    return (seq_out, pair_map)
```

```python
import math

import jax
import jax.numpy as jnp
from jax import lax
from jax.sharding import PartitionSpec as P

KEY_SIZE = 128
VALUE_SIZE = 128
DILATION = 4
POOL = 16
PAIR_CH = 128


EPS = 1e-06


def padded_2(value, sides, width):
    for axis, dim in sides:
        peers, length = (lax.axis_size(axis), value.shape[dim])
        up = [(i, (i + 1) % peers) for i in range(peers - 1)]
        down = [(j, i) for i, j in up]
        last = lax.slice_in_dim(value, length - width, length, axis=dim)
        first = lax.slice_in_dim(value, 0, width, axis=dim)
        before = lax.ppermute(last, axis, up)
        after = lax.ppermute(first, axis, down)
        value = jnp.concatenate([before, value, after], axis=dim)
    return value


def norm_rows(values, gain):
    return values * lax.rsqrt(jnp.mean(values * values, axis=-1, keepdims=True) + EPS) * gain


def conv_rows(padded, conv_weight, row_total):
    summed = jnp.zeros((row_total, conv_weight.shape[2]), jnp.float32)
    for offset in range(conv_weight.shape[0]):
        shifted = lax.dynamic_slice_in_dim(padded, offset * DILATION, row_total, 0)
        summed = summed + jnp.dot(shifted, conv_weight[offset], preferred_element_type=jnp.float32)
    return summed


def line_reduce_scatter(partial, axis):
    n = lax.axis_size(axis)
    me = lax.axis_index(axis)
    rows = partial.shape[0] // n
    blocks = partial.reshape(n, rows, partial.shape[1])
    right = [(i, i + 1) for i in range(n - 1)]
    left = [(i + 1, i) for i in range(n - 1)]
    got_r = jnp.zeros((rows, partial.shape[1]), jnp.bfloat16)
    got_l = jnp.zeros((rows, partial.shape[1]), jnp.bfloat16)
    for step in range(1, n):
        idx_r = jnp.clip(me + n - step, 0, n - 1)
        idx_l = jnp.clip(me - (n - step), 0, n - 1)
        send_r = (blocks[idx_r] + got_r.astype(jnp.float32)).astype(jnp.bfloat16)
        send_l = (blocks[idx_l] + got_l.astype(jnp.float32)).astype(jnp.bfloat16)
        got_r = lax.ppermute(send_r, axis, right)
        got_l = lax.ppermute(send_l, axis, left)
    own = blocks[me]
    return own + got_r.astype(jnp.float32) + got_l.astype(jnp.float32)


def line_all_gather(value, axis):
    n = lax.axis_size(axis)
    me = lax.axis_index(axis)
    rows = value.shape[0]
    right = [(i, i + 1) for i in range(n - 1)]
    left = [(i + 1, i) for i in range(n - 1)]
    slots = jnp.zeros((n + 1, rows) + value.shape[1:], value.dtype)
    slots = lax.dynamic_update_index_in_dim(slots, value, me, 0)
    flow_r, flow_l = value, value
    for step in range(1, n):
        flow_r = lax.ppermute(flow_r, axis, right)
        flow_l = lax.ppermute(flow_l, axis, left)
        at_r = jnp.where(me - step >= 0, me - step, n)
        at_l = jnp.where(me + step < n, me + step, n)
        slots = lax.dynamic_update_index_in_dim(slots, flow_r, at_r, 0)
        slots = lax.dynamic_update_index_in_dim(slots, flow_l, at_l, 0)
    return slots[:n].reshape((n * rows,) + value.shape[1:])


def doubling_all_gather(value, axis):
    n = lax.axis_size(axis)
    assert n & (n - 1) == 0
    me = lax.axis_index(axis)
    out = value
    k = 1
    while k < n:
        other = lax.ppermute(out, axis, [(i, i ^ k) for i in range(n)])
        low = (me & k) == 0
        out = jnp.where(low, jnp.concatenate([out, other], 0), jnp.concatenate([other, out], 0))
        k *= 2
    return out


def shards(
    sequence, gain_conv, conv_weight, gain_attn, w_qkv, w_out, gain_pool, w_pair, w_up, w_down
):
    pair_count = lax.axis_size("pair")
    seq_count = lax.axis_size("seq")
    row_count = sequence.shape[0]
    channels = sequence.shape[1]
    local_rows = row_count * pair_count
    inputs = sequence.astype(jnp.float32)
    normed = norm_rows(inputs, gain_conv).astype(jnp.bfloat16)
    swapped = lax.all_to_all(normed, "pair", split_axis=1, concat_axis=0, tiled=True)
    padded = padded_2(swapped, (("seq", 0),), DILATION * (conv_weight.shape[0] - 1) // 2)
    with jax.named_scope("conv_reduce"):
        summed = line_reduce_scatter(conv_rows(padded, conv_weight, local_rows), "pair")
    first_out = (inputs + summed).astype(jnp.bfloat16)
    attn_in = norm_rows(first_out.astype(jnp.float32), gain_attn).astype(jnp.bfloat16)
    with jax.named_scope("attn_in_gather"):
        block_in = line_all_gather(attn_in, "pair")
    projected = jnp.dot(block_in, w_qkv, preferred_element_type=jnp.float32).astype(jnp.bfloat16)
    head_count = projected.shape[1] // (2 * KEY_SIZE + VALUE_SIZE)
    grouped = projected.reshape(local_rows, head_count, 2 * KEY_SIZE + VALUE_SIZE).transpose(1, 0, 2)
    queries = grouped[:, :, :KEY_SIZE]
    kv = grouped[:, :, KEY_SIZE:]
    scale = 1.0 / math.sqrt(KEY_SIZE)
    ring = [(i, (i + 1) % seq_count) for i in range(seq_count)]

    def attend(state, kv_block):
        running_max, running_sum, weighted = state
        key_block = kv_block[:, :, :KEY_SIZE]
        value_block = kv_block[:, :, KEY_SIZE:]
        scores = (
            jnp.einsum("hqd,hkd->hqk", queries, key_block, preferred_element_type=jnp.float32)
            * scale
        )
        new_max = jnp.maximum(running_max, jnp.max(scores, axis=-1))
        shrink = jnp.exp(running_max - new_max)
        weights = jnp.exp(scores - new_max[:, :, None])
        running_sum = running_sum * shrink + jnp.sum(weights, axis=-1)
        update = jnp.einsum(
            "hqk,hkd->hqd",
            weights.astype(jnp.bfloat16),
            value_block,
            preferred_element_type=jnp.float32,
        )
        weighted = weighted * shrink[:, :, None] + update
        return (new_max, running_sum, weighted)

    state = (
        jnp.full((head_count, local_rows), -1e30, jnp.float32),
        jnp.zeros((head_count, local_rows), jnp.float32),
        jnp.zeros((head_count, local_rows, VALUE_SIZE), jnp.float32),
    )
    with jax.named_scope("kv_ring"):
        current = kv
        for step in range(seq_count):
            if step + 1 < seq_count:
                arriving = lax.ppermute(current, "seq", ring)
            state = attend(state, current)
            if step + 1 < seq_count:
                current = arriving
    running_max, running_sum, weighted = state
    attended = (weighted / running_sum[:, :, None]).astype(jnp.bfloat16)
    attended = attended.transpose(1, 0, 2).reshape(local_rows, head_count * VALUE_SIZE)
    with jax.named_scope("out_reduce"):
        mixed = line_reduce_scatter(
            jnp.dot(attended, w_out, preferred_element_type=jnp.float32), "pair"
        )
    seq_out = (first_out.astype(jnp.float32) + mixed).astype(jnp.bfloat16)
    bin_count = row_count // POOL
    pooled = jnp.mean(seq_out.astype(jnp.float32).reshape(bin_count, POOL, channels), axis=1)
    bin_norm = norm_rows(pooled, gain_pool).astype(jnp.bfloat16)
    sides = jnp.dot(bin_norm, w_pair, preferred_element_type=jnp.float32).astype(jnp.bfloat16)
    with jax.named_scope("sides_gather"):
        all_sides = doubling_all_gather(doubling_all_gather(sides, "pair"), "seq")
    tile_rows = bin_count * pair_count
    tile_cols = bin_count * seq_count
    row_side = lax.dynamic_slice_in_dim(
        all_sides, lax.axis_index("seq") * tile_rows, tile_rows, 0
    )[:, :PAIR_CH]
    column_side = lax.dynamic_slice_in_dim(
        all_sides, lax.axis_index("pair") * tile_cols, tile_cols, 0
    )[:, PAIR_CH:]
    pair_tile = (
        row_side.astype(jnp.float32)[:, None, :] * column_side.astype(jnp.float32)[None, :, :]
    ).astype(jnp.bfloat16)
    flat_rows = pair_tile.reshape(tile_rows * tile_cols, PAIR_CH)
    hidden = jax.nn.relu(jnp.dot(flat_rows, w_up, preferred_element_type=jnp.float32)).astype(
        jnp.bfloat16
    )
    pair_out = flat_rows.astype(jnp.float32) + jnp.dot(
        hidden, w_down, preferred_element_type=jnp.float32
    )
    pair_map = pair_out.astype(jnp.bfloat16).reshape(tile_rows, tile_cols, PAIR_CH)
    return (seq_out, pair_map)


def solution(mesh):
    return jax.shard_map(
        shards,
        mesh=mesh,
        in_specs=(
            P(("groups", "seq", "pair"), None),
            P(),
            P(None, "pair", None),
            P(),
            P(None, "pair"),
            P("pair", None),
            P(),
            P(),
            P(),
            P(),
        ),
        out_specs=(P(("groups", "seq", "pair"), None), P(("groups", "seq"), "pair", None)),
        check_vma=False,
    )
```

```python
import math

import jax
import jax.numpy as jnp
from jax import lax
from jax.sharding import PartitionSpec as P

KEY_SIZE = 128
VALUE_SIZE = 128
DILATION = 4
POOL = 16
PAIR_CH = 128


EPS = 1e-06


def padded_2(value, sides, width):
    for axis, dim in sides:
        peers, length = (lax.axis_size(axis), value.shape[dim])
        up = [(i, (i + 1) % peers) for i in range(peers - 1)]
        down = [(j, i) for i, j in up]
        last = lax.slice_in_dim(value, length - width, length, axis=dim)
        first = lax.slice_in_dim(value, 0, width, axis=dim)
        before = lax.ppermute(last, axis, up)
        after = lax.ppermute(first, axis, down)
        value = jnp.concatenate([before, value, after], axis=dim)
    return value


def norm_rows(values, gain):
    return values * lax.rsqrt(jnp.mean(values * values, axis=-1, keepdims=True) + EPS) * gain


def conv_rows(padded, conv_weight, row_total):
    summed = jnp.zeros((row_total, conv_weight.shape[2]), jnp.float32)
    for offset in range(conv_weight.shape[0]):
        shifted = lax.dynamic_slice_in_dim(padded, offset * DILATION, row_total, 0)
        summed = summed + jnp.dot(shifted, conv_weight[offset], preferred_element_type=jnp.float32)
    return summed


def direct_reduce_scatter(partial, axis):
    n = lax.axis_size(axis)
    me = lax.axis_index(axis)
    rows = partial.shape[0] // n
    blocks = partial.reshape(n, rows, partial.shape[1])
    total = blocks[me]
    for shift in range(1, n):
        outgoing = blocks[(me + shift) % n].astype(jnp.bfloat16)
        incoming = lax.ppermute(outgoing, axis, [(i, (i + shift) % n) for i in range(n)])
        total = total + incoming.astype(jnp.float32)
    return total


def permute_all_to_all(value, axis):
    n = lax.axis_size(axis)
    me = lax.axis_index(axis)
    width = value.shape[1] // n
    pieces = value.reshape(value.shape[0], n, width)
    slots = jnp.zeros((n, value.shape[0], width), value.dtype)
    slots = lax.dynamic_update_index_in_dim(slots, pieces[:, me], me, 0)
    for shift in range(1, n):
        outgoing = pieces[:, (me + shift) % n]
        incoming = lax.ppermute(outgoing, axis, [(i, (i + shift) % n) for i in range(n)])
        slots = lax.dynamic_update_index_in_dim(slots, incoming, (me + n - shift) % n, 0)
    return slots.reshape(n * value.shape[0], width)


def line_all_gather(value, axis):
    n = lax.axis_size(axis)
    me = lax.axis_index(axis)
    rows = value.shape[0]
    right = [(i, i + 1) for i in range(n - 1)]
    left = [(i + 1, i) for i in range(n - 1)]
    slots = jnp.zeros((n + 1, rows) + value.shape[1:], value.dtype)
    slots = lax.dynamic_update_index_in_dim(slots, value, me, 0)
    flow_r, flow_l = value, value
    for step in range(1, n):
        flow_r = lax.ppermute(flow_r, axis, right)
        flow_l = lax.ppermute(flow_l, axis, left)
        at_r = jnp.where(me - step >= 0, me - step, n)
        at_l = jnp.where(me + step < n, me + step, n)
        slots = lax.dynamic_update_index_in_dim(slots, flow_r, at_r, 0)
        slots = lax.dynamic_update_index_in_dim(slots, flow_l, at_l, 0)
    return slots[:n].reshape((n * rows,) + value.shape[1:])


def doubling_all_gather(value, axis):
    n = lax.axis_size(axis)
    assert n & (n - 1) == 0
    me = lax.axis_index(axis)
    out = value
    k = 1
    while k < n:
        other = lax.ppermute(out, axis, [(i, i ^ k) for i in range(n)])
        low = (me & k) == 0
        out = jnp.where(low, jnp.concatenate([out, other], 0), jnp.concatenate([other, out], 0))
        k *= 2
    return out


def shards(
    sequence, gain_conv, conv_weight, gain_attn, w_qkv, w_out, gain_pool, w_pair, w_up, w_down
):
    pair_count = lax.axis_size("pair")
    seq_count = lax.axis_size("seq")
    row_count = sequence.shape[0]
    channels = sequence.shape[1]
    local_rows = row_count * pair_count
    inputs = sequence.astype(jnp.float32)
    normed = norm_rows(inputs, gain_conv).astype(jnp.bfloat16)
    swapped = permute_all_to_all(normed, "pair")
    padded = padded_2(swapped, (("seq", 0),), DILATION * (conv_weight.shape[0] - 1) // 2)
    with jax.named_scope("conv_reduce"):
        summed = direct_reduce_scatter(conv_rows(padded, conv_weight, local_rows), "pair")
    first_out = (inputs + summed).astype(jnp.bfloat16)
    attn_in = norm_rows(first_out.astype(jnp.float32), gain_attn).astype(jnp.bfloat16)
    with jax.named_scope("attn_in_gather"):
        block_in = line_all_gather(attn_in, "pair")
    projected = jnp.dot(block_in, w_qkv, preferred_element_type=jnp.float32).astype(jnp.bfloat16)
    head_count = projected.shape[1] // (2 * KEY_SIZE + VALUE_SIZE)
    grouped = projected.reshape(local_rows, head_count, 2 * KEY_SIZE + VALUE_SIZE).transpose(1, 0, 2)
    queries = grouped[:, :, :KEY_SIZE]
    kv = grouped[:, :, KEY_SIZE:]
    scale = 1.0 / math.sqrt(KEY_SIZE)
    ring = [(i, (i + 1) % seq_count) for i in range(seq_count)]

    def attend(state, kv_block):
        running_max, running_sum, weighted = state
        key_block = kv_block[:, :, :KEY_SIZE]
        value_block = kv_block[:, :, KEY_SIZE:]
        scores = (
            jnp.einsum("hqd,hkd->hqk", queries, key_block, preferred_element_type=jnp.float32)
            * scale
        )
        new_max = jnp.maximum(running_max, jnp.max(scores, axis=-1))
        shrink = jnp.exp(running_max - new_max)
        weights = jnp.exp(scores - new_max[:, :, None])
        running_sum = running_sum * shrink + jnp.sum(weights, axis=-1)
        update = jnp.einsum(
            "hqk,hkd->hqd",
            weights.astype(jnp.bfloat16),
            value_block,
            preferred_element_type=jnp.float32,
        )
        weighted = weighted * shrink[:, :, None] + update
        return (new_max, running_sum, weighted)

    state = (
        jnp.full((head_count, local_rows), -1e30, jnp.float32),
        jnp.zeros((head_count, local_rows), jnp.float32),
        jnp.zeros((head_count, local_rows, VALUE_SIZE), jnp.float32),
    )
    with jax.named_scope("kv_ring"):
        current = kv
        for step in range(seq_count):
            if step + 1 < seq_count:
                arriving = lax.ppermute(current, "seq", ring)
            state = attend(state, current)
            if step + 1 < seq_count:
                current = arriving
    running_max, running_sum, weighted = state
    attended = (weighted / running_sum[:, :, None]).astype(jnp.bfloat16)
    attended = attended.transpose(1, 0, 2).reshape(local_rows, head_count * VALUE_SIZE)
    with jax.named_scope("out_reduce"):
        mixed = direct_reduce_scatter(
            jnp.dot(attended, w_out, preferred_element_type=jnp.float32), "pair"
        )
    seq_out = (first_out.astype(jnp.float32) + mixed).astype(jnp.bfloat16)
    bin_count = row_count // POOL
    pooled = jnp.mean(seq_out.astype(jnp.float32).reshape(bin_count, POOL, channels), axis=1)
    bin_norm = norm_rows(pooled, gain_pool).astype(jnp.bfloat16)
    sides = jnp.dot(bin_norm, w_pair, preferred_element_type=jnp.float32).astype(jnp.bfloat16)
    with jax.named_scope("sides_gather"):
        all_sides = doubling_all_gather(doubling_all_gather(sides, "pair"), "seq")
    tile_rows = bin_count * pair_count
    tile_cols = bin_count * seq_count
    row_side = lax.dynamic_slice_in_dim(
        all_sides, lax.axis_index("seq") * tile_rows, tile_rows, 0
    )[:, :PAIR_CH]
    column_side = lax.dynamic_slice_in_dim(
        all_sides, lax.axis_index("pair") * tile_cols, tile_cols, 0
    )[:, PAIR_CH:]
    pair_tile = (
        row_side.astype(jnp.float32)[:, None, :] * column_side.astype(jnp.float32)[None, :, :]
    ).astype(jnp.bfloat16)
    flat_rows = pair_tile.reshape(tile_rows * tile_cols, PAIR_CH)
    hidden = jax.nn.relu(jnp.dot(flat_rows, w_up, preferred_element_type=jnp.float32)).astype(
        jnp.bfloat16
    )
    pair_out = flat_rows.astype(jnp.float32) + jnp.dot(
        hidden, w_down, preferred_element_type=jnp.float32
    )
    pair_map = pair_out.astype(jnp.bfloat16).reshape(tile_rows, tile_cols, PAIR_CH)
    return (seq_out, pair_map)


def solution(mesh):
    return jax.shard_map(
        shards,
        mesh=mesh,
        in_specs=(
            P(("groups", "seq", "pair"), None),
            P(),
            P(None, "pair", None),
            P(),
            P(None, "pair"),
            P("pair", None),
            P(),
            P(),
            P(),
            P(),
        ),
        out_specs=(P(("groups", "seq", "pair"), None), P(("groups", "seq"), "pair", None)),
        check_vma=False,
    )
```

```python
import math

import jax
import jax.numpy as jnp
from jax import lax
from jax.sharding import PartitionSpec as P

KEY_SIZE = 128
VALUE_SIZE = 128
DILATION = 4
POOL = 16
PAIR_CH = 128


EPS = 1e-06


def padded_2(value, sides, width):
    for axis, dim in sides:
        peers, length = (lax.axis_size(axis), value.shape[dim])
        up = [(i, (i + 1) % peers) for i in range(peers - 1)]
        down = [(j, i) for i, j in up]
        last = lax.slice_in_dim(value, length - width, length, axis=dim)
        first = lax.slice_in_dim(value, 0, width, axis=dim)
        before = lax.ppermute(last, axis, up)
        after = lax.ppermute(first, axis, down)
        value = jnp.concatenate([before, value, after], axis=dim)
    return value


def norm_rows(values, gain):
    return values * lax.rsqrt(jnp.mean(values * values, axis=-1, keepdims=True) + EPS) * gain


def conv_rows(padded, conv_weight, row_total):
    summed = jnp.zeros((row_total, conv_weight.shape[2]), jnp.float32)
    for offset in range(conv_weight.shape[0]):
        shifted = lax.dynamic_slice_in_dim(padded, offset * DILATION, row_total, 0)
        summed = summed + jnp.dot(shifted, conv_weight[offset], preferred_element_type=jnp.float32)
    return summed


def direct_reduce_scatter(partial, axis):
    n = lax.axis_size(axis)
    me = lax.axis_index(axis)
    rows = partial.shape[0] // n
    blocks = partial.reshape(n, rows, partial.shape[1])
    total = blocks[me]
    for shift in range(1, n):
        outgoing = blocks[(me + shift) % n].astype(jnp.bfloat16)
        incoming = lax.ppermute(outgoing, axis, [(i, (i + shift) % n) for i in range(n)])
        total = total + incoming.astype(jnp.float32)
    return total


def permute_all_to_all(value, axis):
    n = lax.axis_size(axis)
    me = lax.axis_index(axis)
    width = value.shape[1] // n
    pieces = value.reshape(value.shape[0], n, width)
    slots = jnp.zeros((n, value.shape[0], width), value.dtype)
    slots = lax.dynamic_update_index_in_dim(slots, pieces[:, me], me, 0)
    for shift in range(1, n):
        outgoing = pieces[:, (me + shift) % n]
        incoming = lax.ppermute(outgoing, axis, [(i, (i + shift) % n) for i in range(n)])
        slots = lax.dynamic_update_index_in_dim(slots, incoming, (me + n - shift) % n, 0)
    return slots.reshape(n * value.shape[0], width)


def line_all_gather(value, axis):
    n = lax.axis_size(axis)
    me = lax.axis_index(axis)
    rows = value.shape[0]
    right = [(i, i + 1) for i in range(n - 1)]
    left = [(i + 1, i) for i in range(n - 1)]
    slots = jnp.zeros((n + 1, rows) + value.shape[1:], value.dtype)
    slots = lax.dynamic_update_index_in_dim(slots, value, me, 0)
    flow_r, flow_l = value, value
    for step in range(1, n):
        flow_r = lax.ppermute(flow_r, axis, right)
        flow_l = lax.ppermute(flow_l, axis, left)
        at_r = jnp.where(me - step >= 0, me - step, n)
        at_l = jnp.where(me + step < n, me + step, n)
        slots = lax.dynamic_update_index_in_dim(slots, flow_r, at_r, 0)
        slots = lax.dynamic_update_index_in_dim(slots, flow_l, at_l, 0)
    return slots[:n].reshape((n * rows,) + value.shape[1:])


def rows_to_heads(value, axis):
    n = lax.axis_size(axis)
    me = lax.axis_index(axis)
    rows = value.shape[0] // n
    pieces = value.reshape(n, rows, value.shape[1])
    slots = jnp.zeros((n, rows, value.shape[1]), value.dtype)
    slots = lax.dynamic_update_index_in_dim(slots, pieces[me], me, 0)
    for shift in range(1, n):
        outgoing = pieces[(me + shift) % n]
        incoming = lax.ppermute(outgoing, axis, [(i, (i + shift) % n) for i in range(n)])
        slots = lax.dynamic_update_index_in_dim(slots, incoming, (me + n - shift) % n, 0)
    return slots.transpose(1, 0, 2).reshape(rows, n * value.shape[1])


def gather_weight_rows(weight, axis, chip_axis):
    peers = lax.axis_size(chip_axis)
    if peers % 2:
        return line_all_gather(weight, axis)
    core = lax.axis_index(chip_axis) % 2
    half = weight.shape[1] // 2
    mine = lax.dynamic_slice_in_dim(weight, core * half, half, 1)
    gathered = line_all_gather(mine, axis)
    other = lax.ppermute(gathered, chip_axis, [(i, i ^ 1) for i in range(peers)])
    return jnp.where(
        core == 0,
        jnp.concatenate([gathered, other], 1),
        jnp.concatenate([other, gathered], 1),
    )


def doubling_all_gather(value, axis):
    n = lax.axis_size(axis)
    assert n & (n - 1) == 0
    me = lax.axis_index(axis)
    out = value
    k = 1
    while k < n:
        other = lax.ppermute(out, axis, [(i, i ^ k) for i in range(n)])
        low = (me & k) == 0
        out = jnp.where(low, jnp.concatenate([out, other], 0), jnp.concatenate([other, out], 0))
        k *= 2
    return out


def shards(
    sequence, gain_conv, conv_weight, gain_attn, w_qkv, w_out, gain_pool, w_pair, w_up, w_down
):
    pair_count = lax.axis_size("pair")
    seq_count = lax.axis_size("seq")
    row_count = sequence.shape[0]
    channels = sequence.shape[1]
    local_rows = row_count * pair_count
    inputs = sequence.astype(jnp.float32)
    normed = norm_rows(inputs, gain_conv).astype(jnp.bfloat16)
    swapped = permute_all_to_all(normed, "pair")
    padded = padded_2(swapped, (("seq", 0),), DILATION * (conv_weight.shape[0] - 1) // 2)
    with jax.named_scope("conv_reduce"):
        summed = direct_reduce_scatter(conv_rows(padded, conv_weight, local_rows), "pair")
    first_out = (inputs + summed).astype(jnp.bfloat16)
    attn_in = norm_rows(first_out.astype(jnp.float32), gain_attn).astype(jnp.bfloat16)
    with jax.named_scope("attn_in_gather"):
        block_in = line_all_gather(attn_in, "pair")
    projected = jnp.dot(block_in, w_qkv, preferred_element_type=jnp.float32).astype(jnp.bfloat16)
    head_count = projected.shape[1] // (2 * KEY_SIZE + VALUE_SIZE)
    grouped = projected.reshape(local_rows, head_count, 2 * KEY_SIZE + VALUE_SIZE).transpose(1, 0, 2)
    queries = grouped[:, :, :KEY_SIZE]
    kv = grouped[:, :, KEY_SIZE:]
    scale = 1.0 / math.sqrt(KEY_SIZE)
    ring = [(i, (i + 1) % seq_count) for i in range(seq_count)]

    def attend(state, kv_block):
        running_max, running_sum, weighted = state
        key_block = kv_block[:, :, :KEY_SIZE]
        value_block = kv_block[:, :, KEY_SIZE:]
        scores = (
            jnp.einsum("hqd,hkd->hqk", queries, key_block, preferred_element_type=jnp.float32)
            * scale
        )
        new_max = jnp.maximum(running_max, jnp.max(scores, axis=-1))
        shrink = jnp.exp(running_max - new_max)
        weights = jnp.exp(scores - new_max[:, :, None])
        running_sum = running_sum * shrink + jnp.sum(weights, axis=-1)
        update = jnp.einsum(
            "hqk,hkd->hqd",
            weights.astype(jnp.bfloat16),
            value_block,
            preferred_element_type=jnp.float32,
        )
        weighted = weighted * shrink[:, :, None] + update
        return (new_max, running_sum, weighted)

    state = (
        jnp.full((head_count, local_rows), -1e30, jnp.float32),
        jnp.zeros((head_count, local_rows), jnp.float32),
        jnp.zeros((head_count, local_rows, VALUE_SIZE), jnp.float32),
    )
    with jax.named_scope("kv_ring"):
        current = kv
        for step in range(seq_count):
            if step + 1 < seq_count:
                arriving = lax.ppermute(current, "seq", ring)
            state = attend(state, current)
            if step + 1 < seq_count:
                current = arriving
    running_max, running_sum, weighted = state
    attended = (weighted / running_sum[:, :, None]).astype(jnp.bfloat16)
    attended = attended.transpose(1, 0, 2).reshape(local_rows, head_count * VALUE_SIZE)
    with jax.named_scope("out_projection"):
        late_w_out, unused = lax.optimization_barrier((w_out, kv))
        full_w_out = gather_weight_rows(late_w_out, "pair", "seq")
        own_heads = rows_to_heads(attended, "pair")
        mixed = jnp.dot(own_heads, full_w_out, preferred_element_type=jnp.float32)
    seq_out = (first_out.astype(jnp.float32) + mixed).astype(jnp.bfloat16)
    bin_count = row_count // POOL
    pooled = jnp.mean(seq_out.astype(jnp.float32).reshape(bin_count, POOL, channels), axis=1)
    bin_norm = norm_rows(pooled, gain_pool).astype(jnp.bfloat16)
    sides = jnp.dot(bin_norm, w_pair, preferred_element_type=jnp.float32).astype(jnp.bfloat16)
    with jax.named_scope("sides_gather"):
        all_sides = doubling_all_gather(doubling_all_gather(sides, "pair"), "seq")
    tile_rows = bin_count * pair_count
    tile_cols = bin_count * seq_count
    row_side = lax.dynamic_slice_in_dim(
        all_sides, lax.axis_index("seq") * tile_rows, tile_rows, 0
    )[:, :PAIR_CH]
    column_side = lax.dynamic_slice_in_dim(
        all_sides, lax.axis_index("pair") * tile_cols, tile_cols, 0
    )[:, PAIR_CH:]
    pair_tile = (
        row_side.astype(jnp.float32)[:, None, :] * column_side.astype(jnp.float32)[None, :, :]
    ).astype(jnp.bfloat16)
    flat_rows = pair_tile.reshape(tile_rows * tile_cols, PAIR_CH)
    hidden = jax.nn.relu(jnp.dot(flat_rows, w_up, preferred_element_type=jnp.float32)).astype(
        jnp.bfloat16
    )
    pair_out = flat_rows.astype(jnp.float32) + jnp.dot(
        hidden, w_down, preferred_element_type=jnp.float32
    )
    pair_map = pair_out.astype(jnp.bfloat16).reshape(tile_rows, tile_cols, PAIR_CH)
    return (seq_out, pair_map)


def solution(mesh):
    return jax.shard_map(
        shards,
        mesh=mesh,
        in_specs=(
            P(("groups", "seq", "pair"), None),
            P(),
            P(None, "pair", None),
            P(),
            P(None, "pair"),
            P("pair", None),
            P(),
            P(),
            P(),
            P(),
        ),
        out_specs=(P(("groups", "seq", "pair"), None), P(("groups", "seq"), "pair", None)),
        check_vma=False,
    )
```

```python
import math

import jax
import jax.numpy as jnp
from jax import lax
from jax.sharding import PartitionSpec as P

KEY_SIZE = 128
VALUE_SIZE = 128
DILATION = 4
POOL = 16
PAIR_CH = 128


EPS = 1e-06


def padded_2(value, sides, width):
    for axis, dim in sides:
        peers, length = (lax.axis_size(axis), value.shape[dim])
        up = [(i, (i + 1) % peers) for i in range(peers - 1)]
        down = [(j, i) for i, j in up]
        last = lax.slice_in_dim(value, length - width, length, axis=dim)
        first = lax.slice_in_dim(value, 0, width, axis=dim)
        before = lax.ppermute(last, axis, up)
        after = lax.ppermute(first, axis, down)
        value = jnp.concatenate([before, value, after], axis=dim)
    return value


def norm_rows(values, gain):
    return values * lax.rsqrt(jnp.mean(values * values, axis=-1, keepdims=True) + EPS) * gain


def conv_rows(padded, conv_weight, row_total):
    summed = jnp.zeros((row_total, conv_weight.shape[2]), jnp.float32)
    for offset in range(conv_weight.shape[0]):
        shifted = lax.dynamic_slice_in_dim(padded, offset * DILATION, row_total, 0)
        summed = summed + jnp.dot(shifted, conv_weight[offset], preferred_element_type=jnp.float32)
    return summed


def direct_reduce_scatter(partial, axis):
    n = lax.axis_size(axis)
    me = lax.axis_index(axis)
    rows = partial.shape[0] // n
    blocks = partial.reshape(n, rows, partial.shape[1])
    total = blocks[me]
    for shift in range(1, n):
        outgoing = blocks[(me + shift) % n].astype(jnp.bfloat16)
        incoming = lax.ppermute(outgoing, axis, [(i, (i + shift) % n) for i in range(n)])
        total = total + incoming.astype(jnp.float32)
    return total


def permute_all_to_all(value, axis):
    n = lax.axis_size(axis)
    me = lax.axis_index(axis)
    width = value.shape[1] // n
    pieces = value.reshape(value.shape[0], n, width)
    slots = jnp.zeros((n, value.shape[0], width), value.dtype)
    slots = lax.dynamic_update_index_in_dim(slots, pieces[:, me], me, 0)
    for shift in range(1, n):
        outgoing = pieces[:, (me + shift) % n]
        incoming = lax.ppermute(outgoing, axis, [(i, (i + shift) % n) for i in range(n)])
        slots = lax.dynamic_update_index_in_dim(slots, incoming, (me + n - shift) % n, 0)
    return slots.reshape(n * value.shape[0], width)


def line_all_gather(value, axis):
    n = lax.axis_size(axis)
    me = lax.axis_index(axis)
    rows = value.shape[0]
    right = [(i, i + 1) for i in range(n - 1)]
    left = [(i + 1, i) for i in range(n - 1)]
    slots = jnp.zeros((n + 1, rows) + value.shape[1:], value.dtype)
    slots = lax.dynamic_update_index_in_dim(slots, value, me, 0)
    flow_r, flow_l = value, value
    for step in range(1, n):
        flow_r = lax.ppermute(flow_r, axis, right)
        flow_l = lax.ppermute(flow_l, axis, left)
        at_r = jnp.where(me - step >= 0, me - step, n)
        at_l = jnp.where(me + step < n, me + step, n)
        slots = lax.dynamic_update_index_in_dim(slots, flow_r, at_r, 0)
        slots = lax.dynamic_update_index_in_dim(slots, flow_l, at_l, 0)
    return slots[:n].reshape((n * rows,) + value.shape[1:])


def rows_to_heads(value, axis):
    n = lax.axis_size(axis)
    me = lax.axis_index(axis)
    rows = value.shape[0] // n
    pieces = value.reshape(n, rows, value.shape[1])
    slots = jnp.zeros((n, rows, value.shape[1]), value.dtype)
    slots = lax.dynamic_update_index_in_dim(slots, pieces[me], me, 0)
    for shift in range(1, n):
        outgoing = pieces[(me + shift) % n]
        incoming = lax.ppermute(outgoing, axis, [(i, (i + shift) % n) for i in range(n)])
        slots = lax.dynamic_update_index_in_dim(slots, incoming, (me + n - shift) % n, 0)
    return slots.transpose(1, 0, 2).reshape(rows, n * value.shape[1])


def gather_weight_rows(weight, axis, chip_axis):
    peers = lax.axis_size(chip_axis)
    if peers % 2:
        return line_all_gather(weight, axis)
    core = lax.axis_index(chip_axis) % 2
    half = weight.shape[1] // 2
    mine = lax.dynamic_slice_in_dim(weight, core * half, half, 1)
    gathered = line_all_gather(mine, axis)
    other = lax.ppermute(gathered, chip_axis, [(i, i ^ 1) for i in range(peers)])
    return jnp.where(
        core == 0,
        jnp.concatenate([gathered, other], 1),
        jnp.concatenate([other, gathered], 1),
    )


def direct_all_gather(value, axis):
    n = lax.axis_size(axis)
    if n > 4:
        return line_all_gather(value, axis)
    me = lax.axis_index(axis)
    slots = jnp.zeros((n,) + value.shape, value.dtype)
    slots = lax.dynamic_update_index_in_dim(slots, value, me, 0)
    for shift in range(1, n):
        incoming = lax.ppermute(value, axis, [(i, (i + shift) % n) for i in range(n)])
        slots = lax.dynamic_update_index_in_dim(slots, incoming, (me + n - shift) % n, 0)
    return slots.reshape((n * value.shape[0],) + value.shape[1:])


def doubling_all_gather(value, axis):
    n = lax.axis_size(axis)
    assert n & (n - 1) == 0
    me = lax.axis_index(axis)
    out = value
    k = 1
    while k < n:
        other = lax.ppermute(out, axis, [(i, i ^ k) for i in range(n)])
        low = (me & k) == 0
        out = jnp.where(low, jnp.concatenate([out, other], 0), jnp.concatenate([other, out], 0))
        k *= 2
    return out


def shards(
    sequence, gain_conv, conv_weight, gain_attn, w_qkv, w_out, gain_pool, w_pair, w_up, w_down
):
    pair_count = lax.axis_size("pair")
    seq_count = lax.axis_size("seq")
    row_count = sequence.shape[0]
    channels = sequence.shape[1]
    local_rows = row_count * pair_count
    inputs = sequence.astype(jnp.float32)
    normed = norm_rows(inputs, gain_conv).astype(jnp.bfloat16)
    swapped = permute_all_to_all(normed, "pair")
    padded = padded_2(swapped, (("seq", 0),), DILATION * (conv_weight.shape[0] - 1) // 2)
    with jax.named_scope("conv_reduce"):
        summed = direct_reduce_scatter(conv_rows(padded, conv_weight, local_rows), "pair")
    first_out = (inputs + summed).astype(jnp.bfloat16)
    attn_in = norm_rows(first_out.astype(jnp.float32), gain_attn).astype(jnp.bfloat16)
    with jax.named_scope("attn_in_gather"):
        block_in = direct_all_gather(attn_in, "pair")
    projected = jnp.dot(block_in, w_qkv, preferred_element_type=jnp.float32).astype(jnp.bfloat16)
    head_count = projected.shape[1] // (2 * KEY_SIZE + VALUE_SIZE)
    grouped = projected.reshape(local_rows, head_count, 2 * KEY_SIZE + VALUE_SIZE).transpose(1, 0, 2)
    queries = grouped[:, :, :KEY_SIZE]
    kv = grouped[:, :, KEY_SIZE:]
    scale = 1.0 / math.sqrt(KEY_SIZE)
    ring = [(i, (i + 1) % seq_count) for i in range(seq_count)]

    def attend(state, kv_block):
        running_max, running_sum, weighted = state
        key_block = kv_block[:, :, :KEY_SIZE]
        value_block = kv_block[:, :, KEY_SIZE:]
        scores = (
            jnp.einsum("hqd,hkd->hqk", queries, key_block, preferred_element_type=jnp.float32)
            * scale
        )
        new_max = jnp.maximum(running_max, jnp.max(scores, axis=-1))
        shrink = jnp.exp(running_max - new_max)
        weights = jnp.exp(scores - new_max[:, :, None])
        running_sum = running_sum * shrink + jnp.sum(weights, axis=-1)
        update = jnp.einsum(
            "hqk,hkd->hqd",
            weights.astype(jnp.bfloat16),
            value_block,
            preferred_element_type=jnp.float32,
        )
        weighted = weighted * shrink[:, :, None] + update
        return (new_max, running_sum, weighted)

    state = (
        jnp.full((head_count, local_rows), -1e30, jnp.float32),
        jnp.zeros((head_count, local_rows), jnp.float32),
        jnp.zeros((head_count, local_rows, VALUE_SIZE), jnp.float32),
    )
    with jax.named_scope("kv_ring"):
        current = kv
        for step in range(seq_count):
            if step + 1 < seq_count:
                arriving = lax.ppermute(current, "seq", ring)
            state = attend(state, current)
            if step + 1 < seq_count:
                current = arriving
    running_max, running_sum, weighted = state
    attended = (weighted / running_sum[:, :, None]).astype(jnp.bfloat16)
    attended = attended.transpose(1, 0, 2).reshape(local_rows, head_count * VALUE_SIZE)
    with jax.named_scope("out_projection"):
        late_w_out, unused = lax.optimization_barrier((w_out, kv))
        full_w_out = gather_weight_rows(late_w_out, "pair", "seq")
        own_heads = rows_to_heads(attended, "pair")
        mixed = jnp.dot(own_heads, full_w_out, preferred_element_type=jnp.float32)
    seq_out = (first_out.astype(jnp.float32) + mixed).astype(jnp.bfloat16)
    bin_count = row_count // POOL
    pooled = jnp.mean(seq_out.astype(jnp.float32).reshape(bin_count, POOL, channels), axis=1)
    bin_norm = norm_rows(pooled, gain_pool).astype(jnp.bfloat16)
    sides = jnp.dot(bin_norm, w_pair, preferred_element_type=jnp.float32).astype(jnp.bfloat16)
    with jax.named_scope("sides_gather"):
        if seq_count > 4:
            all_sides = doubling_all_gather(doubling_all_gather(sides, "pair"), "seq")
        else:
            all_sides = direct_all_gather(direct_all_gather(sides, "pair"), "seq")
    tile_rows = bin_count * pair_count
    tile_cols = bin_count * seq_count
    row_side = lax.dynamic_slice_in_dim(
        all_sides, lax.axis_index("seq") * tile_rows, tile_rows, 0
    )[:, :PAIR_CH]
    column_side = lax.dynamic_slice_in_dim(
        all_sides, lax.axis_index("pair") * tile_cols, tile_cols, 0
    )[:, PAIR_CH:]
    pair_tile = (
        row_side.astype(jnp.float32)[:, None, :] * column_side.astype(jnp.float32)[None, :, :]
    ).astype(jnp.bfloat16)
    flat_rows = pair_tile.reshape(tile_rows * tile_cols, PAIR_CH)
    hidden = jax.nn.relu(jnp.dot(flat_rows, w_up, preferred_element_type=jnp.float32)).astype(
        jnp.bfloat16
    )
    pair_out = flat_rows.astype(jnp.float32) + jnp.dot(
        hidden, w_down, preferred_element_type=jnp.float32
    )
    pair_map = pair_out.astype(jnp.bfloat16).reshape(tile_rows, tile_cols, PAIR_CH)
    return (seq_out, pair_map)


def solution(mesh):
    return jax.shard_map(
        shards,
        mesh=mesh,
        in_specs=(
            P(("groups", "seq", "pair"), None),
            P(),
            P(None, "pair", None),
            P(),
            P(None, "pair"),
            P("pair", None),
            P(),
            P(),
            P(),
            P(),
        ),
        out_specs=(P(("groups", "seq", "pair"), None), P(("groups", "seq"), "pair", None)),
        check_vma=False,
    )
```

```python
import math

import jax
import jax.numpy as jnp
from jax import lax
from jax.sharding import PartitionSpec as P

KEY_SIZE = 128
VALUE_SIZE = 128
DILATION = 4
POOL = 16
PAIR_CH = 128


EPS = 1e-06


def padded_2(value, sides, width):
    for axis, dim in sides:
        peers, length = (lax.axis_size(axis), value.shape[dim])
        up = [(i, (i + 1) % peers) for i in range(peers - 1)]
        down = [(j, i) for i, j in up]
        last = lax.slice_in_dim(value, length - width, length, axis=dim)
        first = lax.slice_in_dim(value, 0, width, axis=dim)
        before = lax.ppermute(last, axis, up)
        after = lax.ppermute(first, axis, down)
        value = jnp.concatenate([before, value, after], axis=dim)
    return value


def norm_rows(values, gain):
    return values * lax.rsqrt(jnp.mean(values * values, axis=-1, keepdims=True) + EPS) * gain


def conv_rows(padded, conv_weight, row_total):
    summed = jnp.zeros((row_total, conv_weight.shape[2]), jnp.float32)
    for offset in range(conv_weight.shape[0]):
        shifted = lax.dynamic_slice_in_dim(padded, offset * DILATION, row_total, 0)
        summed = summed + jnp.dot(shifted, conv_weight[offset], preferred_element_type=jnp.float32)
    return summed


def direct_reduce_scatter(partial, axis):
    n = lax.axis_size(axis)
    me = lax.axis_index(axis)
    rows = partial.shape[0] // n
    blocks = partial.reshape(n, rows, partial.shape[1])
    total = blocks[me]
    for shift in range(1, n):
        outgoing = blocks[(me + shift) % n].astype(jnp.bfloat16)
        incoming = lax.ppermute(outgoing, axis, [(i, (i + shift) % n) for i in range(n)])
        total = total + incoming.astype(jnp.float32)
    return total


def permute_all_to_all(value, axis):
    n = lax.axis_size(axis)
    me = lax.axis_index(axis)
    width = value.shape[1] // n
    pieces = value.reshape(value.shape[0], n, width)
    slots = jnp.zeros((n, value.shape[0], width), value.dtype)
    slots = lax.dynamic_update_index_in_dim(slots, pieces[:, me], me, 0)
    for shift in range(1, n):
        outgoing = pieces[:, (me + shift) % n]
        incoming = lax.ppermute(outgoing, axis, [(i, (i + shift) % n) for i in range(n)])
        slots = lax.dynamic_update_index_in_dim(slots, incoming, (me + n - shift) % n, 0)
    return slots.reshape(n * value.shape[0], width)


def line_all_gather(value, axis):
    n = lax.axis_size(axis)
    me = lax.axis_index(axis)
    rows = value.shape[0]
    right = [(i, i + 1) for i in range(n - 1)]
    left = [(i + 1, i) for i in range(n - 1)]
    slots = jnp.zeros((n + 1, rows) + value.shape[1:], value.dtype)
    slots = lax.dynamic_update_index_in_dim(slots, value, me, 0)
    flow_r, flow_l = value, value
    for step in range(1, n):
        flow_r = lax.ppermute(flow_r, axis, right)
        flow_l = lax.ppermute(flow_l, axis, left)
        at_r = jnp.where(me - step >= 0, me - step, n)
        at_l = jnp.where(me + step < n, me + step, n)
        slots = lax.dynamic_update_index_in_dim(slots, flow_r, at_r, 0)
        slots = lax.dynamic_update_index_in_dim(slots, flow_l, at_l, 0)
    return slots[:n].reshape((n * rows,) + value.shape[1:])


def rows_to_heads(value, axis):
    n = lax.axis_size(axis)
    me = lax.axis_index(axis)
    rows = value.shape[0] // n
    pieces = value.reshape(n, rows, value.shape[1])
    slots = jnp.zeros((n, rows, value.shape[1]), value.dtype)
    slots = lax.dynamic_update_index_in_dim(slots, pieces[me], me, 0)
    for shift in range(1, n):
        outgoing = pieces[(me + shift) % n]
        incoming = lax.ppermute(outgoing, axis, [(i, (i + shift) % n) for i in range(n)])
        slots = lax.dynamic_update_index_in_dim(slots, incoming, (me + n - shift) % n, 0)
    return slots.transpose(1, 0, 2).reshape(rows, n * value.shape[1])


def gather_weight_rows(weight, axis, chip_axis):
    peers = lax.axis_size(chip_axis)
    if peers % 2:
        return line_all_gather(weight, axis)
    core = lax.axis_index(chip_axis) % 2
    half = weight.shape[1] // 2
    mine = lax.dynamic_slice_in_dim(weight, core * half, half, 1)
    gathered = direct_all_gather(mine, axis)
    other = lax.ppermute(gathered, chip_axis, [(i, i ^ 1) for i in range(peers)])
    return jnp.where(
        core == 0,
        jnp.concatenate([gathered, other], 1),
        jnp.concatenate([other, gathered], 1),
    )


def direct_all_gather(value, axis):
    n = lax.axis_size(axis)
    if n > 4:
        return line_all_gather(value, axis)
    me = lax.axis_index(axis)
    slots = jnp.zeros((n,) + value.shape, value.dtype)
    slots = lax.dynamic_update_index_in_dim(slots, value, me, 0)
    for shift in range(1, n):
        incoming = lax.ppermute(value, axis, [(i, (i + shift) % n) for i in range(n)])
        slots = lax.dynamic_update_index_in_dim(slots, incoming, (me + n - shift) % n, 0)
    return slots.reshape((n * value.shape[0],) + value.shape[1:])


def doubling_all_gather(value, axis):
    n = lax.axis_size(axis)
    assert n & (n - 1) == 0
    me = lax.axis_index(axis)
    out = value
    k = 1
    while k < n:
        other = lax.ppermute(out, axis, [(i, i ^ k) for i in range(n)])
        low = (me & k) == 0
        out = jnp.where(low, jnp.concatenate([out, other], 0), jnp.concatenate([other, out], 0))
        k *= 2
    return out


def shards(
    sequence, gain_conv, conv_weight, gain_attn, w_qkv, w_out, gain_pool, w_pair, w_up, w_down
):
    pair_count = lax.axis_size("pair")
    seq_count = lax.axis_size("seq")
    row_count = sequence.shape[0]
    channels = sequence.shape[1]
    local_rows = row_count * pair_count
    inputs = sequence.astype(jnp.float32)
    normed = norm_rows(inputs, gain_conv).astype(jnp.bfloat16)
    swapped = permute_all_to_all(normed, "pair")
    padded = padded_2(swapped, (("seq", 0),), DILATION * (conv_weight.shape[0] - 1) // 2)
    early_w_out = pair_count <= 4
    with jax.named_scope("conv_reduce"):
        conv_partial = conv_rows(padded, conv_weight, local_rows)
        if early_w_out:
            full_w_out = gather_weight_rows(w_out, "pair", "seq")
            conv_partial, full_w_out = lax.optimization_barrier((conv_partial, full_w_out))
        summed = direct_reduce_scatter(conv_partial, "pair")
    first_out = (inputs + summed).astype(jnp.bfloat16)
    attn_in = norm_rows(first_out.astype(jnp.float32), gain_attn).astype(jnp.bfloat16)
    with jax.named_scope("attn_in_gather"):
        block_in = direct_all_gather(attn_in, "pair")
    projected = jnp.dot(block_in, w_qkv, preferred_element_type=jnp.float32).astype(jnp.bfloat16)
    head_count = projected.shape[1] // (2 * KEY_SIZE + VALUE_SIZE)
    grouped = projected.reshape(local_rows, head_count, 2 * KEY_SIZE + VALUE_SIZE).transpose(1, 0, 2)
    queries = grouped[:, :, :KEY_SIZE]
    kv = grouped[:, :, KEY_SIZE:]
    scale = 1.0 / math.sqrt(KEY_SIZE)
    ring = [(i, (i + 1) % seq_count) for i in range(seq_count)]

    def attend(state, kv_block):
        running_max, running_sum, weighted = state
        key_block = kv_block[:, :, :KEY_SIZE]
        value_block = kv_block[:, :, KEY_SIZE:]
        scores = (
            jnp.einsum("hqd,hkd->hqk", queries, key_block, preferred_element_type=jnp.float32)
            * scale
        )
        new_max = jnp.maximum(running_max, jnp.max(scores, axis=-1))
        shrink = jnp.exp(running_max - new_max)
        weights = jnp.exp(scores - new_max[:, :, None])
        running_sum = running_sum * shrink + jnp.sum(weights, axis=-1)
        update = jnp.einsum(
            "hqk,hkd->hqd",
            weights.astype(jnp.bfloat16),
            value_block,
            preferred_element_type=jnp.float32,
        )
        weighted = weighted * shrink[:, :, None] + update
        return (new_max, running_sum, weighted)

    state = (
        jnp.full((head_count, local_rows), -1e30, jnp.float32),
        jnp.zeros((head_count, local_rows), jnp.float32),
        jnp.zeros((head_count, local_rows, VALUE_SIZE), jnp.float32),
    )
    with jax.named_scope("kv_ring"):
        current = kv
        for step in range(seq_count):
            if step + 1 < seq_count:
                arriving = lax.ppermute(current, "seq", ring)
            state = attend(state, current)
            if step + 1 < seq_count:
                current = arriving
    running_max, running_sum, weighted = state
    attended = (weighted / running_sum[:, :, None]).astype(jnp.bfloat16)
    attended = attended.transpose(1, 0, 2).reshape(local_rows, head_count * VALUE_SIZE)
    with jax.named_scope("out_projection"):
        if not early_w_out:
            late_w_out, unused = lax.optimization_barrier((w_out, kv))
            full_w_out = gather_weight_rows(late_w_out, "pair", "seq")
        own_heads = rows_to_heads(attended, "pair")
        mixed = jnp.dot(own_heads, full_w_out, preferred_element_type=jnp.float32)
    seq_out = (first_out.astype(jnp.float32) + mixed).astype(jnp.bfloat16)
    bin_count = row_count // POOL
    pooled = jnp.mean(seq_out.astype(jnp.float32).reshape(bin_count, POOL, channels), axis=1)
    bin_norm = norm_rows(pooled, gain_pool).astype(jnp.bfloat16)
    sides = jnp.dot(bin_norm, w_pair, preferred_element_type=jnp.float32).astype(jnp.bfloat16)
    with jax.named_scope("sides_gather"):
        if seq_count > 4:
            all_sides = doubling_all_gather(doubling_all_gather(sides, "pair"), "seq")
        else:
            all_sides = direct_all_gather(direct_all_gather(sides, "pair"), "seq")
    tile_rows = bin_count * pair_count
    tile_cols = bin_count * seq_count
    row_side = lax.dynamic_slice_in_dim(
        all_sides, lax.axis_index("seq") * tile_rows, tile_rows, 0
    )[:, :PAIR_CH]
    column_side = lax.dynamic_slice_in_dim(
        all_sides, lax.axis_index("pair") * tile_cols, tile_cols, 0
    )[:, PAIR_CH:]
    pair_tile = (
        row_side.astype(jnp.float32)[:, None, :] * column_side.astype(jnp.float32)[None, :, :]
    ).astype(jnp.bfloat16)
    flat_rows = pair_tile.reshape(tile_rows * tile_cols, PAIR_CH)
    hidden = jax.nn.relu(jnp.dot(flat_rows, w_up, preferred_element_type=jnp.float32)).astype(
        jnp.bfloat16
    )
    pair_out = flat_rows.astype(jnp.float32) + jnp.dot(
        hidden, w_down, preferred_element_type=jnp.float32
    )
    pair_map = pair_out.astype(jnp.bfloat16).reshape(tile_rows, tile_cols, PAIR_CH)
    return (seq_out, pair_map)


def solution(mesh):
    return jax.shard_map(
        shards,
        mesh=mesh,
        in_specs=(
            P(("groups", "seq", "pair"), None),
            P(),
            P(None, "pair", None),
            P(),
            P(None, "pair"),
            P("pair", None),
            P(),
            P(),
            P(),
            P(),
        ),
        out_specs=(P(("groups", "seq", "pair"), None), P(("groups", "seq"), "pair", None)),
        check_vma=False,
    )
```

```python
import math

import jax
import jax.numpy as jnp
from jax import lax
from jax.sharding import PartitionSpec as P

KEY_SIZE = 128
VALUE_SIZE = 128
DILATION = 4
POOL = 16
PAIR_CH = 128


EPS = 1e-06


def padded_2(value, sides, width):
    for axis, dim in sides:
        peers, length = (lax.axis_size(axis), value.shape[dim])
        up = [(i, (i + 1) % peers) for i in range(peers - 1)]
        down = [(j, i) for i, j in up]
        last = lax.slice_in_dim(value, length - width, length, axis=dim)
        first = lax.slice_in_dim(value, 0, width, axis=dim)
        before = lax.ppermute(last, axis, up)
        after = lax.ppermute(first, axis, down)
        value = jnp.concatenate([before, value, after], axis=dim)
    return value


def norm_rows(values, gain):
    return values * lax.rsqrt(jnp.mean(values * values, axis=-1, keepdims=True) + EPS) * gain


def conv_rows(padded, conv_weight, row_total):
    summed = jnp.zeros((row_total, conv_weight.shape[2]), jnp.float32)
    for offset in range(conv_weight.shape[0]):
        shifted = lax.dynamic_slice_in_dim(padded, offset * DILATION, row_total, 0)
        summed = summed + jnp.dot(shifted, conv_weight[offset], preferred_element_type=jnp.float32)
    return summed


def direct_reduce_scatter(partial, axis):
    n = lax.axis_size(axis)
    me = lax.axis_index(axis)
    rows = partial.shape[0] // n
    blocks = partial.reshape(n, rows, partial.shape[1])
    total = blocks[me]
    for shift in range(1, n):
        outgoing = blocks[(me + shift) % n].astype(jnp.bfloat16)
        incoming = lax.ppermute(outgoing, axis, [(i, (i + shift) % n) for i in range(n)])
        total = total + incoming.astype(jnp.float32)
    return total


def permute_all_to_all(value, axis):
    n = lax.axis_size(axis)
    me = lax.axis_index(axis)
    width = value.shape[1] // n
    pieces = value.reshape(value.shape[0], n, width)
    slots = jnp.zeros((n, value.shape[0], width), value.dtype)
    slots = lax.dynamic_update_index_in_dim(slots, pieces[:, me], me, 0)
    for shift in range(1, n):
        outgoing = pieces[:, (me + shift) % n]
        incoming = lax.ppermute(outgoing, axis, [(i, (i + shift) % n) for i in range(n)])
        slots = lax.dynamic_update_index_in_dim(slots, incoming, (me + n - shift) % n, 0)
    return slots.reshape(n * value.shape[0], width)


def line_all_gather(value, axis):
    n = lax.axis_size(axis)
    me = lax.axis_index(axis)
    rows = value.shape[0]
    right = [(i, i + 1) for i in range(n - 1)]
    left = [(i + 1, i) for i in range(n - 1)]
    slots = jnp.zeros((n + 1, rows) + value.shape[1:], value.dtype)
    slots = lax.dynamic_update_index_in_dim(slots, value, me, 0)
    flow_r, flow_l = value, value
    for step in range(1, n):
        flow_r = lax.ppermute(flow_r, axis, right)
        flow_l = lax.ppermute(flow_l, axis, left)
        at_r = jnp.where(me - step >= 0, me - step, n)
        at_l = jnp.where(me + step < n, me + step, n)
        slots = lax.dynamic_update_index_in_dim(slots, flow_r, at_r, 0)
        slots = lax.dynamic_update_index_in_dim(slots, flow_l, at_l, 0)
    return slots[:n].reshape((n * rows,) + value.shape[1:])


def rows_to_heads(value, axis):
    n = lax.axis_size(axis)
    me = lax.axis_index(axis)
    rows = value.shape[0] // n
    pieces = value.reshape(n, rows, value.shape[1])
    slots = jnp.zeros((n, rows, value.shape[1]), value.dtype)
    slots = lax.dynamic_update_index_in_dim(slots, pieces[me], me, 0)
    for shift in range(1, n):
        outgoing = pieces[(me + shift) % n]
        incoming = lax.ppermute(outgoing, axis, [(i, (i + shift) % n) for i in range(n)])
        slots = lax.dynamic_update_index_in_dim(slots, incoming, (me + n - shift) % n, 0)
    return slots.transpose(1, 0, 2).reshape(rows, n * value.shape[1])


def gather_weight_rows(weight, axis, chip_axis):
    peers = lax.axis_size(chip_axis)
    if peers % 2:
        return line_all_gather(weight, axis)
    core = lax.axis_index(chip_axis) % 2
    half = weight.shape[1] // 2
    mine = lax.dynamic_slice_in_dim(weight, core * half, half, 1)
    gathered = line_all_gather(mine, axis)
    other = lax.ppermute(gathered, chip_axis, [(i, i ^ 1) for i in range(peers)])
    return jnp.where(
        core == 0,
        jnp.concatenate([gathered, other], 1),
        jnp.concatenate([other, gathered], 1),
    )


def direct_all_gather(value, axis):
    n = lax.axis_size(axis)
    if n > 4:
        return line_all_gather(value, axis)
    me = lax.axis_index(axis)
    slots = jnp.zeros((n,) + value.shape, value.dtype)
    slots = lax.dynamic_update_index_in_dim(slots, value, me, 0)
    for shift in range(1, n):
        incoming = lax.ppermute(value, axis, [(i, (i + shift) % n) for i in range(n)])
        slots = lax.dynamic_update_index_in_dim(slots, incoming, (me + n - shift) % n, 0)
    return slots.reshape((n * value.shape[0],) + value.shape[1:])


def doubling_all_gather(value, axis):
    n = lax.axis_size(axis)
    assert n & (n - 1) == 0
    me = lax.axis_index(axis)
    out = value
    k = 1
    while k < n:
        other = lax.ppermute(out, axis, [(i, i ^ k) for i in range(n)])
        low = (me & k) == 0
        out = jnp.where(low, jnp.concatenate([out, other], 0), jnp.concatenate([other, out], 0))
        k *= 2
    return out


def shards(
    sequence, gain_conv, conv_weight, gain_attn, w_qkv, w_out, gain_pool, w_pair, w_up, w_down
):
    pair_count = lax.axis_size("pair")
    seq_count = lax.axis_size("seq")
    row_count = sequence.shape[0]
    channels = sequence.shape[1]
    local_rows = row_count * pair_count
    inputs = sequence.astype(jnp.float32)
    normed = norm_rows(inputs, gain_conv).astype(jnp.bfloat16)
    swapped = permute_all_to_all(normed, "pair")
    padded = padded_2(swapped, (("seq", 0),), DILATION * (conv_weight.shape[0] - 1) // 2)
    with jax.named_scope("conv_reduce"):
        summed = direct_reduce_scatter(conv_rows(padded, conv_weight, local_rows), "pair")
    first_out = (inputs + summed).astype(jnp.bfloat16)
    attn_in = norm_rows(first_out.astype(jnp.float32), gain_attn).astype(jnp.bfloat16)
    with jax.named_scope("attn_in_gather"):
        block_in = direct_all_gather(attn_in, "pair")
    projected = jnp.dot(block_in, w_qkv, preferred_element_type=jnp.float32).astype(jnp.bfloat16)
    head_count = projected.shape[1] // (2 * KEY_SIZE + VALUE_SIZE)
    grouped = projected.reshape(local_rows, head_count, 2 * KEY_SIZE + VALUE_SIZE).transpose(1, 0, 2)
    queries = grouped[:, :, :KEY_SIZE]
    kv = grouped[:, :, KEY_SIZE:]
    scale = 1.0 / math.sqrt(KEY_SIZE)

    def attend(state, kv_block):
        running_max, running_sum, weighted = state
        key_block = kv_block[:, :, :KEY_SIZE]
        value_block = kv_block[:, :, KEY_SIZE:]
        scores = (
            jnp.einsum("hqd,hkd->hqk", queries, key_block, preferred_element_type=jnp.float32)
            * scale
        )
        new_max = jnp.maximum(running_max, jnp.max(scores, axis=-1))
        shrink = jnp.exp(running_max - new_max)
        weights = jnp.exp(scores - new_max[:, :, None])
        running_sum = running_sum * shrink + jnp.sum(weights, axis=-1)
        update = jnp.einsum(
            "hqk,hkd->hqd",
            weights.astype(jnp.bfloat16),
            value_block,
            preferred_element_type=jnp.float32,
        )
        weighted = weighted * shrink[:, :, None] + update
        return (new_max, running_sum, weighted)

    state = (
        jnp.full((head_count, local_rows), -1e30, jnp.float32),
        jnp.zeros((head_count, local_rows), jnp.float32),
        jnp.zeros((head_count, local_rows, VALUE_SIZE), jnp.float32),
    )
    with jax.named_scope("kv_ring"):
        forward = [(i, (i + 1) % seq_count) for i in range(seq_count)]
        backward = [((i + 1) % seq_count, i) for i in range(seq_count)]
        half = local_rows // 2
        going = kv[:, :half]
        coming = kv[:, half:]
        for step in range(seq_count):
            if step + 1 < seq_count:
                next_going = lax.ppermute(going, "seq", forward)
                next_coming = lax.ppermute(coming, "seq", backward)
            state = attend(state, going)
            state = attend(state, coming)
            if step + 1 < seq_count:
                going, coming = next_going, next_coming
    running_max, running_sum, weighted = state
    attended = (weighted / running_sum[:, :, None]).astype(jnp.bfloat16)
    attended = attended.transpose(1, 0, 2).reshape(local_rows, head_count * VALUE_SIZE)
    with jax.named_scope("out_projection"):
        late_w_out, unused = lax.optimization_barrier((w_out, kv))
        full_w_out = gather_weight_rows(late_w_out, "pair", "seq")
        own_heads = rows_to_heads(attended, "pair")
        mixed = jnp.dot(own_heads, full_w_out, preferred_element_type=jnp.float32)
    seq_out = (first_out.astype(jnp.float32) + mixed).astype(jnp.bfloat16)
    bin_count = row_count // POOL
    pooled = jnp.mean(seq_out.astype(jnp.float32).reshape(bin_count, POOL, channels), axis=1)
    bin_norm = norm_rows(pooled, gain_pool).astype(jnp.bfloat16)
    sides = jnp.dot(bin_norm, w_pair, preferred_element_type=jnp.float32).astype(jnp.bfloat16)
    with jax.named_scope("sides_gather"):
        if seq_count > 4:
            all_sides = doubling_all_gather(doubling_all_gather(sides, "pair"), "seq")
        else:
            all_sides = direct_all_gather(direct_all_gather(sides, "pair"), "seq")
    tile_rows = bin_count * pair_count
    tile_cols = bin_count * seq_count
    row_side = lax.dynamic_slice_in_dim(
        all_sides, lax.axis_index("seq") * tile_rows, tile_rows, 0
    )[:, :PAIR_CH]
    column_side = lax.dynamic_slice_in_dim(
        all_sides, lax.axis_index("pair") * tile_cols, tile_cols, 0
    )[:, PAIR_CH:]
    pair_tile = (
        row_side.astype(jnp.float32)[:, None, :] * column_side.astype(jnp.float32)[None, :, :]
    ).astype(jnp.bfloat16)
    flat_rows = pair_tile.reshape(tile_rows * tile_cols, PAIR_CH)
    hidden = jax.nn.relu(jnp.dot(flat_rows, w_up, preferred_element_type=jnp.float32)).astype(
        jnp.bfloat16
    )
    pair_out = flat_rows.astype(jnp.float32) + jnp.dot(
        hidden, w_down, preferred_element_type=jnp.float32
    )
    pair_map = pair_out.astype(jnp.bfloat16).reshape(tile_rows, tile_cols, PAIR_CH)
    return (seq_out, pair_map)


def solution(mesh):
    return jax.shard_map(
        shards,
        mesh=mesh,
        in_specs=(
            P(("groups", "seq", "pair"), None),
            P(),
            P(None, "pair", None),
            P(),
            P(None, "pair"),
            P("pair", None),
            P(),
            P(),
            P(),
            P(),
        ),
        out_specs=(P(("groups", "seq", "pair"), None), P(("groups", "seq"), "pair", None)),
        check_vma=False,
    )
```

```python
import math

import jax
import jax.numpy as jnp
from jax import lax
from jax.sharding import PartitionSpec as P

KEY_SIZE = 128
VALUE_SIZE = 128
DILATION = 4
POOL = 16
PAIR_CH = 128


EPS = 1e-06


def padded_2(value, sides, width):
    for axis, dim in sides:
        peers, length = (lax.axis_size(axis), value.shape[dim])
        up = [(i, (i + 1) % peers) for i in range(peers - 1)]
        down = [(j, i) for i, j in up]
        last = lax.slice_in_dim(value, length - width, length, axis=dim)
        first = lax.slice_in_dim(value, 0, width, axis=dim)
        before = lax.ppermute(last, axis, up)
        after = lax.ppermute(first, axis, down)
        value = jnp.concatenate([before, value, after], axis=dim)
    return value


def norm_rows(values, gain):
    return values * lax.rsqrt(jnp.mean(values * values, axis=-1, keepdims=True) + EPS) * gain


def conv_rows(padded, conv_weight, row_total):
    summed = jnp.zeros((row_total, conv_weight.shape[2]), jnp.float32)
    for offset in range(conv_weight.shape[0]):
        shifted = lax.dynamic_slice_in_dim(padded, offset * DILATION, row_total, 0)
        summed = summed + jnp.dot(shifted, conv_weight[offset], preferred_element_type=jnp.float32)
    return summed


def direct_reduce_scatter(partial, axis):
    n = lax.axis_size(axis)
    me = lax.axis_index(axis)
    rows = partial.shape[0] // n
    blocks = partial.reshape(n, rows, partial.shape[1])
    total = blocks[me]
    for shift in range(1, n):
        outgoing = blocks[(me + shift) % n].astype(jnp.bfloat16)
        incoming = lax.ppermute(outgoing, axis, [(i, (i + shift) % n) for i in range(n)])
        total = total + incoming.astype(jnp.float32)
    return total


def permute_all_to_all(value, axis):
    n = lax.axis_size(axis)
    me = lax.axis_index(axis)
    width = value.shape[1] // n
    pieces = value.reshape(value.shape[0], n, width)
    slots = jnp.zeros((n, value.shape[0], width), value.dtype)
    slots = lax.dynamic_update_index_in_dim(slots, pieces[:, me], me, 0)
    for shift in range(1, n):
        outgoing = pieces[:, (me + shift) % n]
        incoming = lax.ppermute(outgoing, axis, [(i, (i + shift) % n) for i in range(n)])
        slots = lax.dynamic_update_index_in_dim(slots, incoming, (me + n - shift) % n, 0)
    return slots.reshape(n * value.shape[0], width)


def line_all_gather(value, axis):
    n = lax.axis_size(axis)
    me = lax.axis_index(axis)
    rows = value.shape[0]
    right = [(i, i + 1) for i in range(n - 1)]
    left = [(i + 1, i) for i in range(n - 1)]
    slots = jnp.zeros((n + 1, rows) + value.shape[1:], value.dtype)
    slots = lax.dynamic_update_index_in_dim(slots, value, me, 0)
    flow_r, flow_l = value, value
    for step in range(1, n):
        flow_r = lax.ppermute(flow_r, axis, right)
        flow_l = lax.ppermute(flow_l, axis, left)
        at_r = jnp.where(me - step >= 0, me - step, n)
        at_l = jnp.where(me + step < n, me + step, n)
        slots = lax.dynamic_update_index_in_dim(slots, flow_r, at_r, 0)
        slots = lax.dynamic_update_index_in_dim(slots, flow_l, at_l, 0)
    return slots[:n].reshape((n * rows,) + value.shape[1:])


def rows_to_heads(value, axis):
    n = lax.axis_size(axis)
    me = lax.axis_index(axis)
    rows = value.shape[0] // n
    pieces = value.reshape(n, rows, value.shape[1])
    slots = jnp.zeros((n, rows, value.shape[1]), value.dtype)
    slots = lax.dynamic_update_index_in_dim(slots, pieces[me], me, 0)
    for shift in range(1, n):
        outgoing = pieces[(me + shift) % n]
        incoming = lax.ppermute(outgoing, axis, [(i, (i + shift) % n) for i in range(n)])
        slots = lax.dynamic_update_index_in_dim(slots, incoming, (me + n - shift) % n, 0)
    return slots.transpose(1, 0, 2).reshape(rows, n * value.shape[1])


def gather_weight_rows(weight, axis, chip_axis):
    peers = lax.axis_size(chip_axis)
    if peers % 2:
        return line_all_gather(weight, axis)
    core = lax.axis_index(chip_axis) % 2
    half = weight.shape[1] // 2
    mine = lax.dynamic_slice_in_dim(weight, core * half, half, 1)
    gathered = line_all_gather(mine, axis)
    other = lax.ppermute(gathered, chip_axis, [(i, i ^ 1) for i in range(peers)])
    return jnp.where(
        core == 0,
        jnp.concatenate([gathered, other], 1),
        jnp.concatenate([other, gathered], 1),
    )


def direct_all_gather(value, axis):
    n = lax.axis_size(axis)
    if n > 4:
        return line_all_gather(value, axis)
    me = lax.axis_index(axis)
    slots = jnp.zeros((n,) + value.shape, value.dtype)
    slots = lax.dynamic_update_index_in_dim(slots, value, me, 0)
    for shift in range(1, n):
        incoming = lax.ppermute(value, axis, [(i, (i + shift) % n) for i in range(n)])
        slots = lax.dynamic_update_index_in_dim(slots, incoming, (me + n - shift) % n, 0)
    return slots.reshape((n * value.shape[0],) + value.shape[1:])


def doubling_all_gather(value, axis):
    n = lax.axis_size(axis)
    assert n & (n - 1) == 0
    me = lax.axis_index(axis)
    out = value
    k = 1
    while k < n:
        other = lax.ppermute(out, axis, [(i, i ^ k) for i in range(n)])
        low = (me & k) == 0
        out = jnp.where(low, jnp.concatenate([out, other], 0), jnp.concatenate([other, out], 0))
        k *= 2
    return out


def shards(
    sequence, gain_conv, conv_weight, gain_attn, w_qkv, w_out, gain_pool, w_pair, w_up, w_down
):
    pair_count = lax.axis_size("pair")
    seq_count = lax.axis_size("seq")
    row_count = sequence.shape[0]
    channels = sequence.shape[1]
    local_rows = row_count * pair_count
    inputs = sequence.astype(jnp.float32)
    normed = norm_rows(inputs, gain_conv).astype(jnp.bfloat16)
    swapped = permute_all_to_all(normed, "pair")
    padded = padded_2(swapped, (("seq", 0),), DILATION * (conv_weight.shape[0] - 1) // 2)
    with jax.named_scope("conv_reduce"):
        summed = direct_reduce_scatter(conv_rows(padded, conv_weight, local_rows), "pair")
    first_out = (inputs + summed).astype(jnp.bfloat16)
    attn_in = norm_rows(first_out.astype(jnp.float32), gain_attn).astype(jnp.bfloat16)
    with jax.named_scope("attn_in_gather"):
        block_in = direct_all_gather(attn_in, "pair")
    projected = jnp.dot(block_in, w_qkv, preferred_element_type=jnp.float32).astype(jnp.bfloat16)
    head_count = projected.shape[1] // (2 * KEY_SIZE + VALUE_SIZE)
    grouped = projected.reshape(local_rows, head_count, 2 * KEY_SIZE + VALUE_SIZE).transpose(1, 0, 2)
    queries = grouped[:, :, :KEY_SIZE]
    kv = grouped[:, :, KEY_SIZE:]
    late_w_out, kv = lax.optimization_barrier((w_out, kv))
    scale = 1.0 / math.sqrt(KEY_SIZE)

    def attend(state, kv_block):
        running_max, running_sum, weighted = state
        key_block = kv_block[:, :, :KEY_SIZE]
        value_block = kv_block[:, :, KEY_SIZE:]
        scores = (
            jnp.einsum("hqd,hkd->hqk", queries, key_block, preferred_element_type=jnp.float32)
            * scale
        )
        new_max = jnp.maximum(running_max, jnp.max(scores, axis=-1))
        shrink = jnp.exp(running_max - new_max)
        weights = jnp.exp(scores - new_max[:, :, None])
        running_sum = running_sum * shrink + jnp.sum(weights, axis=-1)
        update = jnp.einsum(
            "hqk,hkd->hqd",
            weights.astype(jnp.bfloat16),
            value_block,
            preferred_element_type=jnp.float32,
        )
        weighted = weighted * shrink[:, :, None] + update
        return (new_max, running_sum, weighted)

    state = (
        jnp.full((head_count, local_rows), -1e30, jnp.float32),
        jnp.zeros((head_count, local_rows), jnp.float32),
        jnp.zeros((head_count, local_rows, VALUE_SIZE), jnp.float32),
    )
    with jax.named_scope("kv_ring"):
        forward = [(i, (i + 1) % seq_count) for i in range(seq_count)]
        backward = [((i + 1) % seq_count, i) for i in range(seq_count)]
        half = local_rows // 2
        going = kv[:, :half]
        coming = kv[:, half:]
        for step in range(seq_count):
            if step + 1 < seq_count:
                next_going = lax.ppermute(going, "seq", forward)
                next_coming = lax.ppermute(coming, "seq", backward)
            state = attend(state, going)
            state = attend(state, coming)
            if step + 1 < seq_count:
                going, coming = next_going, next_coming
    running_max, running_sum, weighted = state
    attended = (weighted / running_sum[:, :, None]).astype(jnp.bfloat16)
    attended = attended.transpose(1, 0, 2).reshape(local_rows, head_count * VALUE_SIZE)
    with jax.named_scope("out_projection"):
        full_w_out = gather_weight_rows(late_w_out, "pair", "seq")
        own_heads = rows_to_heads(attended, "pair")
        mixed = jnp.dot(own_heads, full_w_out, preferred_element_type=jnp.float32)
    seq_out = (first_out.astype(jnp.float32) + mixed).astype(jnp.bfloat16)
    bin_count = row_count // POOL
    pooled = jnp.mean(seq_out.astype(jnp.float32).reshape(bin_count, POOL, channels), axis=1)
    bin_norm = norm_rows(pooled, gain_pool).astype(jnp.bfloat16)
    sides = jnp.dot(bin_norm, w_pair, preferred_element_type=jnp.float32).astype(jnp.bfloat16)
    with jax.named_scope("sides_gather"):
        if seq_count > 4:
            all_sides = doubling_all_gather(doubling_all_gather(sides, "pair"), "seq")
        else:
            all_sides = direct_all_gather(direct_all_gather(sides, "pair"), "seq")
    tile_rows = bin_count * pair_count
    tile_cols = bin_count * seq_count
    row_side = lax.dynamic_slice_in_dim(
        all_sides, lax.axis_index("seq") * tile_rows, tile_rows, 0
    )[:, :PAIR_CH]
    column_side = lax.dynamic_slice_in_dim(
        all_sides, lax.axis_index("pair") * tile_cols, tile_cols, 0
    )[:, PAIR_CH:]
    pair_tile = (
        row_side.astype(jnp.float32)[:, None, :] * column_side.astype(jnp.float32)[None, :, :]
    ).astype(jnp.bfloat16)
    flat_rows = pair_tile.reshape(tile_rows * tile_cols, PAIR_CH)
    hidden = jax.nn.relu(jnp.dot(flat_rows, w_up, preferred_element_type=jnp.float32)).astype(
        jnp.bfloat16
    )
    pair_out = flat_rows.astype(jnp.float32) + jnp.dot(
        hidden, w_down, preferred_element_type=jnp.float32
    )
    pair_map = pair_out.astype(jnp.bfloat16).reshape(tile_rows, tile_cols, PAIR_CH)
    return (seq_out, pair_map)


def solution(mesh):
    return jax.shard_map(
        shards,
        mesh=mesh,
        in_specs=(
            P(("groups", "seq", "pair"), None),
            P(),
            P(None, "pair", None),
            P(),
            P(None, "pair"),
            P("pair", None),
            P(),
            P(),
            P(),
            P(),
        ),
        out_specs=(P(("groups", "seq", "pair"), None), P(("groups", "seq"), "pair", None)),
        check_vma=False,
    )
```

```python
import math

import jax
import jax.numpy as jnp
from jax import lax
from jax.sharding import PartitionSpec as P

KEY_SIZE = 128
VALUE_SIZE = 128
DILATION = 4
POOL = 16
PAIR_CH = 128


EPS = 1e-06


def padded_2(value, sides, width):
    for axis, dim in sides:
        peers, length = (lax.axis_size(axis), value.shape[dim])
        up = [(i, (i + 1) % peers) for i in range(peers - 1)]
        down = [(j, i) for i, j in up]
        last = lax.slice_in_dim(value, length - width, length, axis=dim)
        first = lax.slice_in_dim(value, 0, width, axis=dim)
        before = lax.ppermute(last, axis, up)
        after = lax.ppermute(first, axis, down)
        value = jnp.concatenate([before, value, after], axis=dim)
    return value


def norm_rows(values, gain):
    return values * lax.rsqrt(jnp.mean(values * values, axis=-1, keepdims=True) + EPS) * gain


def conv_rows(padded, conv_weight, row_total):
    summed = jnp.zeros((row_total, conv_weight.shape[2]), jnp.float32)
    for offset in range(conv_weight.shape[0]):
        shifted = lax.dynamic_slice_in_dim(padded, offset * DILATION, row_total, 0)
        summed = summed + jnp.dot(shifted, conv_weight[offset], preferred_element_type=jnp.float32)
    return summed


def direct_reduce_scatter(partial, axis):
    n = lax.axis_size(axis)
    me = lax.axis_index(axis)
    rows = partial.shape[0] // n
    blocks = partial.reshape(n, rows, partial.shape[1])
    total = blocks[me]
    for shift in range(1, n):
        outgoing = blocks[(me + shift) % n].astype(jnp.bfloat16)
        incoming = lax.ppermute(outgoing, axis, [(i, (i + shift) % n) for i in range(n)])
        total = total + incoming.astype(jnp.float32)
    return total


def permute_all_to_all(value, axis):
    n = lax.axis_size(axis)
    me = lax.axis_index(axis)
    width = value.shape[1] // n
    pieces = value.reshape(value.shape[0], n, width)
    slots = jnp.zeros((n, value.shape[0], width), value.dtype)
    slots = lax.dynamic_update_index_in_dim(slots, pieces[:, me], me, 0)
    for shift in range(1, n):
        outgoing = pieces[:, (me + shift) % n]
        incoming = lax.ppermute(outgoing, axis, [(i, (i + shift) % n) for i in range(n)])
        slots = lax.dynamic_update_index_in_dim(slots, incoming, (me + n - shift) % n, 0)
    return slots.reshape(n * value.shape[0], width)


def line_all_gather(value, axis):
    n = lax.axis_size(axis)
    me = lax.axis_index(axis)
    rows = value.shape[0]
    right = [(i, i + 1) for i in range(n - 1)]
    left = [(i + 1, i) for i in range(n - 1)]
    slots = jnp.zeros((n + 1, rows) + value.shape[1:], value.dtype)
    slots = lax.dynamic_update_index_in_dim(slots, value, me, 0)
    flow_r, flow_l = value, value
    for step in range(1, n):
        flow_r = lax.ppermute(flow_r, axis, right)
        flow_l = lax.ppermute(flow_l, axis, left)
        at_r = jnp.where(me - step >= 0, me - step, n)
        at_l = jnp.where(me + step < n, me + step, n)
        slots = lax.dynamic_update_index_in_dim(slots, flow_r, at_r, 0)
        slots = lax.dynamic_update_index_in_dim(slots, flow_l, at_l, 0)
    return slots[:n].reshape((n * rows,) + value.shape[1:])


def rows_to_heads(value, axis):
    n = lax.axis_size(axis)
    me = lax.axis_index(axis)
    rows = value.shape[0] // n
    pieces = value.reshape(n, rows, value.shape[1])
    slots = jnp.zeros((n, rows, value.shape[1]), value.dtype)
    slots = lax.dynamic_update_index_in_dim(slots, pieces[me], me, 0)
    for shift in range(1, n):
        outgoing = pieces[(me + shift) % n]
        incoming = lax.ppermute(outgoing, axis, [(i, (i + shift) % n) for i in range(n)])
        slots = lax.dynamic_update_index_in_dim(slots, incoming, (me + n - shift) % n, 0)
    return slots.transpose(1, 0, 2).reshape(rows, n * value.shape[1])


def gather_weight_rows(weight, axis, chip_axis):
    peers = lax.axis_size(chip_axis)
    if peers % 2:
        return line_all_gather(weight, axis)
    core = lax.axis_index(chip_axis) % 2
    half = weight.shape[1] // 2
    mine = lax.dynamic_slice_in_dim(weight, core * half, half, 1)
    gathered = line_all_gather(mine, axis)
    other = lax.ppermute(gathered, chip_axis, [(i, i ^ 1) for i in range(peers)])
    return jnp.where(
        core == 0,
        jnp.concatenate([gathered, other], 1),
        jnp.concatenate([other, gathered], 1),
    )


def direct_all_gather(value, axis):
    n = lax.axis_size(axis)
    if n > 4:
        return line_all_gather(value, axis)
    me = lax.axis_index(axis)
    slots = jnp.zeros((n,) + value.shape, value.dtype)
    slots = lax.dynamic_update_index_in_dim(slots, value, me, 0)
    for shift in range(1, n):
        incoming = lax.ppermute(value, axis, [(i, (i + shift) % n) for i in range(n)])
        slots = lax.dynamic_update_index_in_dim(slots, incoming, (me + n - shift) % n, 0)
    return slots.reshape((n * value.shape[0],) + value.shape[1:])


def doubling_all_gather(value, axis):
    n = lax.axis_size(axis)
    assert n & (n - 1) == 0
    me = lax.axis_index(axis)
    out = value
    k = 1
    while k < n:
        other = lax.ppermute(out, axis, [(i, i ^ k) for i in range(n)])
        low = (me & k) == 0
        out = jnp.where(low, jnp.concatenate([out, other], 0), jnp.concatenate([other, out], 0))
        k *= 2
    return out


def shards(
    sequence, gain_conv, conv_weight, gain_attn, w_qkv, w_out, gain_pool, w_pair, w_up, w_down
):
    pair_count = lax.axis_size("pair")
    seq_count = lax.axis_size("seq")
    row_count = sequence.shape[0]
    channels = sequence.shape[1]
    local_rows = row_count * pair_count
    inputs = sequence.astype(jnp.float32)
    normed = norm_rows(inputs, gain_conv).astype(jnp.bfloat16)
    swapped = permute_all_to_all(normed, "pair")
    padded = padded_2(swapped, (("seq", 0),), DILATION * (conv_weight.shape[0] - 1) // 2)
    with jax.named_scope("conv_reduce"):
        summed = direct_reduce_scatter(conv_rows(padded, conv_weight, local_rows), "pair")
    first_out = (inputs + summed).astype(jnp.bfloat16)
    attn_in = norm_rows(first_out.astype(jnp.float32), gain_attn).astype(jnp.bfloat16)
    with jax.named_scope("attn_in_gather"):
        block_in = direct_all_gather(attn_in, "pair")
    projected = jnp.dot(block_in, w_qkv, preferred_element_type=jnp.float32).astype(jnp.bfloat16)
    head_count = projected.shape[1] // (2 * KEY_SIZE + VALUE_SIZE)
    grouped = projected.reshape(local_rows, head_count, 2 * KEY_SIZE + VALUE_SIZE).transpose(1, 0, 2)
    queries = grouped[:, :, :KEY_SIZE]
    kv = grouped[:, :, KEY_SIZE:]
    scale = 1.0 / math.sqrt(KEY_SIZE)

    def attend(state, kv_block):
        running_max, running_sum, weighted = state
        key_block = kv_block[:, :, :KEY_SIZE]
        value_block = kv_block[:, :, KEY_SIZE:]
        scores = (
            jnp.einsum("hqd,hkd->hqk", queries, key_block, preferred_element_type=jnp.float32)
            * scale
        )
        new_max = jnp.maximum(running_max, jnp.max(scores, axis=-1))
        shrink = jnp.exp(running_max - new_max)
        weights = jnp.exp(scores - new_max[:, :, None])
        running_sum = running_sum * shrink + jnp.sum(weights, axis=-1)
        update = jnp.einsum(
            "hqk,hkd->hqd",
            weights.astype(jnp.bfloat16),
            value_block,
            preferred_element_type=jnp.float32,
        )
        weighted = weighted * shrink[:, :, None] + update
        return (new_max, running_sum, weighted)

    state = (
        jnp.full((head_count, local_rows), -1e30, jnp.float32),
        jnp.zeros((head_count, local_rows), jnp.float32),
        jnp.zeros((head_count, local_rows, VALUE_SIZE), jnp.float32),
    )
    with jax.named_scope("kv_ring"):
        forward = [(i, (i + 1) % seq_count) for i in range(seq_count)]
        backward = [((i + 1) % seq_count, i) for i in range(seq_count)]
        half = local_rows // 2
        going = kv[:, :half]
        coming = kv[:, half:]
        for step in range(seq_count):
            if step + 1 < seq_count:
                next_going = lax.ppermute(going, "seq", forward)
                next_coming = lax.ppermute(coming, "seq", backward)
            state = attend(state, going)
            state = attend(state, coming)
            if step + 1 < seq_count:
                going, coming = next_going, next_coming
    running_max, running_sum, weighted = state
    attended = (weighted / running_sum[:, :, None]).astype(jnp.bfloat16)
    attended = attended.transpose(1, 0, 2).reshape(local_rows, head_count * VALUE_SIZE)
    with jax.named_scope("out_reduce"):
        mixed = direct_reduce_scatter(
            jnp.dot(attended, w_out, preferred_element_type=jnp.float32), "pair"
        )
    seq_out = (first_out.astype(jnp.float32) + mixed).astype(jnp.bfloat16)
    bin_count = row_count // POOL
    pooled = jnp.mean(seq_out.astype(jnp.float32).reshape(bin_count, POOL, channels), axis=1)
    bin_norm = norm_rows(pooled, gain_pool).astype(jnp.bfloat16)
    sides = jnp.dot(bin_norm, w_pair, preferred_element_type=jnp.float32).astype(jnp.bfloat16)
    with jax.named_scope("sides_gather"):
        if seq_count > 4:
            all_sides = doubling_all_gather(doubling_all_gather(sides, "pair"), "seq")
        else:
            all_sides = direct_all_gather(direct_all_gather(sides, "pair"), "seq")
    tile_rows = bin_count * pair_count
    tile_cols = bin_count * seq_count
    row_side = lax.dynamic_slice_in_dim(
        all_sides, lax.axis_index("seq") * tile_rows, tile_rows, 0
    )[:, :PAIR_CH]
    column_side = lax.dynamic_slice_in_dim(
        all_sides, lax.axis_index("pair") * tile_cols, tile_cols, 0
    )[:, PAIR_CH:]
    pair_tile = (
        row_side.astype(jnp.float32)[:, None, :] * column_side.astype(jnp.float32)[None, :, :]
    ).astype(jnp.bfloat16)
    flat_rows = pair_tile.reshape(tile_rows * tile_cols, PAIR_CH)
    hidden = jax.nn.relu(jnp.dot(flat_rows, w_up, preferred_element_type=jnp.float32)).astype(
        jnp.bfloat16
    )
    pair_out = flat_rows.astype(jnp.float32) + jnp.dot(
        hidden, w_down, preferred_element_type=jnp.float32
    )
    pair_map = pair_out.astype(jnp.bfloat16).reshape(tile_rows, tile_cols, PAIR_CH)
    return (seq_out, pair_map)


def solution(mesh):
    return jax.shard_map(
        shards,
        mesh=mesh,
        in_specs=(
            P(("groups", "seq", "pair"), None),
            P(),
            P(None, "pair", None),
            P(),
            P(None, "pair"),
            P("pair", None),
            P(),
            P(),
            P(),
            P(),
        ),
        out_specs=(P(("groups", "seq", "pair"), None), P(("groups", "seq"), "pair", None)),
        check_vma=False,
    )
```

```python
import math

import jax
import jax.numpy as jnp
from jax import lax
from jax.sharding import PartitionSpec as P

KEY_SIZE = 128
VALUE_SIZE = 128
DILATION = 4
POOL = 16
PAIR_CH = 128


EPS = 1e-06


def padded_2(value, sides, width):
    for axis, dim in sides:
        peers, length = (lax.axis_size(axis), value.shape[dim])
        up = [(i, (i + 1) % peers) for i in range(peers - 1)]
        down = [(j, i) for i, j in up]
        last = lax.slice_in_dim(value, length - width, length, axis=dim)
        first = lax.slice_in_dim(value, 0, width, axis=dim)
        before = lax.ppermute(last, axis, up)
        after = lax.ppermute(first, axis, down)
        value = jnp.concatenate([before, value, after], axis=dim)
    return value


def norm_rows(values, gain):
    return values * lax.rsqrt(jnp.mean(values * values, axis=-1, keepdims=True) + EPS) * gain


def conv_rows(padded, conv_weight, row_total):
    summed = jnp.zeros((row_total, conv_weight.shape[2]), jnp.float32)
    for offset in range(conv_weight.shape[0]):
        shifted = lax.dynamic_slice_in_dim(padded, offset * DILATION, row_total, 0)
        summed = summed + jnp.dot(shifted, conv_weight[offset], preferred_element_type=jnp.float32)
    return summed


def direct_reduce_scatter_of(block_of, axis):
    n = lax.axis_size(axis)
    me = lax.axis_index(axis)
    incoming = []
    for shift in range(1, n):
        outgoing = block_of((me + shift) % n).astype(jnp.bfloat16)
        incoming.append(lax.ppermute(outgoing, axis, [(i, (i + shift) % n) for i in range(n)]))
    total = block_of(me)
    for piece in incoming:
        total = total + piece.astype(jnp.float32)
    return total


def conv_block(padded, conv_weight, block, rows):
    start = block * rows
    summed = jnp.zeros((rows, conv_weight.shape[2]), jnp.float32)
    for offset in range(conv_weight.shape[0]):
        shifted = lax.dynamic_slice_in_dim(padded, start + offset * DILATION, rows, 0)
        summed = summed + jnp.dot(shifted, conv_weight[offset], preferred_element_type=jnp.float32)
    return summed


def direct_reduce_scatter(partial, axis):
    n = lax.axis_size(axis)
    me = lax.axis_index(axis)
    rows = partial.shape[0] // n
    blocks = partial.reshape(n, rows, partial.shape[1])
    total = blocks[me]
    for shift in range(1, n):
        outgoing = blocks[(me + shift) % n].astype(jnp.bfloat16)
        incoming = lax.ppermute(outgoing, axis, [(i, (i + shift) % n) for i in range(n)])
        total = total + incoming.astype(jnp.float32)
    return total


def permute_all_to_all(value, axis):
    n = lax.axis_size(axis)
    me = lax.axis_index(axis)
    width = value.shape[1] // n
    pieces = value.reshape(value.shape[0], n, width)
    slots = jnp.zeros((n, value.shape[0], width), value.dtype)
    slots = lax.dynamic_update_index_in_dim(slots, pieces[:, me], me, 0)
    for shift in range(1, n):
        outgoing = pieces[:, (me + shift) % n]
        incoming = lax.ppermute(outgoing, axis, [(i, (i + shift) % n) for i in range(n)])
        slots = lax.dynamic_update_index_in_dim(slots, incoming, (me + n - shift) % n, 0)
    return slots.reshape(n * value.shape[0], width)


def line_all_gather(value, axis):
    n = lax.axis_size(axis)
    me = lax.axis_index(axis)
    rows = value.shape[0]
    right = [(i, i + 1) for i in range(n - 1)]
    left = [(i + 1, i) for i in range(n - 1)]
    slots = jnp.zeros((n + 1, rows) + value.shape[1:], value.dtype)
    slots = lax.dynamic_update_index_in_dim(slots, value, me, 0)
    flow_r, flow_l = value, value
    for step in range(1, n):
        flow_r = lax.ppermute(flow_r, axis, right)
        flow_l = lax.ppermute(flow_l, axis, left)
        at_r = jnp.where(me - step >= 0, me - step, n)
        at_l = jnp.where(me + step < n, me + step, n)
        slots = lax.dynamic_update_index_in_dim(slots, flow_r, at_r, 0)
        slots = lax.dynamic_update_index_in_dim(slots, flow_l, at_l, 0)
    return slots[:n].reshape((n * rows,) + value.shape[1:])


def rows_to_heads(value, axis):
    n = lax.axis_size(axis)
    me = lax.axis_index(axis)
    rows = value.shape[0] // n
    pieces = value.reshape(n, rows, value.shape[1])
    slots = jnp.zeros((n, rows, value.shape[1]), value.dtype)
    slots = lax.dynamic_update_index_in_dim(slots, pieces[me], me, 0)
    for shift in range(1, n):
        outgoing = pieces[(me + shift) % n]
        incoming = lax.ppermute(outgoing, axis, [(i, (i + shift) % n) for i in range(n)])
        slots = lax.dynamic_update_index_in_dim(slots, incoming, (me + n - shift) % n, 0)
    return slots.transpose(1, 0, 2).reshape(rows, n * value.shape[1])


def gather_weight_rows(weight, axis, chip_axis):
    peers = lax.axis_size(chip_axis)
    if peers % 2:
        return line_all_gather(weight, axis)
    core = lax.axis_index(chip_axis) % 2
    half = weight.shape[1] // 2
    mine = lax.dynamic_slice_in_dim(weight, core * half, half, 1)
    gathered = line_all_gather(mine, axis)
    other = lax.ppermute(gathered, chip_axis, [(i, i ^ 1) for i in range(peers)])
    return jnp.where(
        core == 0,
        jnp.concatenate([gathered, other], 1),
        jnp.concatenate([other, gathered], 1),
    )


def projected_all_gather(value, weight, axis):
    n = lax.axis_size(axis)
    if n > 4:
        gathered = line_all_gather(value, axis)
        return jnp.dot(gathered, weight, preferred_element_type=jnp.float32).astype(jnp.bfloat16)
    me = lax.axis_index(axis)

    def project(rows):
        return jnp.dot(rows, weight, preferred_element_type=jnp.float32).astype(jnp.bfloat16)

    slots = jnp.zeros((n, value.shape[0], weight.shape[1]), jnp.bfloat16)
    for shift in range(1, n):
        incoming = lax.ppermute(value, axis, [(i, (i + shift) % n) for i in range(n)])
        slots = lax.dynamic_update_index_in_dim(slots, project(incoming), (me + n - shift) % n, 0)
    slots = lax.dynamic_update_index_in_dim(slots, project(value), me, 0)
    return slots.reshape(n * value.shape[0], weight.shape[1])


def direct_all_gather(value, axis):
    n = lax.axis_size(axis)
    if n > 4:
        return line_all_gather(value, axis)
    me = lax.axis_index(axis)
    slots = jnp.zeros((n,) + value.shape, value.dtype)
    slots = lax.dynamic_update_index_in_dim(slots, value, me, 0)
    for shift in range(1, n):
        incoming = lax.ppermute(value, axis, [(i, (i + shift) % n) for i in range(n)])
        slots = lax.dynamic_update_index_in_dim(slots, incoming, (me + n - shift) % n, 0)
    return slots.reshape((n * value.shape[0],) + value.shape[1:])


def doubling_all_gather(value, axis):
    n = lax.axis_size(axis)
    assert n & (n - 1) == 0
    me = lax.axis_index(axis)
    out = value
    k = 1
    while k < n:
        other = lax.ppermute(out, axis, [(i, i ^ k) for i in range(n)])
        low = (me & k) == 0
        out = jnp.where(low, jnp.concatenate([out, other], 0), jnp.concatenate([other, out], 0))
        k *= 2
    return out


def shards(
    sequence, gain_conv, conv_weight, gain_attn, w_qkv, w_out, gain_pool, w_pair, w_up, w_down
):
    pair_count = lax.axis_size("pair")
    seq_count = lax.axis_size("seq")
    row_count = sequence.shape[0]
    channels = sequence.shape[1]
    local_rows = row_count * pair_count
    inputs = sequence.astype(jnp.float32)
    normed = norm_rows(inputs, gain_conv).astype(jnp.bfloat16)
    swapped = permute_all_to_all(normed, "pair")
    padded = padded_2(swapped, (("seq", 0),), DILATION * (conv_weight.shape[0] - 1) // 2)
    with jax.named_scope("conv_reduce"):
        summed = direct_reduce_scatter_of(
            lambda block: conv_block(padded, conv_weight, block, row_count), "pair"
        )
    first_out = (inputs + summed).astype(jnp.bfloat16)
    attn_in = norm_rows(first_out.astype(jnp.float32), gain_attn).astype(jnp.bfloat16)
    with jax.named_scope("attn_in_gather"):
        projected = projected_all_gather(attn_in, w_qkv, "pair")
    head_count = projected.shape[1] // (2 * KEY_SIZE + VALUE_SIZE)
    grouped = projected.reshape(local_rows, head_count, 2 * KEY_SIZE + VALUE_SIZE).transpose(1, 0, 2)
    queries = grouped[:, :, :KEY_SIZE]
    kv = grouped[:, :, KEY_SIZE:]
    scale = 1.0 / math.sqrt(KEY_SIZE)

    def attend(state, kv_block):
        running_max, running_sum, weighted = state
        key_block = kv_block[:, :, :KEY_SIZE]
        value_block = kv_block[:, :, KEY_SIZE:]
        scores = (
            jnp.einsum("hqd,hkd->hqk", queries, key_block, preferred_element_type=jnp.float32)
            * scale
        )
        new_max = jnp.maximum(running_max, jnp.max(scores, axis=-1))
        shrink = jnp.exp(running_max - new_max)
        weights = jnp.exp(scores - new_max[:, :, None])
        running_sum = running_sum * shrink + jnp.sum(weights, axis=-1)
        update = jnp.einsum(
            "hqk,hkd->hqd",
            weights.astype(jnp.bfloat16),
            value_block,
            preferred_element_type=jnp.float32,
        )
        weighted = weighted * shrink[:, :, None] + update
        return (new_max, running_sum, weighted)

    state = (
        jnp.full((head_count, local_rows), -1e30, jnp.float32),
        jnp.zeros((head_count, local_rows), jnp.float32),
        jnp.zeros((head_count, local_rows, VALUE_SIZE), jnp.float32),
    )
    with jax.named_scope("kv_ring"):
        forward = [(i, (i + 1) % seq_count) for i in range(seq_count)]
        backward = [((i + 1) % seq_count, i) for i in range(seq_count)]
        half = local_rows // 2
        going = kv[:, :half]
        coming = kv[:, half:]
        for step in range(seq_count):
            if step + 1 < seq_count:
                next_going = lax.ppermute(going, "seq", forward)
                next_coming = lax.ppermute(coming, "seq", backward)
            state = attend(state, going)
            state = attend(state, coming)
            if step + 1 < seq_count:
                going, coming = next_going, next_coming
    running_max, running_sum, weighted = state
    attended = (weighted / running_sum[:, :, None]).astype(jnp.bfloat16)
    attended = attended.transpose(1, 0, 2).reshape(local_rows, head_count * VALUE_SIZE)
    with jax.named_scope("out_projection"):
        late_w_out, unused = lax.optimization_barrier((w_out, kv))
        full_w_out = gather_weight_rows(late_w_out, "pair", "seq")
        own_heads = rows_to_heads(attended, "pair")
        mixed = jnp.dot(own_heads, full_w_out, preferred_element_type=jnp.float32)
    seq_out = (first_out.astype(jnp.float32) + mixed).astype(jnp.bfloat16)
    bin_count = row_count // POOL
    pooled = jnp.mean(seq_out.astype(jnp.float32).reshape(bin_count, POOL, channels), axis=1)
    bin_norm = norm_rows(pooled, gain_pool).astype(jnp.bfloat16)
    sides = jnp.dot(bin_norm, w_pair, preferred_element_type=jnp.float32).astype(jnp.bfloat16)
    with jax.named_scope("sides_gather"):
        if seq_count > 4:
            all_sides = doubling_all_gather(doubling_all_gather(sides, "pair"), "seq")
        else:
            all_sides = direct_all_gather(direct_all_gather(sides, "pair"), "seq")
    tile_rows = bin_count * pair_count
    tile_cols = bin_count * seq_count
    row_side = lax.dynamic_slice_in_dim(
        all_sides, lax.axis_index("seq") * tile_rows, tile_rows, 0
    )[:, :PAIR_CH]
    column_side = lax.dynamic_slice_in_dim(
        all_sides, lax.axis_index("pair") * tile_cols, tile_cols, 0
    )[:, PAIR_CH:]
    pair_tile = (
        row_side.astype(jnp.float32)[:, None, :] * column_side.astype(jnp.float32)[None, :, :]
    ).astype(jnp.bfloat16)
    flat_rows = pair_tile.reshape(tile_rows * tile_cols, PAIR_CH)
    hidden = jax.nn.relu(jnp.dot(flat_rows, w_up, preferred_element_type=jnp.float32)).astype(
        jnp.bfloat16
    )
    pair_out = flat_rows.astype(jnp.float32) + jnp.dot(
        hidden, w_down, preferred_element_type=jnp.float32
    )
    pair_map = pair_out.astype(jnp.bfloat16).reshape(tile_rows, tile_cols, PAIR_CH)
    return (seq_out, pair_map)


def solution(mesh):
    return jax.shard_map(
        shards,
        mesh=mesh,
        in_specs=(
            P(("groups", "seq", "pair"), None),
            P(),
            P(None, "pair", None),
            P(),
            P(None, "pair"),
            P("pair", None),
            P(),
            P(),
            P(),
            P(),
        ),
        out_specs=(P(("groups", "seq", "pair"), None), P(("groups", "seq"), "pair", None)),
        check_vma=False,
    )
```

```python
import math

import jax
import jax.numpy as jnp
from jax import lax
from jax.sharding import PartitionSpec as P

KEY_SIZE = 128
VALUE_SIZE = 128
DILATION = 4
POOL = 16
PAIR_CH = 128


EPS = 1e-06


def padded_2(value, sides, width):
    for axis, dim in sides:
        peers, length = (lax.axis_size(axis), value.shape[dim])
        up = [(i, (i + 1) % peers) for i in range(peers - 1)]
        down = [(j, i) for i, j in up]
        last = lax.slice_in_dim(value, length - width, length, axis=dim)
        first = lax.slice_in_dim(value, 0, width, axis=dim)
        before = lax.ppermute(last, axis, up)
        after = lax.ppermute(first, axis, down)
        value = jnp.concatenate([before, value, after], axis=dim)
    return value


def norm_rows(values, gain):
    return values * lax.rsqrt(jnp.mean(values * values, axis=-1, keepdims=True) + EPS) * gain


def conv_rows(padded, conv_weight, row_total):
    summed = jnp.zeros((row_total, conv_weight.shape[2]), jnp.float32)
    for offset in range(conv_weight.shape[0]):
        shifted = lax.dynamic_slice_in_dim(padded, offset * DILATION, row_total, 0)
        summed = summed + jnp.dot(shifted, conv_weight[offset], preferred_element_type=jnp.float32)
    return summed


def direct_reduce_scatter(partial, axis):
    n = lax.axis_size(axis)
    me = lax.axis_index(axis)
    rows = partial.shape[0] // n
    blocks = partial.reshape(n, rows, partial.shape[1])
    total = blocks[me]
    for shift in range(1, n):
        outgoing = blocks[(me + shift) % n].astype(jnp.bfloat16)
        incoming = lax.ppermute(outgoing, axis, [(i, (i + shift) % n) for i in range(n)])
        total = total + incoming.astype(jnp.float32)
    return total


def permute_all_to_all(value, axis):
    n = lax.axis_size(axis)
    me = lax.axis_index(axis)
    width = value.shape[1] // n
    pieces = value.reshape(value.shape[0], n, width)
    slots = jnp.zeros((n, value.shape[0], width), value.dtype)
    slots = lax.dynamic_update_index_in_dim(slots, pieces[:, me], me, 0)
    for shift in range(1, n):
        outgoing = pieces[:, (me + shift) % n]
        incoming = lax.ppermute(outgoing, axis, [(i, (i + shift) % n) for i in range(n)])
        slots = lax.dynamic_update_index_in_dim(slots, incoming, (me + n - shift) % n, 0)
    return slots.reshape(n * value.shape[0], width)


def line_all_gather(value, axis):
    n = lax.axis_size(axis)
    me = lax.axis_index(axis)
    rows = value.shape[0]
    right = [(i, i + 1) for i in range(n - 1)]
    left = [(i + 1, i) for i in range(n - 1)]
    slots = jnp.zeros((n + 1, rows) + value.shape[1:], value.dtype)
    slots = lax.dynamic_update_index_in_dim(slots, value, me, 0)
    flow_r, flow_l = value, value
    for step in range(1, n):
        flow_r = lax.ppermute(flow_r, axis, right)
        flow_l = lax.ppermute(flow_l, axis, left)
        at_r = jnp.where(me - step >= 0, me - step, n)
        at_l = jnp.where(me + step < n, me + step, n)
        slots = lax.dynamic_update_index_in_dim(slots, flow_r, at_r, 0)
        slots = lax.dynamic_update_index_in_dim(slots, flow_l, at_l, 0)
    return slots[:n].reshape((n * rows,) + value.shape[1:])


def rows_to_heads(value, axis):
    n = lax.axis_size(axis)
    me = lax.axis_index(axis)
    rows = value.shape[0] // n
    pieces = value.reshape(n, rows, value.shape[1])
    slots = jnp.zeros((n, rows, value.shape[1]), value.dtype)
    slots = lax.dynamic_update_index_in_dim(slots, pieces[me], me, 0)
    for shift in range(1, n):
        outgoing = pieces[(me + shift) % n]
        incoming = lax.ppermute(outgoing, axis, [(i, (i + shift) % n) for i in range(n)])
        slots = lax.dynamic_update_index_in_dim(slots, incoming, (me + n - shift) % n, 0)
    return slots.transpose(1, 0, 2).reshape(rows, n * value.shape[1])


def gather_weight_rows(weight, axis, chip_axis):
    peers = lax.axis_size(chip_axis)
    if peers % 2:
        return line_all_gather(weight, axis)
    core = lax.axis_index(chip_axis) % 2
    half = weight.shape[1] // 2
    mine = lax.dynamic_slice_in_dim(weight, core * half, half, 1)
    gathered = lax.all_gather(mine, axis, axis=0, tiled=True)
    other = lax.ppermute(gathered, chip_axis, [(i, i ^ 1) for i in range(peers)])
    return jnp.where(
        core == 0,
        jnp.concatenate([gathered, other], 1),
        jnp.concatenate([other, gathered], 1),
    )


def direct_all_gather(value, axis):
    n = lax.axis_size(axis)
    if n > 4:
        return line_all_gather(value, axis)
    me = lax.axis_index(axis)
    slots = jnp.zeros((n,) + value.shape, value.dtype)
    slots = lax.dynamic_update_index_in_dim(slots, value, me, 0)
    for shift in range(1, n):
        incoming = lax.ppermute(value, axis, [(i, (i + shift) % n) for i in range(n)])
        slots = lax.dynamic_update_index_in_dim(slots, incoming, (me + n - shift) % n, 0)
    return slots.reshape((n * value.shape[0],) + value.shape[1:])


def doubling_all_gather(value, axis):
    n = lax.axis_size(axis)
    assert n & (n - 1) == 0
    me = lax.axis_index(axis)
    out = value
    k = 1
    while k < n:
        other = lax.ppermute(out, axis, [(i, i ^ k) for i in range(n)])
        low = (me & k) == 0
        out = jnp.where(low, jnp.concatenate([out, other], 0), jnp.concatenate([other, out], 0))
        k *= 2
    return out


def shards(
    sequence, gain_conv, conv_weight, gain_attn, w_qkv, w_out, gain_pool, w_pair, w_up, w_down
):
    pair_count = lax.axis_size("pair")
    seq_count = lax.axis_size("seq")
    row_count = sequence.shape[0]
    channels = sequence.shape[1]
    local_rows = row_count * pair_count
    inputs = sequence.astype(jnp.float32)
    normed = norm_rows(inputs, gain_conv).astype(jnp.bfloat16)
    swapped = permute_all_to_all(normed, "pair")
    padded = padded_2(swapped, (("seq", 0),), DILATION * (conv_weight.shape[0] - 1) // 2)
    with jax.named_scope("conv_reduce"):
        summed = direct_reduce_scatter(conv_rows(padded, conv_weight, local_rows), "pair")
    first_out = (inputs + summed).astype(jnp.bfloat16)
    attn_in = norm_rows(first_out.astype(jnp.float32), gain_attn).astype(jnp.bfloat16)
    with jax.named_scope("attn_in_gather"):
        block_in = direct_all_gather(attn_in, "pair")
    projected = jnp.dot(block_in, w_qkv, preferred_element_type=jnp.float32).astype(jnp.bfloat16)
    head_count = projected.shape[1] // (2 * KEY_SIZE + VALUE_SIZE)
    grouped = projected.reshape(local_rows, head_count, 2 * KEY_SIZE + VALUE_SIZE).transpose(1, 0, 2)
    queries = grouped[:, :, :KEY_SIZE]
    kv = grouped[:, :, KEY_SIZE:]
    scale = 1.0 / math.sqrt(KEY_SIZE)

    def attend(state, kv_block):
        running_max, running_sum, weighted = state
        key_block = kv_block[:, :, :KEY_SIZE]
        value_block = kv_block[:, :, KEY_SIZE:]
        scores = (
            jnp.einsum("hqd,hkd->hqk", queries, key_block, preferred_element_type=jnp.float32)
            * scale
        )
        new_max = jnp.maximum(running_max, jnp.max(scores, axis=-1))
        shrink = jnp.exp(running_max - new_max)
        weights = jnp.exp(scores - new_max[:, :, None])
        running_sum = running_sum * shrink + jnp.sum(weights, axis=-1)
        update = jnp.einsum(
            "hqk,hkd->hqd",
            weights.astype(jnp.bfloat16),
            value_block,
            preferred_element_type=jnp.float32,
        )
        weighted = weighted * shrink[:, :, None] + update
        return (new_max, running_sum, weighted)

    state = (
        jnp.full((head_count, local_rows), -1e30, jnp.float32),
        jnp.zeros((head_count, local_rows), jnp.float32),
        jnp.zeros((head_count, local_rows, VALUE_SIZE), jnp.float32),
    )
    with jax.named_scope("kv_ring"):
        forward = [(i, (i + 1) % seq_count) for i in range(seq_count)]
        backward = [((i + 1) % seq_count, i) for i in range(seq_count)]
        half = local_rows // 2
        going = kv[:, :half]
        coming = kv[:, half:]
        for step in range(seq_count):
            if step + 1 < seq_count:
                next_going = lax.ppermute(going, "seq", forward)
                next_coming = lax.ppermute(coming, "seq", backward)
            state = attend(state, going)
            state = attend(state, coming)
            if step + 1 < seq_count:
                going, coming = next_going, next_coming
    running_max, running_sum, weighted = state
    attended = (weighted / running_sum[:, :, None]).astype(jnp.bfloat16)
    attended = attended.transpose(1, 0, 2).reshape(local_rows, head_count * VALUE_SIZE)
    with jax.named_scope("out_projection"):
        late_w_out, unused = lax.optimization_barrier((w_out, kv))
        full_w_out = gather_weight_rows(late_w_out, "pair", "seq")
        own_heads = rows_to_heads(attended, "pair")
        mixed = jnp.dot(own_heads, full_w_out, preferred_element_type=jnp.float32)
    seq_out = (first_out.astype(jnp.float32) + mixed).astype(jnp.bfloat16)
    bin_count = row_count // POOL
    pooled = jnp.mean(seq_out.astype(jnp.float32).reshape(bin_count, POOL, channels), axis=1)
    bin_norm = norm_rows(pooled, gain_pool).astype(jnp.bfloat16)
    sides = jnp.dot(bin_norm, w_pair, preferred_element_type=jnp.float32).astype(jnp.bfloat16)
    with jax.named_scope("sides_gather"):
        if seq_count > 4:
            all_sides = doubling_all_gather(doubling_all_gather(sides, "pair"), "seq")
        else:
            all_sides = direct_all_gather(direct_all_gather(sides, "pair"), "seq")
    tile_rows = bin_count * pair_count
    tile_cols = bin_count * seq_count
    row_side = lax.dynamic_slice_in_dim(
        all_sides, lax.axis_index("seq") * tile_rows, tile_rows, 0
    )[:, :PAIR_CH]
    column_side = lax.dynamic_slice_in_dim(
        all_sides, lax.axis_index("pair") * tile_cols, tile_cols, 0
    )[:, PAIR_CH:]
    pair_tile = (
        row_side.astype(jnp.float32)[:, None, :] * column_side.astype(jnp.float32)[None, :, :]
    ).astype(jnp.bfloat16)
    flat_rows = pair_tile.reshape(tile_rows * tile_cols, PAIR_CH)
    hidden = jax.nn.relu(jnp.dot(flat_rows, w_up, preferred_element_type=jnp.float32)).astype(
        jnp.bfloat16
    )
    pair_out = flat_rows.astype(jnp.float32) + jnp.dot(
        hidden, w_down, preferred_element_type=jnp.float32
    )
    pair_map = pair_out.astype(jnp.bfloat16).reshape(tile_rows, tile_cols, PAIR_CH)
    return (seq_out, pair_map)


def solution(mesh):
    return jax.shard_map(
        shards,
        mesh=mesh,
        in_specs=(
            P(("groups", "seq", "pair"), None),
            P(),
            P(None, "pair", None),
            P(),
            P(None, "pair"),
            P("pair", None),
            P(),
            P(),
            P(),
            P(),
        ),
        out_specs=(P(("groups", "seq", "pair"), None), P(("groups", "seq"), "pair", None)),
        check_vma=False,
    )
```

```python
import math

import jax
import jax.numpy as jnp
from jax import lax
from jax.sharding import PartitionSpec as P

KEY_SIZE = 128
VALUE_SIZE = 128
DILATION = 4
POOL = 16
PAIR_CH = 128


EPS = 1e-06


def padded_2(value, sides, width):
    for axis, dim in sides:
        peers, length = (lax.axis_size(axis), value.shape[dim])
        up = [(i, (i + 1) % peers) for i in range(peers - 1)]
        down = [(j, i) for i, j in up]
        last = lax.slice_in_dim(value, length - width, length, axis=dim)
        first = lax.slice_in_dim(value, 0, width, axis=dim)
        before = lax.ppermute(last, axis, up)
        after = lax.ppermute(first, axis, down)
        value = jnp.concatenate([before, value, after], axis=dim)
    return value


def norm_rows(values, gain):
    return values * lax.rsqrt(jnp.mean(values * values, axis=-1, keepdims=True) + EPS) * gain


def conv_rows(padded, conv_weight, row_total):
    summed = jnp.zeros((row_total, conv_weight.shape[2]), jnp.float32)
    for offset in range(conv_weight.shape[0]):
        shifted = lax.dynamic_slice_in_dim(padded, offset * DILATION, row_total, 0)
        summed = summed + jnp.dot(shifted, conv_weight[offset], preferred_element_type=jnp.float32)
    return summed


def direct_reduce_scatter(partial, axis):
    n = lax.axis_size(axis)
    me = lax.axis_index(axis)
    rows = partial.shape[0] // n
    blocks = partial.reshape(n, rows, partial.shape[1])
    total = blocks[me]
    for shift in range(1, n):
        outgoing = blocks[(me + shift) % n].astype(jnp.bfloat16)
        incoming = lax.ppermute(outgoing, axis, [(i, (i + shift) % n) for i in range(n)])
        total = total + incoming.astype(jnp.float32)
    return total


def permute_all_to_all(value, axis):
    n = lax.axis_size(axis)
    me = lax.axis_index(axis)
    width = value.shape[1] // n
    pieces = value.reshape(value.shape[0], n, width)
    slots = jnp.zeros((n, value.shape[0], width), value.dtype)
    slots = lax.dynamic_update_index_in_dim(slots, pieces[:, me], me, 0)
    for shift in range(1, n):
        outgoing = pieces[:, (me + shift) % n]
        incoming = lax.ppermute(outgoing, axis, [(i, (i + shift) % n) for i in range(n)])
        slots = lax.dynamic_update_index_in_dim(slots, incoming, (me + n - shift) % n, 0)
    return slots.reshape(n * value.shape[0], width)


def line_all_gather(value, axis):
    n = lax.axis_size(axis)
    me = lax.axis_index(axis)
    rows = value.shape[0]
    right = [(i, i + 1) for i in range(n - 1)]
    left = [(i + 1, i) for i in range(n - 1)]
    slots = jnp.zeros((n + 1, rows) + value.shape[1:], value.dtype)
    slots = lax.dynamic_update_index_in_dim(slots, value, me, 0)
    flow_r, flow_l = value, value
    for step in range(1, n):
        flow_r = lax.ppermute(flow_r, axis, right)
        flow_l = lax.ppermute(flow_l, axis, left)
        at_r = jnp.where(me - step >= 0, me - step, n)
        at_l = jnp.where(me + step < n, me + step, n)
        slots = lax.dynamic_update_index_in_dim(slots, flow_r, at_r, 0)
        slots = lax.dynamic_update_index_in_dim(slots, flow_l, at_l, 0)
    return slots[:n].reshape((n * rows,) + value.shape[1:])


def rows_to_heads(value, axis):
    n = lax.axis_size(axis)
    me = lax.axis_index(axis)
    rows = value.shape[0] // n
    pieces = value.reshape(n, rows, value.shape[1])
    slots = jnp.zeros((n, rows, value.shape[1]), value.dtype)
    slots = lax.dynamic_update_index_in_dim(slots, pieces[me], me, 0)
    for shift in range(1, n):
        outgoing = pieces[(me + shift) % n]
        incoming = lax.ppermute(outgoing, axis, [(i, (i + shift) % n) for i in range(n)])
        slots = lax.dynamic_update_index_in_dim(slots, incoming, (me + n - shift) % n, 0)
    return slots.transpose(1, 0, 2).reshape(rows, n * value.shape[1])


def gather_weight_rows(weight, axis, chip_axis):
    peers = lax.axis_size(chip_axis)
    if peers % 2:
        return line_all_gather(weight, axis)
    core = lax.axis_index(chip_axis) % 2
    half = weight.shape[1] // 2
    mine = lax.dynamic_slice_in_dim(weight, core * half, half, 1)
    gathered = line_all_gather(mine, axis)
    other = lax.ppermute(gathered, chip_axis, [(i, i ^ 1) for i in range(peers)])
    return jnp.where(
        core == 0,
        jnp.concatenate([gathered, other], 1),
        jnp.concatenate([other, gathered], 1),
    )


def rotated_all_gather(value, axis):
    n = lax.axis_size(axis)
    pieces = [value]
    for shift in range(1, n):
        pieces.append(lax.ppermute(value, axis, [(i, (i + shift) % n) for i in range(n)]))
    return jnp.concatenate(pieces, 0)


def direct_all_gather(value, axis):
    n = lax.axis_size(axis)
    if n > 4:
        return line_all_gather(value, axis)
    me = lax.axis_index(axis)
    slots = jnp.zeros((n,) + value.shape, value.dtype)
    slots = lax.dynamic_update_index_in_dim(slots, value, me, 0)
    for shift in range(1, n):
        incoming = lax.ppermute(value, axis, [(i, (i + shift) % n) for i in range(n)])
        slots = lax.dynamic_update_index_in_dim(slots, incoming, (me + n - shift) % n, 0)
    return slots.reshape((n * value.shape[0],) + value.shape[1:])


def doubling_all_gather(value, axis):
    n = lax.axis_size(axis)
    assert n & (n - 1) == 0
    me = lax.axis_index(axis)
    out = value
    k = 1
    while k < n:
        other = lax.ppermute(out, axis, [(i, i ^ k) for i in range(n)])
        low = (me & k) == 0
        out = jnp.where(low, jnp.concatenate([out, other], 0), jnp.concatenate([other, out], 0))
        k *= 2
    return out


def shards(
    sequence, gain_conv, conv_weight, gain_attn, w_qkv, w_out, gain_pool, w_pair, w_up, w_down
):
    pair_count = lax.axis_size("pair")
    seq_count = lax.axis_size("seq")
    row_count = sequence.shape[0]
    channels = sequence.shape[1]
    local_rows = row_count * pair_count
    inputs = sequence.astype(jnp.float32)
    normed = norm_rows(inputs, gain_conv).astype(jnp.bfloat16)
    swapped = permute_all_to_all(normed, "pair")
    padded = padded_2(swapped, (("seq", 0),), DILATION * (conv_weight.shape[0] - 1) // 2)
    with jax.named_scope("conv_reduce"):
        summed = direct_reduce_scatter(conv_rows(padded, conv_weight, local_rows), "pair")
    first_out = (inputs + summed).astype(jnp.bfloat16)
    attn_in = norm_rows(first_out.astype(jnp.float32), gain_attn).astype(jnp.bfloat16)
    with jax.named_scope("attn_in_gather"):
        rotated = pair_count <= 4
        if rotated:
            block_in = rotated_all_gather(attn_in, "pair")
        else:
            block_in = direct_all_gather(attn_in, "pair")
    projected = jnp.dot(block_in, w_qkv, preferred_element_type=jnp.float32).astype(jnp.bfloat16)
    head_count = projected.shape[1] // (2 * KEY_SIZE + VALUE_SIZE)
    grouped = projected.reshape(local_rows, head_count, 2 * KEY_SIZE + VALUE_SIZE).transpose(1, 0, 2)
    queries = grouped[:, :, :KEY_SIZE]
    kv = grouped[:, :, KEY_SIZE:]
    scale = 1.0 / math.sqrt(KEY_SIZE)

    def attend(state, kv_block):
        running_max, running_sum, weighted = state
        key_block = kv_block[:, :, :KEY_SIZE]
        value_block = kv_block[:, :, KEY_SIZE:]
        scores = (
            jnp.einsum("hqd,hkd->hqk", queries, key_block, preferred_element_type=jnp.float32)
            * scale
        )
        new_max = jnp.maximum(running_max, jnp.max(scores, axis=-1))
        shrink = jnp.exp(running_max - new_max)
        weights = jnp.exp(scores - new_max[:, :, None])
        running_sum = running_sum * shrink + jnp.sum(weights, axis=-1)
        update = jnp.einsum(
            "hqk,hkd->hqd",
            weights.astype(jnp.bfloat16),
            value_block,
            preferred_element_type=jnp.float32,
        )
        weighted = weighted * shrink[:, :, None] + update
        return (new_max, running_sum, weighted)

    state = (
        jnp.full((head_count, local_rows), -1e30, jnp.float32),
        jnp.zeros((head_count, local_rows), jnp.float32),
        jnp.zeros((head_count, local_rows, VALUE_SIZE), jnp.float32),
    )
    with jax.named_scope("kv_ring"):
        forward = [(i, (i + 1) % seq_count) for i in range(seq_count)]
        backward = [((i + 1) % seq_count, i) for i in range(seq_count)]
        half = local_rows // 2
        going = kv[:, :half]
        coming = kv[:, half:]
        for step in range(seq_count):
            if step + 1 < seq_count:
                next_going = lax.ppermute(going, "seq", forward)
                next_coming = lax.ppermute(coming, "seq", backward)
            state = attend(state, going)
            state = attend(state, coming)
            if step + 1 < seq_count:
                going, coming = next_going, next_coming
    running_max, running_sum, weighted = state
    attended = (weighted / running_sum[:, :, None]).astype(jnp.bfloat16)
    attended = attended.transpose(1, 0, 2).reshape(local_rows, head_count * VALUE_SIZE)
    with jax.named_scope("out_projection"):
        late_w_out, unused = lax.optimization_barrier((w_out, kv))
        full_w_out = gather_weight_rows(late_w_out, "pair", "seq")
        if rotated:
            me = lax.axis_index("pair")
            pieces = attended.reshape(pair_count, row_count, attended.shape[1])
            head_rows = attended.shape[1]
            mixed = jnp.dot(
                pieces[0],
                lax.dynamic_slice_in_dim(full_w_out, me * head_rows, head_rows, 0),
                preferred_element_type=jnp.float32,
            )
            for shift in range(1, pair_count):
                incoming = lax.ppermute(
                    pieces[pair_count - shift],
                    "pair",
                    [(i, (i + shift) % pair_count) for i in range(pair_count)],
                )
                source = (me + pair_count - shift) % pair_count
                mixed = mixed + jnp.dot(
                    incoming,
                    lax.dynamic_slice_in_dim(full_w_out, source * head_rows, head_rows, 0),
                    preferred_element_type=jnp.float32,
                )
        else:
            own_heads = rows_to_heads(attended, "pair")
            mixed = jnp.dot(own_heads, full_w_out, preferred_element_type=jnp.float32)
    seq_out = (first_out.astype(jnp.float32) + mixed).astype(jnp.bfloat16)
    bin_count = row_count // POOL
    pooled = jnp.mean(seq_out.astype(jnp.float32).reshape(bin_count, POOL, channels), axis=1)
    bin_norm = norm_rows(pooled, gain_pool).astype(jnp.bfloat16)
    sides = jnp.dot(bin_norm, w_pair, preferred_element_type=jnp.float32).astype(jnp.bfloat16)
    with jax.named_scope("sides_gather"):
        if seq_count > 4:
            all_sides = doubling_all_gather(doubling_all_gather(sides, "pair"), "seq")
        else:
            all_sides = direct_all_gather(direct_all_gather(sides, "pair"), "seq")
    tile_rows = bin_count * pair_count
    tile_cols = bin_count * seq_count
    row_side = lax.dynamic_slice_in_dim(
        all_sides, lax.axis_index("seq") * tile_rows, tile_rows, 0
    )[:, :PAIR_CH]
    column_side = lax.dynamic_slice_in_dim(
        all_sides, lax.axis_index("pair") * tile_cols, tile_cols, 0
    )[:, PAIR_CH:]
    pair_tile = (
        row_side.astype(jnp.float32)[:, None, :] * column_side.astype(jnp.float32)[None, :, :]
    ).astype(jnp.bfloat16)
    flat_rows = pair_tile.reshape(tile_rows * tile_cols, PAIR_CH)
    hidden = jax.nn.relu(jnp.dot(flat_rows, w_up, preferred_element_type=jnp.float32)).astype(
        jnp.bfloat16
    )
    pair_out = flat_rows.astype(jnp.float32) + jnp.dot(
        hidden, w_down, preferred_element_type=jnp.float32
    )
    pair_map = pair_out.astype(jnp.bfloat16).reshape(tile_rows, tile_cols, PAIR_CH)
    return (seq_out, pair_map)


def solution(mesh):
    return jax.shard_map(
        shards,
        mesh=mesh,
        in_specs=(
            P(("groups", "seq", "pair"), None),
            P(),
            P(None, "pair", None),
            P(),
            P(None, "pair"),
            P("pair", None),
            P(),
            P(),
            P(),
            P(),
        ),
        out_specs=(P(("groups", "seq", "pair"), None), P(("groups", "seq"), "pair", None)),
        check_vma=False,
    )
```

```python
import math

import jax
import jax.numpy as jnp
from jax import lax
from jax.sharding import PartitionSpec as P

KEY_SIZE = 128
VALUE_SIZE = 128
DILATION = 4
POOL = 16
PAIR_CH = 128


EPS = 1e-06


def padded_2(value, sides, width):
    for axis, dim in sides:
        peers, length = (lax.axis_size(axis), value.shape[dim])
        up = [(i, (i + 1) % peers) for i in range(peers - 1)]
        down = [(j, i) for i, j in up]
        last = lax.slice_in_dim(value, length - width, length, axis=dim)
        first = lax.slice_in_dim(value, 0, width, axis=dim)
        before = lax.ppermute(last, axis, up)
        after = lax.ppermute(first, axis, down)
        value = jnp.concatenate([before, value, after], axis=dim)
    return value


def norm_rows(values, gain):
    return values * lax.rsqrt(jnp.mean(values * values, axis=-1, keepdims=True) + EPS) * gain


def conv_rows(padded, conv_weight, row_total):
    summed = jnp.zeros((row_total, conv_weight.shape[2]), jnp.float32)
    for offset in range(conv_weight.shape[0]):
        shifted = lax.dynamic_slice_in_dim(padded, offset * DILATION, row_total, 0)
        summed = summed + jnp.dot(shifted, conv_weight[offset], preferred_element_type=jnp.float32)
    return summed


def direct_reduce_scatter(partial, axis):
    n = lax.axis_size(axis)
    me = lax.axis_index(axis)
    rows = partial.shape[0] // n
    blocks = partial.reshape(n, rows, partial.shape[1])
    total = blocks[me]
    for shift in range(1, n):
        outgoing = blocks[(me + shift) % n].astype(jnp.bfloat16)
        incoming = lax.ppermute(outgoing, axis, [(i, (i + shift) % n) for i in range(n)])
        total = total + incoming.astype(jnp.float32)
    return total


def permute_all_to_all(value, axis):
    n = lax.axis_size(axis)
    me = lax.axis_index(axis)
    width = value.shape[1] // n
    pieces = value.reshape(value.shape[0], n, width)
    slots = jnp.zeros((n, value.shape[0], width), value.dtype)
    slots = lax.dynamic_update_index_in_dim(slots, pieces[:, me], me, 0)
    for shift in range(1, n):
        outgoing = pieces[:, (me + shift) % n]
        incoming = lax.ppermute(outgoing, axis, [(i, (i + shift) % n) for i in range(n)])
        slots = lax.dynamic_update_index_in_dim(slots, incoming, (me + n - shift) % n, 0)
    return slots.reshape(n * value.shape[0], width)


def line_all_gather(value, axis):
    n = lax.axis_size(axis)
    me = lax.axis_index(axis)
    rows = value.shape[0]
    right = [(i, i + 1) for i in range(n - 1)]
    left = [(i + 1, i) for i in range(n - 1)]
    slots = jnp.zeros((n + 1, rows) + value.shape[1:], value.dtype)
    slots = lax.dynamic_update_index_in_dim(slots, value, me, 0)
    flow_r, flow_l = value, value
    for step in range(1, n):
        flow_r = lax.ppermute(flow_r, axis, right)
        flow_l = lax.ppermute(flow_l, axis, left)
        at_r = jnp.where(me - step >= 0, me - step, n)
        at_l = jnp.where(me + step < n, me + step, n)
        slots = lax.dynamic_update_index_in_dim(slots, flow_r, at_r, 0)
        slots = lax.dynamic_update_index_in_dim(slots, flow_l, at_l, 0)
    return slots[:n].reshape((n * rows,) + value.shape[1:])


def rows_to_heads(value, axis):
    n = lax.axis_size(axis)
    me = lax.axis_index(axis)
    rows = value.shape[0] // n
    pieces = value.reshape(n, rows, value.shape[1])
    slots = jnp.zeros((n, rows, value.shape[1]), value.dtype)
    slots = lax.dynamic_update_index_in_dim(slots, pieces[me], me, 0)
    for shift in range(1, n):
        outgoing = pieces[(me + shift) % n]
        incoming = lax.ppermute(outgoing, axis, [(i, (i + shift) % n) for i in range(n)])
        slots = lax.dynamic_update_index_in_dim(slots, incoming, (me + n - shift) % n, 0)
    return slots.transpose(1, 0, 2).reshape(rows, n * value.shape[1])


def gather_weight_rows(weight, axis, chip_axis):
    peers = lax.axis_size(chip_axis)
    if peers % 2:
        return line_all_gather(weight, axis)
    core = lax.axis_index(chip_axis) % 2
    half = weight.shape[1] // 2
    mine = lax.dynamic_slice_in_dim(weight, core * half, half, 1)
    gathered = line_all_gather(mine, axis)
    other = lax.ppermute(gathered, chip_axis, [(i, i ^ 1) for i in range(peers)])
    return jnp.where(
        core == 0,
        jnp.concatenate([gathered, other], 1),
        jnp.concatenate([other, gathered], 1),
    )


def rotated_all_gather(value, axis):
    n = lax.axis_size(axis)
    pieces = [value]
    for shift in range(1, n):
        pieces.append(lax.ppermute(value, axis, [(i, (i + shift) % n) for i in range(n)]))
    return jnp.concatenate(pieces, 0)


def direct_all_gather(value, axis):
    n = lax.axis_size(axis)
    if n > 4:
        return line_all_gather(value, axis)
    me = lax.axis_index(axis)
    slots = jnp.zeros((n,) + value.shape, value.dtype)
    slots = lax.dynamic_update_index_in_dim(slots, value, me, 0)
    for shift in range(1, n):
        incoming = lax.ppermute(value, axis, [(i, (i + shift) % n) for i in range(n)])
        slots = lax.dynamic_update_index_in_dim(slots, incoming, (me + n - shift) % n, 0)
    return slots.reshape((n * value.shape[0],) + value.shape[1:])


def doubling_all_gather(value, axis):
    n = lax.axis_size(axis)
    assert n & (n - 1) == 0
    me = lax.axis_index(axis)
    out = value
    k = 1
    while k < n:
        other = lax.ppermute(out, axis, [(i, i ^ k) for i in range(n)])
        low = (me & k) == 0
        out = jnp.where(low, jnp.concatenate([out, other], 0), jnp.concatenate([other, out], 0))
        k *= 2
    return out


def shards(
    sequence, gain_conv, conv_weight, gain_attn, w_qkv, w_out, gain_pool, w_pair, w_up, w_down
):
    pair_count = lax.axis_size("pair")
    seq_count = lax.axis_size("seq")
    row_count = sequence.shape[0]
    channels = sequence.shape[1]
    local_rows = row_count * pair_count
    inputs = sequence.astype(jnp.float32)
    normed = norm_rows(inputs, gain_conv).astype(jnp.bfloat16)
    swapped = permute_all_to_all(normed, "pair")
    padded = padded_2(swapped, (("seq", 0),), DILATION * (conv_weight.shape[0] - 1) // 2)
    with jax.named_scope("conv_reduce"):
        summed = direct_reduce_scatter(conv_rows(padded, conv_weight, local_rows), "pair")
    first_out = (inputs + summed).astype(jnp.bfloat16)
    attn_in = norm_rows(first_out.astype(jnp.float32), gain_attn).astype(jnp.bfloat16)
    with jax.named_scope("attn_in_gather"):
        rotated = pair_count <= 4
        if rotated:
            block_in = rotated_all_gather(attn_in, "pair")
        else:
            block_in = direct_all_gather(attn_in, "pair")
    projected = jnp.dot(block_in, w_qkv, preferred_element_type=jnp.float32).astype(jnp.bfloat16)
    head_count = projected.shape[1] // (2 * KEY_SIZE + VALUE_SIZE)
    grouped = projected.reshape(local_rows, head_count, 2 * KEY_SIZE + VALUE_SIZE).transpose(1, 0, 2)
    queries = grouped[:, :, :KEY_SIZE]
    kv = grouped[:, :, KEY_SIZE:]
    if rotated and seq_count % 2 == 0:
        late_w_out, kv = lax.optimization_barrier((w_out, kv))
    scale = 1.0 / math.sqrt(KEY_SIZE)

    def attend(state, kv_block):
        running_max, running_sum, weighted = state
        key_block = kv_block[:, :, :KEY_SIZE]
        value_block = kv_block[:, :, KEY_SIZE:]
        scores = (
            jnp.einsum("hqd,hkd->hqk", queries, key_block, preferred_element_type=jnp.float32)
            * scale
        )
        new_max = jnp.maximum(running_max, jnp.max(scores, axis=-1))
        shrink = jnp.exp(running_max - new_max)
        weights = jnp.exp(scores - new_max[:, :, None])
        running_sum = running_sum * shrink + jnp.sum(weights, axis=-1)
        update = jnp.einsum(
            "hqk,hkd->hqd",
            weights.astype(jnp.bfloat16),
            value_block,
            preferred_element_type=jnp.float32,
        )
        weighted = weighted * shrink[:, :, None] + update
        return (new_max, running_sum, weighted)

    state = (
        jnp.full((head_count, local_rows), -1e30, jnp.float32),
        jnp.zeros((head_count, local_rows), jnp.float32),
        jnp.zeros((head_count, local_rows, VALUE_SIZE), jnp.float32),
    )
    with jax.named_scope("kv_ring"):
        forward = [(i, (i + 1) % seq_count) for i in range(seq_count)]
        backward = [((i + 1) % seq_count, i) for i in range(seq_count)]
        half = local_rows // 2
        going = kv[:, :half]
        coming = kv[:, half:]
        for step in range(seq_count):
            if step + 1 < seq_count:
                next_going = lax.ppermute(going, "seq", forward)
                next_coming = lax.ppermute(coming, "seq", backward)
            state = attend(state, going)
            state = attend(state, coming)
            if step + 1 < seq_count:
                going, coming = next_going, next_coming
    running_max, running_sum, weighted = state
    attended = (weighted / running_sum[:, :, None]).astype(jnp.bfloat16)
    attended = attended.transpose(1, 0, 2).reshape(local_rows, head_count * VALUE_SIZE)
    with jax.named_scope("out_projection"):
        if rotated and seq_count % 2 == 0:
            me = lax.axis_index("pair")
            core = lax.axis_index("seq") % 2
            half = w_out.shape[1] // 2
            mine_w = lax.dynamic_slice_in_dim(late_w_out, core * half, half, 1)
            other_w = lax.dynamic_slice_in_dim(late_w_out, (1 - core) * half, half, 1)
            pieces = attended.reshape(pair_count, row_count, attended.shape[1])
            fetched = []
            for shift in range(1, pair_count):
                fetched.append(
                    lax.ppermute(
                        mine_w, "pair", [(i, (i + shift) % pair_count) for i in range(pair_count)]
                    )
                )
            swapped_w = lax.ppermute(
                jnp.stack(fetched), "seq", [(i, i ^ 1) for i in range(seq_count)]
            )
            mixed_mine = jnp.dot(pieces[0], mine_w, preferred_element_type=jnp.float32)
            mixed_other = jnp.dot(pieces[0], other_w, preferred_element_type=jnp.float32)
            for shift in range(1, pair_count):
                incoming = lax.ppermute(
                    pieces[pair_count - shift],
                    "pair",
                    [(i, (i + shift) % pair_count) for i in range(pair_count)],
                )
                mixed_mine = mixed_mine + jnp.dot(
                    incoming, fetched[shift - 1], preferred_element_type=jnp.float32
                )
                mixed_other = mixed_other + jnp.dot(
                    incoming, swapped_w[shift - 1], preferred_element_type=jnp.float32
                )
            mixed = jnp.where(
                core == 0,
                jnp.concatenate([mixed_mine, mixed_other], 1),
                jnp.concatenate([mixed_other, mixed_mine], 1),
            )
        else:
            late_w_out, unused = lax.optimization_barrier((w_out, kv))
            full_w_out = gather_weight_rows(late_w_out, "pair", "seq")
            own_heads = rows_to_heads(attended, "pair")
            mixed = jnp.dot(own_heads, full_w_out, preferred_element_type=jnp.float32)
    seq_out = (first_out.astype(jnp.float32) + mixed).astype(jnp.bfloat16)
    bin_count = row_count // POOL
    pooled = jnp.mean(seq_out.astype(jnp.float32).reshape(bin_count, POOL, channels), axis=1)
    bin_norm = norm_rows(pooled, gain_pool).astype(jnp.bfloat16)
    sides = jnp.dot(bin_norm, w_pair, preferred_element_type=jnp.float32).astype(jnp.bfloat16)
    with jax.named_scope("sides_gather"):
        if seq_count > 4:
            all_sides = doubling_all_gather(doubling_all_gather(sides, "pair"), "seq")
        else:
            all_sides = direct_all_gather(direct_all_gather(sides, "pair"), "seq")
    tile_rows = bin_count * pair_count
    tile_cols = bin_count * seq_count
    row_side = lax.dynamic_slice_in_dim(
        all_sides, lax.axis_index("seq") * tile_rows, tile_rows, 0
    )[:, :PAIR_CH]
    column_side = lax.dynamic_slice_in_dim(
        all_sides, lax.axis_index("pair") * tile_cols, tile_cols, 0
    )[:, PAIR_CH:]
    pair_tile = (
        row_side.astype(jnp.float32)[:, None, :] * column_side.astype(jnp.float32)[None, :, :]
    ).astype(jnp.bfloat16)
    flat_rows = pair_tile.reshape(tile_rows * tile_cols, PAIR_CH)
    hidden = jax.nn.relu(jnp.dot(flat_rows, w_up, preferred_element_type=jnp.float32)).astype(
        jnp.bfloat16
    )
    pair_out = flat_rows.astype(jnp.float32) + jnp.dot(
        hidden, w_down, preferred_element_type=jnp.float32
    )
    pair_map = pair_out.astype(jnp.bfloat16).reshape(tile_rows, tile_cols, PAIR_CH)
    return (seq_out, pair_map)


def solution(mesh):
    return jax.shard_map(
        shards,
        mesh=mesh,
        in_specs=(
            P(("groups", "seq", "pair"), None),
            P(),
            P(None, "pair", None),
            P(),
            P(None, "pair"),
            P("pair", None),
            P(),
            P(),
            P(),
            P(),
        ),
        out_specs=(P(("groups", "seq", "pair"), None), P(("groups", "seq"), "pair", None)),
        check_vma=False,
    )
```

```python
import math

import jax
import jax.numpy as jnp
from jax import lax
from jax.sharding import PartitionSpec as P

KEY_SIZE = 128
VALUE_SIZE = 128
DILATION = 4
POOL = 16
PAIR_CH = 128


EPS = 1e-06


def padded_2(value, sides, width):
    for axis, dim in sides:
        peers, length = (lax.axis_size(axis), value.shape[dim])
        up = [(i, (i + 1) % peers) for i in range(peers - 1)]
        down = [(j, i) for i, j in up]
        last = lax.slice_in_dim(value, length - width, length, axis=dim)
        first = lax.slice_in_dim(value, 0, width, axis=dim)
        before = lax.ppermute(last, axis, up)
        after = lax.ppermute(first, axis, down)
        value = jnp.concatenate([before, value, after], axis=dim)
    return value


def norm_rows(values, gain):
    return values * lax.rsqrt(jnp.mean(values * values, axis=-1, keepdims=True) + EPS) * gain


def conv_rows(padded, conv_weight, row_total):
    summed = jnp.zeros((row_total, conv_weight.shape[2]), jnp.float32)
    for offset in range(conv_weight.shape[0]):
        shifted = lax.dynamic_slice_in_dim(padded, offset * DILATION, row_total, 0)
        summed = summed + jnp.dot(shifted, conv_weight[offset], preferred_element_type=jnp.float32)
    return summed


def direct_reduce_scatter(partial, axis):
    n = lax.axis_size(axis)
    me = lax.axis_index(axis)
    rows = partial.shape[0] // n
    blocks = partial.reshape(n, rows, partial.shape[1])
    total = blocks[me]
    for shift in range(1, n):
        outgoing = blocks[(me + shift) % n].astype(jnp.bfloat16)
        incoming = lax.ppermute(outgoing, axis, [(i, (i + shift) % n) for i in range(n)])
        total = total + incoming.astype(jnp.float32)
    return total


def permute_all_to_all(value, axis):
    n = lax.axis_size(axis)
    me = lax.axis_index(axis)
    width = value.shape[1] // n
    pieces = value.reshape(value.shape[0], n, width)
    slots = jnp.zeros((n, value.shape[0], width), value.dtype)
    slots = lax.dynamic_update_index_in_dim(slots, pieces[:, me], me, 0)
    for shift in range(1, n):
        outgoing = pieces[:, (me + shift) % n]
        incoming = lax.ppermute(outgoing, axis, [(i, (i + shift) % n) for i in range(n)])
        slots = lax.dynamic_update_index_in_dim(slots, incoming, (me + n - shift) % n, 0)
    return slots.reshape(n * value.shape[0], width)


def line_all_gather(value, axis):
    n = lax.axis_size(axis)
    me = lax.axis_index(axis)
    rows = value.shape[0]
    right = [(i, i + 1) for i in range(n - 1)]
    left = [(i + 1, i) for i in range(n - 1)]
    slots = jnp.zeros((n + 1, rows) + value.shape[1:], value.dtype)
    slots = lax.dynamic_update_index_in_dim(slots, value, me, 0)
    flow_r, flow_l = value, value
    for step in range(1, n):
        flow_r = lax.ppermute(flow_r, axis, right)
        flow_l = lax.ppermute(flow_l, axis, left)
        at_r = jnp.where(me - step >= 0, me - step, n)
        at_l = jnp.where(me + step < n, me + step, n)
        slots = lax.dynamic_update_index_in_dim(slots, flow_r, at_r, 0)
        slots = lax.dynamic_update_index_in_dim(slots, flow_l, at_l, 0)
    return slots[:n].reshape((n * rows,) + value.shape[1:])


def rows_to_heads(value, axis):
    n = lax.axis_size(axis)
    me = lax.axis_index(axis)
    rows = value.shape[0] // n
    pieces = value.reshape(n, rows, value.shape[1])
    slots = jnp.zeros((n, rows, value.shape[1]), value.dtype)
    slots = lax.dynamic_update_index_in_dim(slots, pieces[me], me, 0)
    for shift in range(1, n):
        outgoing = pieces[(me + shift) % n]
        incoming = lax.ppermute(outgoing, axis, [(i, (i + shift) % n) for i in range(n)])
        slots = lax.dynamic_update_index_in_dim(slots, incoming, (me + n - shift) % n, 0)
    return slots.transpose(1, 0, 2).reshape(rows, n * value.shape[1])


def gather_weight_rows(weight, axis, chip_axis):
    peers = lax.axis_size(chip_axis)
    if peers % 2:
        return line_all_gather(weight, axis)
    core = lax.axis_index(chip_axis) % 2
    half = weight.shape[1] // 2
    mine = lax.dynamic_slice_in_dim(weight, core * half, half, 1)
    gathered = line_all_gather(mine, axis)
    other = lax.ppermute(gathered, chip_axis, [(i, i ^ 1) for i in range(peers)])
    return jnp.where(
        core == 0,
        jnp.concatenate([gathered, other], 1),
        jnp.concatenate([other, gathered], 1),
    )


def rotated_all_gather(value, axis):
    n = lax.axis_size(axis)
    pieces = [value]
    for shift in range(1, n):
        pieces.append(lax.ppermute(value, axis, [(i, (i + shift) % n) for i in range(n)]))
    return jnp.concatenate(pieces, 0)


def direct_all_gather(value, axis):
    n = lax.axis_size(axis)
    if n > 4:
        return line_all_gather(value, axis)
    me = lax.axis_index(axis)
    slots = jnp.zeros((n,) + value.shape, value.dtype)
    slots = lax.dynamic_update_index_in_dim(slots, value, me, 0)
    for shift in range(1, n):
        incoming = lax.ppermute(value, axis, [(i, (i + shift) % n) for i in range(n)])
        slots = lax.dynamic_update_index_in_dim(slots, incoming, (me + n - shift) % n, 0)
    return slots.reshape((n * value.shape[0],) + value.shape[1:])


def doubling_all_gather(value, axis):
    n = lax.axis_size(axis)
    assert n & (n - 1) == 0
    me = lax.axis_index(axis)
    out = value
    k = 1
    while k < n:
        other = lax.ppermute(out, axis, [(i, i ^ k) for i in range(n)])
        low = (me & k) == 0
        out = jnp.where(low, jnp.concatenate([out, other], 0), jnp.concatenate([other, out], 0))
        k *= 2
    return out


def shards(
    sequence, gain_conv, conv_weight, gain_attn, w_qkv, w_out, gain_pool, w_pair, w_up, w_down
):
    pair_count = lax.axis_size("pair")
    seq_count = lax.axis_size("seq")
    row_count = sequence.shape[0]
    channels = sequence.shape[1]
    local_rows = row_count * pair_count
    inputs = sequence.astype(jnp.float32)
    normed = norm_rows(inputs, gain_conv).astype(jnp.bfloat16)
    swapped = permute_all_to_all(normed, "pair")
    padded = padded_2(swapped, (("seq", 0),), DILATION * (conv_weight.shape[0] - 1) // 2)
    with jax.named_scope("conv_reduce"):
        summed = direct_reduce_scatter(conv_rows(padded, conv_weight, local_rows), "pair")
    first_out = (inputs + summed).astype(jnp.bfloat16)
    attn_in = norm_rows(first_out.astype(jnp.float32), gain_attn).astype(jnp.bfloat16)
    with jax.named_scope("attn_in_gather"):
        rotated = pair_count <= 4
        if rotated:
            block_in = rotated_all_gather(attn_in, "pair")
        else:
            block_in = direct_all_gather(attn_in, "pair")
    projected = jnp.dot(block_in, w_qkv, preferred_element_type=jnp.float32).astype(jnp.bfloat16)
    head_count = projected.shape[1] // (2 * KEY_SIZE + VALUE_SIZE)
    grouped = projected.reshape(local_rows, head_count, 2 * KEY_SIZE + VALUE_SIZE).transpose(1, 0, 2)
    queries = grouped[:, :, :KEY_SIZE]
    kv = grouped[:, :, KEY_SIZE:]
    if rotated and seq_count % 2 == 0:
        late_w_out = w_out
    scale = 1.0 / math.sqrt(KEY_SIZE)

    def attend(state, kv_block):
        running_max, running_sum, weighted = state
        key_block = kv_block[:, :, :KEY_SIZE]
        value_block = kv_block[:, :, KEY_SIZE:]
        scores = (
            jnp.einsum("hqd,hkd->hqk", queries, key_block, preferred_element_type=jnp.float32)
            * scale
        )
        new_max = jnp.maximum(running_max, jnp.max(scores, axis=-1))
        shrink = jnp.exp(running_max - new_max)
        weights = jnp.exp(scores - new_max[:, :, None])
        running_sum = running_sum * shrink + jnp.sum(weights, axis=-1)
        update = jnp.einsum(
            "hqk,hkd->hqd",
            weights.astype(jnp.bfloat16),
            value_block,
            preferred_element_type=jnp.float32,
        )
        weighted = weighted * shrink[:, :, None] + update
        return (new_max, running_sum, weighted)

    state = (
        jnp.full((head_count, local_rows), -1e30, jnp.float32),
        jnp.zeros((head_count, local_rows), jnp.float32),
        jnp.zeros((head_count, local_rows, VALUE_SIZE), jnp.float32),
    )
    with jax.named_scope("kv_ring"):
        forward = [(i, (i + 1) % seq_count) for i in range(seq_count)]
        backward = [((i + 1) % seq_count, i) for i in range(seq_count)]
        half = local_rows // 2
        going = kv[:, :half]
        coming = kv[:, half:]
        for step in range(seq_count):
            if step + 1 < seq_count:
                next_going = lax.ppermute(going, "seq", forward)
                next_coming = lax.ppermute(coming, "seq", backward)
            state = attend(state, going)
            state = attend(state, coming)
            if step + 1 < seq_count:
                going, coming = next_going, next_coming
    running_max, running_sum, weighted = state
    attended = (weighted / running_sum[:, :, None]).astype(jnp.bfloat16)
    attended = attended.transpose(1, 0, 2).reshape(local_rows, head_count * VALUE_SIZE)
    with jax.named_scope("out_projection"):
        if rotated and seq_count % 2 == 0:
            me = lax.axis_index("pair")
            core = lax.axis_index("seq") % 2
            half = w_out.shape[1] // 2
            mine_w = lax.dynamic_slice_in_dim(late_w_out, core * half, half, 1)
            other_w = lax.dynamic_slice_in_dim(late_w_out, (1 - core) * half, half, 1)
            pieces = attended.reshape(pair_count, row_count, attended.shape[1])
            fetched = []
            for shift in range(1, pair_count):
                fetched.append(
                    lax.ppermute(
                        mine_w, "pair", [(i, (i + shift) % pair_count) for i in range(pair_count)]
                    )
                )
            swapped_w = lax.ppermute(
                jnp.stack(fetched), "seq", [(i, i ^ 1) for i in range(seq_count)]
            )
            mixed_mine = jnp.dot(pieces[0], mine_w, preferred_element_type=jnp.float32)
            mixed_other = jnp.dot(pieces[0], other_w, preferred_element_type=jnp.float32)
            for shift in range(1, pair_count):
                incoming = lax.ppermute(
                    pieces[pair_count - shift],
                    "pair",
                    [(i, (i + shift) % pair_count) for i in range(pair_count)],
                )
                mixed_mine = mixed_mine + jnp.dot(
                    incoming, fetched[shift - 1], preferred_element_type=jnp.float32
                )
                mixed_other = mixed_other + jnp.dot(
                    incoming, swapped_w[shift - 1], preferred_element_type=jnp.float32
                )
            mixed = jnp.where(
                core == 0,
                jnp.concatenate([mixed_mine, mixed_other], 1),
                jnp.concatenate([mixed_other, mixed_mine], 1),
            )
        else:
            late_w_out, unused = lax.optimization_barrier((w_out, kv))
            full_w_out = gather_weight_rows(late_w_out, "pair", "seq")
            own_heads = rows_to_heads(attended, "pair")
            mixed = jnp.dot(own_heads, full_w_out, preferred_element_type=jnp.float32)
    seq_out = (first_out.astype(jnp.float32) + mixed).astype(jnp.bfloat16)
    bin_count = row_count // POOL
    pooled = jnp.mean(seq_out.astype(jnp.float32).reshape(bin_count, POOL, channels), axis=1)
    bin_norm = norm_rows(pooled, gain_pool).astype(jnp.bfloat16)
    sides = jnp.dot(bin_norm, w_pair, preferred_element_type=jnp.float32).astype(jnp.bfloat16)
    with jax.named_scope("sides_gather"):
        if seq_count > 4:
            all_sides = doubling_all_gather(doubling_all_gather(sides, "pair"), "seq")
        else:
            all_sides = direct_all_gather(direct_all_gather(sides, "pair"), "seq")
    tile_rows = bin_count * pair_count
    tile_cols = bin_count * seq_count
    row_side = lax.dynamic_slice_in_dim(
        all_sides, lax.axis_index("seq") * tile_rows, tile_rows, 0
    )[:, :PAIR_CH]
    column_side = lax.dynamic_slice_in_dim(
        all_sides, lax.axis_index("pair") * tile_cols, tile_cols, 0
    )[:, PAIR_CH:]
    pair_tile = (
        row_side.astype(jnp.float32)[:, None, :] * column_side.astype(jnp.float32)[None, :, :]
    ).astype(jnp.bfloat16)
    flat_rows = pair_tile.reshape(tile_rows * tile_cols, PAIR_CH)
    hidden = jax.nn.relu(jnp.dot(flat_rows, w_up, preferred_element_type=jnp.float32)).astype(
        jnp.bfloat16
    )
    pair_out = flat_rows.astype(jnp.float32) + jnp.dot(
        hidden, w_down, preferred_element_type=jnp.float32
    )
    pair_map = pair_out.astype(jnp.bfloat16).reshape(tile_rows, tile_cols, PAIR_CH)
    return (seq_out, pair_map)


def solution(mesh):
    return jax.shard_map(
        shards,
        mesh=mesh,
        in_specs=(
            P(("groups", "seq", "pair"), None),
            P(),
            P(None, "pair", None),
            P(),
            P(None, "pair"),
            P("pair", None),
            P(),
            P(),
            P(),
            P(),
        ),
        out_specs=(P(("groups", "seq", "pair"), None), P(("groups", "seq"), "pair", None)),
        check_vma=False,
    )
```

```python
import math

import jax
import jax.numpy as jnp
from jax import lax
from jax.sharding import PartitionSpec as P

KEY_SIZE = 128
VALUE_SIZE = 128
DILATION = 4
POOL = 16
PAIR_CH = 128


EPS = 1e-06


def padded_2(value, sides, width):
    for axis, dim in sides:
        peers, length = (lax.axis_size(axis), value.shape[dim])
        up = [(i, (i + 1) % peers) for i in range(peers - 1)]
        down = [(j, i) for i, j in up]
        last = lax.slice_in_dim(value, length - width, length, axis=dim)
        first = lax.slice_in_dim(value, 0, width, axis=dim)
        before = lax.ppermute(last, axis, up)
        after = lax.ppermute(first, axis, down)
        value = jnp.concatenate([before, value, after], axis=dim)
    return value


def norm_rows(values, gain):
    return values * lax.rsqrt(jnp.mean(values * values, axis=-1, keepdims=True) + EPS) * gain


def conv_rows(padded, conv_weight, row_total):
    summed = jnp.zeros((row_total, conv_weight.shape[2]), jnp.float32)
    for offset in range(conv_weight.shape[0]):
        shifted = lax.dynamic_slice_in_dim(padded, offset * DILATION, row_total, 0)
        summed = summed + jnp.dot(shifted, conv_weight[offset], preferred_element_type=jnp.float32)
    return summed


def direct_reduce_scatter(partial, axis):
    n = lax.axis_size(axis)
    me = lax.axis_index(axis)
    rows = partial.shape[0] // n
    blocks = partial.reshape(n, rows, partial.shape[1])
    total = blocks[me]
    for shift in range(1, n):
        outgoing = blocks[(me + shift) % n].astype(jnp.bfloat16)
        incoming = lax.ppermute(outgoing, axis, [(i, (i + shift) % n) for i in range(n)])
        total = total + incoming.astype(jnp.float32)
    return total


def permute_all_to_all(value, axis):
    n = lax.axis_size(axis)
    me = lax.axis_index(axis)
    width = value.shape[1] // n
    pieces = value.reshape(value.shape[0], n, width)
    slots = jnp.zeros((n, value.shape[0], width), value.dtype)
    slots = lax.dynamic_update_index_in_dim(slots, pieces[:, me], me, 0)
    for shift in range(1, n):
        outgoing = pieces[:, (me + shift) % n]
        incoming = lax.ppermute(outgoing, axis, [(i, (i + shift) % n) for i in range(n)])
        slots = lax.dynamic_update_index_in_dim(slots, incoming, (me + n - shift) % n, 0)
    return slots.reshape(n * value.shape[0], width)


def line_flows(value, axis):
    n = lax.axis_size(axis)
    me = lax.axis_index(axis)
    right = [(i, i + 1) for i in range(n - 1)]
    left = [(i + 1, i) for i in range(n - 1)]
    flow_r, flow_l = value, value
    from_left, from_right = [], []
    for step in range(1, n):
        flow_r = lax.ppermute(flow_r, axis, right)
        flow_l = lax.ppermute(flow_l, axis, left)
        from_left.append(flow_r)
        from_right.append(flow_l)
    return [
        jnp.where(me >= shift, from_left[shift - 1], from_right[n - shift - 1])
        for shift in range(1, n)
    ]


def line_all_gather(value, axis):
    n = lax.axis_size(axis)
    me = lax.axis_index(axis)
    rows = value.shape[0]
    right = [(i, i + 1) for i in range(n - 1)]
    left = [(i + 1, i) for i in range(n - 1)]
    slots = jnp.zeros((n + 1, rows) + value.shape[1:], value.dtype)
    slots = lax.dynamic_update_index_in_dim(slots, value, me, 0)
    flow_r, flow_l = value, value
    for step in range(1, n):
        flow_r = lax.ppermute(flow_r, axis, right)
        flow_l = lax.ppermute(flow_l, axis, left)
        at_r = jnp.where(me - step >= 0, me - step, n)
        at_l = jnp.where(me + step < n, me + step, n)
        slots = lax.dynamic_update_index_in_dim(slots, flow_r, at_r, 0)
        slots = lax.dynamic_update_index_in_dim(slots, flow_l, at_l, 0)
    return slots[:n].reshape((n * rows,) + value.shape[1:])


def rows_to_heads(value, axis):
    n = lax.axis_size(axis)
    me = lax.axis_index(axis)
    rows = value.shape[0] // n
    pieces = value.reshape(n, rows, value.shape[1])
    slots = jnp.zeros((n, rows, value.shape[1]), value.dtype)
    slots = lax.dynamic_update_index_in_dim(slots, pieces[me], me, 0)
    for shift in range(1, n):
        outgoing = pieces[(me + shift) % n]
        incoming = lax.ppermute(outgoing, axis, [(i, (i + shift) % n) for i in range(n)])
        slots = lax.dynamic_update_index_in_dim(slots, incoming, (me + n - shift) % n, 0)
    return slots.transpose(1, 0, 2).reshape(rows, n * value.shape[1])


def gather_weight_rows(weight, axis, chip_axis):
    peers = lax.axis_size(chip_axis)
    if peers % 2:
        return line_all_gather(weight, axis)
    core = lax.axis_index(chip_axis) % 2
    half = weight.shape[1] // 2
    mine = lax.dynamic_slice_in_dim(weight, core * half, half, 1)
    gathered = line_all_gather(mine, axis)
    other = lax.ppermute(gathered, chip_axis, [(i, i ^ 1) for i in range(peers)])
    return jnp.where(
        core == 0,
        jnp.concatenate([gathered, other], 1),
        jnp.concatenate([other, gathered], 1),
    )


def rotated_all_gather(value, axis):
    n = lax.axis_size(axis)
    pieces = [value]
    for shift in range(1, n):
        pieces.append(lax.ppermute(value, axis, [(i, (i + shift) % n) for i in range(n)]))
    return jnp.concatenate(pieces, 0)


def direct_all_gather(value, axis):
    n = lax.axis_size(axis)
    if n > 4:
        return line_all_gather(value, axis)
    me = lax.axis_index(axis)
    slots = jnp.zeros((n,) + value.shape, value.dtype)
    slots = lax.dynamic_update_index_in_dim(slots, value, me, 0)
    for shift in range(1, n):
        incoming = lax.ppermute(value, axis, [(i, (i + shift) % n) for i in range(n)])
        slots = lax.dynamic_update_index_in_dim(slots, incoming, (me + n - shift) % n, 0)
    return slots.reshape((n * value.shape[0],) + value.shape[1:])


def doubling_all_gather(value, axis):
    n = lax.axis_size(axis)
    assert n & (n - 1) == 0
    me = lax.axis_index(axis)
    out = value
    k = 1
    while k < n:
        other = lax.ppermute(out, axis, [(i, i ^ k) for i in range(n)])
        low = (me & k) == 0
        out = jnp.where(low, jnp.concatenate([out, other], 0), jnp.concatenate([other, out], 0))
        k *= 2
    return out


def shards(
    sequence, gain_conv, conv_weight, gain_attn, w_qkv, w_out, gain_pool, w_pair, w_up, w_down
):
    pair_count = lax.axis_size("pair")
    seq_count = lax.axis_size("seq")
    row_count = sequence.shape[0]
    channels = sequence.shape[1]
    local_rows = row_count * pair_count
    inputs = sequence.astype(jnp.float32)
    normed = norm_rows(inputs, gain_conv).astype(jnp.bfloat16)
    swapped = permute_all_to_all(normed, "pair")
    padded = padded_2(swapped, (("seq", 0),), DILATION * (conv_weight.shape[0] - 1) // 2)
    with jax.named_scope("conv_reduce"):
        summed = direct_reduce_scatter(conv_rows(padded, conv_weight, local_rows), "pair")
    first_out = (inputs + summed).astype(jnp.bfloat16)
    attn_in = norm_rows(first_out.astype(jnp.float32), gain_attn).astype(jnp.bfloat16)
    with jax.named_scope("attn_in_gather"):
        rotated = pair_count <= 4
        if rotated:
            block_in = rotated_all_gather(attn_in, "pair")
        else:
            block_in = direct_all_gather(attn_in, "pair")
    projected = jnp.dot(block_in, w_qkv, preferred_element_type=jnp.float32).astype(jnp.bfloat16)
    head_count = projected.shape[1] // (2 * KEY_SIZE + VALUE_SIZE)
    grouped = projected.reshape(local_rows, head_count, 2 * KEY_SIZE + VALUE_SIZE).transpose(1, 0, 2)
    queries = grouped[:, :, :KEY_SIZE]
    kv = grouped[:, :, KEY_SIZE:]
    scale = 1.0 / math.sqrt(KEY_SIZE)

    def attend(state, kv_block):
        running_max, running_sum, weighted = state
        key_block = kv_block[:, :, :KEY_SIZE]
        value_block = kv_block[:, :, KEY_SIZE:]
        scores = (
            jnp.einsum("hqd,hkd->hqk", queries, key_block, preferred_element_type=jnp.float32)
            * scale
        )
        new_max = jnp.maximum(running_max, jnp.max(scores, axis=-1))
        shrink = jnp.exp(running_max - new_max)
        weights = jnp.exp(scores - new_max[:, :, None])
        running_sum = running_sum * shrink + jnp.sum(weights, axis=-1)
        update = jnp.einsum(
            "hqk,hkd->hqd",
            weights.astype(jnp.bfloat16),
            value_block,
            preferred_element_type=jnp.float32,
        )
        weighted = weighted * shrink[:, :, None] + update
        return (new_max, running_sum, weighted)

    state = (
        jnp.full((head_count, local_rows), -1e30, jnp.float32),
        jnp.zeros((head_count, local_rows), jnp.float32),
        jnp.zeros((head_count, local_rows, VALUE_SIZE), jnp.float32),
    )
    with jax.named_scope("kv_ring"):
        forward = [(i, (i + 1) % seq_count) for i in range(seq_count)]
        backward = [((i + 1) % seq_count, i) for i in range(seq_count)]
        half = local_rows // 2
        going = kv[:, :half]
        coming = kv[:, half:]
        for step in range(seq_count):
            if step + 1 < seq_count:
                next_going = lax.ppermute(going, "seq", forward)
                next_coming = lax.ppermute(coming, "seq", backward)
            state = attend(state, going)
            state = attend(state, coming)
            if step + 1 < seq_count:
                going, coming = next_going, next_coming
    running_max, running_sum, weighted = state
    attended = (weighted / running_sum[:, :, None]).astype(jnp.bfloat16)
    attended = attended.transpose(1, 0, 2).reshape(local_rows, head_count * VALUE_SIZE)
    with jax.named_scope("out_projection"):
        late_w_out, unused = lax.optimization_barrier((w_out, kv))
        if rotated and seq_count % 2 == 0:
            me = lax.axis_index("pair")
            core = lax.axis_index("seq") % 2
            half = w_out.shape[1] // 2
            mine_w = lax.dynamic_slice_in_dim(late_w_out, core * half, half, 1)
            other_w = lax.dynamic_slice_in_dim(late_w_out, (1 - core) * half, half, 1)
            fetched = line_flows(mine_w, "pair")
            swapped_w = lax.ppermute(
                jnp.stack(fetched), "seq", [(i, i ^ 1) for i in range(seq_count)]
            )
            pieces = attended.reshape(pair_count, row_count, attended.shape[1])
            mixed_mine = jnp.dot(pieces[0], mine_w, preferred_element_type=jnp.float32)
            mixed_other = jnp.dot(pieces[0], other_w, preferred_element_type=jnp.float32)
            for shift in range(1, pair_count):
                incoming = lax.ppermute(
                    pieces[pair_count - shift],
                    "pair",
                    [(i, (i + shift) % pair_count) for i in range(pair_count)],
                )
                mixed_mine = mixed_mine + jnp.dot(
                    incoming, fetched[shift - 1], preferred_element_type=jnp.float32
                )
                mixed_other = mixed_other + jnp.dot(
                    incoming, swapped_w[shift - 1], preferred_element_type=jnp.float32
                )
            mixed = jnp.where(
                core == 0,
                jnp.concatenate([mixed_mine, mixed_other], 1),
                jnp.concatenate([mixed_other, mixed_mine], 1),
            )
        else:
            full_w_out = gather_weight_rows(late_w_out, "pair", "seq")
            own_heads = rows_to_heads(attended, "pair")
            mixed = jnp.dot(own_heads, full_w_out, preferred_element_type=jnp.float32)
    seq_out = (first_out.astype(jnp.float32) + mixed).astype(jnp.bfloat16)
    bin_count = row_count // POOL
    pooled = jnp.mean(seq_out.astype(jnp.float32).reshape(bin_count, POOL, channels), axis=1)
    bin_norm = norm_rows(pooled, gain_pool).astype(jnp.bfloat16)
    sides = jnp.dot(bin_norm, w_pair, preferred_element_type=jnp.float32).astype(jnp.bfloat16)
    with jax.named_scope("sides_gather"):
        if seq_count > 4:
            all_sides = doubling_all_gather(doubling_all_gather(sides, "pair"), "seq")
        else:
            all_sides = direct_all_gather(direct_all_gather(sides, "pair"), "seq")
    tile_rows = bin_count * pair_count
    tile_cols = bin_count * seq_count
    row_side = lax.dynamic_slice_in_dim(
        all_sides, lax.axis_index("seq") * tile_rows, tile_rows, 0
    )[:, :PAIR_CH]
    column_side = lax.dynamic_slice_in_dim(
        all_sides, lax.axis_index("pair") * tile_cols, tile_cols, 0
    )[:, PAIR_CH:]
    pair_tile = (
        row_side.astype(jnp.float32)[:, None, :] * column_side.astype(jnp.float32)[None, :, :]
    ).astype(jnp.bfloat16)
    flat_rows = pair_tile.reshape(tile_rows * tile_cols, PAIR_CH)
    hidden = jax.nn.relu(jnp.dot(flat_rows, w_up, preferred_element_type=jnp.float32)).astype(
        jnp.bfloat16
    )
    pair_out = flat_rows.astype(jnp.float32) + jnp.dot(
        hidden, w_down, preferred_element_type=jnp.float32
    )
    pair_map = pair_out.astype(jnp.bfloat16).reshape(tile_rows, tile_cols, PAIR_CH)
    return (seq_out, pair_map)


def solution(mesh):
    return jax.shard_map(
        shards,
        mesh=mesh,
        in_specs=(
            P(("groups", "seq", "pair"), None),
            P(),
            P(None, "pair", None),
            P(),
            P(None, "pair"),
            P("pair", None),
            P(),
            P(),
            P(),
            P(),
        ),
        out_specs=(P(("groups", "seq", "pair"), None), P(("groups", "seq"), "pair", None)),
        check_vma=False,
    )
```

```python
import math

import jax
import jax.numpy as jnp
from jax import lax
from jax.sharding import PartitionSpec as P

KEY_SIZE = 128
VALUE_SIZE = 128
DILATION = 4
POOL = 16
PAIR_CH = 128


EPS = 1e-06


def padded_2(value, sides, width):
    for axis, dim in sides:
        peers, length = (lax.axis_size(axis), value.shape[dim])
        up = [(i, (i + 1) % peers) for i in range(peers - 1)]
        down = [(j, i) for i, j in up]
        last = lax.slice_in_dim(value, length - width, length, axis=dim)
        first = lax.slice_in_dim(value, 0, width, axis=dim)
        before = lax.ppermute(last, axis, up)
        after = lax.ppermute(first, axis, down)
        value = jnp.concatenate([before, value, after], axis=dim)
    return value


def norm_rows(values, gain):
    return values * lax.rsqrt(jnp.mean(values * values, axis=-1, keepdims=True) + EPS) * gain


def conv_rows(padded, conv_weight, row_total):
    summed = jnp.zeros((row_total, conv_weight.shape[2]), jnp.float32)
    for offset in range(conv_weight.shape[0]):
        shifted = lax.dynamic_slice_in_dim(padded, offset * DILATION, row_total, 0)
        summed = summed + jnp.dot(shifted, conv_weight[offset], preferred_element_type=jnp.float32)
    return summed


def line4_reduce_scatter(partial, axis):
    me = lax.axis_index(axis)
    rows = partial.shape[0] // 4
    blocks = partial.reshape(4, rows, partial.shape[1])

    def send(index, pairs):
        return lax.ppermute(blocks[index].astype(jnp.bfloat16), axis, pairs)

    near_r = send(jnp.clip(me + 1, 0, 3), [(0, 1), (1, 2), (2, 3)])
    near_l = send(jnp.clip(me - 1, 0, 3), [(1, 0), (2, 1), (3, 2)])
    far_seed = send(jnp.where(me == 0, 3, 0), [(0, 1), (3, 2)])
    two_hop = send(jnp.where(me == 0, 2, 1), [(0, 2), (3, 1)])
    far_sum = (blocks[jnp.where(me == 1, 3, 0)] + far_seed.astype(jnp.float32)).astype(jnp.bfloat16)
    far = lax.ppermute(far_sum, axis, [(1, 3), (2, 0)])
    total = blocks[me]
    for piece in (near_r, near_l, two_hop, far):
        total = total + piece.astype(jnp.float32)
    return total


def direct_reduce_scatter(partial, axis):
    n = lax.axis_size(axis)
    me = lax.axis_index(axis)
    rows = partial.shape[0] // n
    blocks = partial.reshape(n, rows, partial.shape[1])
    total = blocks[me]
    for shift in range(1, n):
        outgoing = blocks[(me + shift) % n].astype(jnp.bfloat16)
        incoming = lax.ppermute(outgoing, axis, [(i, (i + shift) % n) for i in range(n)])
        total = total + incoming.astype(jnp.float32)
    return total


def permute_all_to_all(value, axis):
    n = lax.axis_size(axis)
    me = lax.axis_index(axis)
    width = value.shape[1] // n
    pieces = value.reshape(value.shape[0], n, width)
    slots = jnp.zeros((n, value.shape[0], width), value.dtype)
    slots = lax.dynamic_update_index_in_dim(slots, pieces[:, me], me, 0)
    for shift in range(1, n):
        outgoing = pieces[:, (me + shift) % n]
        incoming = lax.ppermute(outgoing, axis, [(i, (i + shift) % n) for i in range(n)])
        slots = lax.dynamic_update_index_in_dim(slots, incoming, (me + n - shift) % n, 0)
    return slots.reshape(n * value.shape[0], width)


def line_flows(value, axis):
    n = lax.axis_size(axis)
    me = lax.axis_index(axis)
    right = [(i, i + 1) for i in range(n - 1)]
    left = [(i + 1, i) for i in range(n - 1)]
    flow_r, flow_l = value, value
    from_left, from_right = [], []
    for step in range(1, n):
        flow_r = lax.ppermute(flow_r, axis, right)
        flow_l = lax.ppermute(flow_l, axis, left)
        from_left.append(flow_r)
        from_right.append(flow_l)
    return [
        jnp.where(me >= shift, from_left[shift - 1], from_right[n - shift - 1])
        for shift in range(1, n)
    ]


def line_all_gather(value, axis):
    n = lax.axis_size(axis)
    me = lax.axis_index(axis)
    rows = value.shape[0]
    right = [(i, i + 1) for i in range(n - 1)]
    left = [(i + 1, i) for i in range(n - 1)]
    slots = jnp.zeros((n + 1, rows) + value.shape[1:], value.dtype)
    slots = lax.dynamic_update_index_in_dim(slots, value, me, 0)
    flow_r, flow_l = value, value
    for step in range(1, n):
        flow_r = lax.ppermute(flow_r, axis, right)
        flow_l = lax.ppermute(flow_l, axis, left)
        at_r = jnp.where(me - step >= 0, me - step, n)
        at_l = jnp.where(me + step < n, me + step, n)
        slots = lax.dynamic_update_index_in_dim(slots, flow_r, at_r, 0)
        slots = lax.dynamic_update_index_in_dim(slots, flow_l, at_l, 0)
    return slots[:n].reshape((n * rows,) + value.shape[1:])


def rows_to_heads(value, axis):
    n = lax.axis_size(axis)
    me = lax.axis_index(axis)
    rows = value.shape[0] // n
    pieces = value.reshape(n, rows, value.shape[1])
    slots = jnp.zeros((n, rows, value.shape[1]), value.dtype)
    slots = lax.dynamic_update_index_in_dim(slots, pieces[me], me, 0)
    for shift in range(1, n):
        outgoing = pieces[(me + shift) % n]
        incoming = lax.ppermute(outgoing, axis, [(i, (i + shift) % n) for i in range(n)])
        slots = lax.dynamic_update_index_in_dim(slots, incoming, (me + n - shift) % n, 0)
    return slots.transpose(1, 0, 2).reshape(rows, n * value.shape[1])


def gather_weight_rows(weight, axis, chip_axis):
    peers = lax.axis_size(chip_axis)
    if peers % 2:
        return line_all_gather(weight, axis)
    core = lax.axis_index(chip_axis) % 2
    half = weight.shape[1] // 2
    mine = lax.dynamic_slice_in_dim(weight, core * half, half, 1)
    gathered = line_all_gather(mine, axis)
    other = lax.ppermute(gathered, chip_axis, [(i, i ^ 1) for i in range(peers)])
    return jnp.where(
        core == 0,
        jnp.concatenate([gathered, other], 1),
        jnp.concatenate([other, gathered], 1),
    )


def rotated_all_gather(value, axis):
    n = lax.axis_size(axis)
    pieces = [value]
    for shift in range(1, n):
        pieces.append(lax.ppermute(value, axis, [(i, (i + shift) % n) for i in range(n)]))
    return jnp.concatenate(pieces, 0)


def direct_all_gather(value, axis):
    n = lax.axis_size(axis)
    if n > 4:
        return line_all_gather(value, axis)
    me = lax.axis_index(axis)
    slots = jnp.zeros((n,) + value.shape, value.dtype)
    slots = lax.dynamic_update_index_in_dim(slots, value, me, 0)
    for shift in range(1, n):
        incoming = lax.ppermute(value, axis, [(i, (i + shift) % n) for i in range(n)])
        slots = lax.dynamic_update_index_in_dim(slots, incoming, (me + n - shift) % n, 0)
    return slots.reshape((n * value.shape[0],) + value.shape[1:])


def doubling_all_gather(value, axis):
    n = lax.axis_size(axis)
    assert n & (n - 1) == 0
    me = lax.axis_index(axis)
    out = value
    k = 1
    while k < n:
        other = lax.ppermute(out, axis, [(i, i ^ k) for i in range(n)])
        low = (me & k) == 0
        out = jnp.where(low, jnp.concatenate([out, other], 0), jnp.concatenate([other, out], 0))
        k *= 2
    return out


def shards(
    sequence, gain_conv, conv_weight, gain_attn, w_qkv, w_out, gain_pool, w_pair, w_up, w_down
):
    pair_count = lax.axis_size("pair")
    seq_count = lax.axis_size("seq")
    row_count = sequence.shape[0]
    channels = sequence.shape[1]
    local_rows = row_count * pair_count
    inputs = sequence.astype(jnp.float32)
    normed = norm_rows(inputs, gain_conv).astype(jnp.bfloat16)
    swapped = permute_all_to_all(normed, "pair")
    padded = padded_2(swapped, (("seq", 0),), DILATION * (conv_weight.shape[0] - 1) // 2)
    with jax.named_scope("conv_reduce"):
        conv_partial = conv_rows(padded, conv_weight, local_rows)
        if pair_count == 4:
            summed = line4_reduce_scatter(conv_partial, "pair")
        else:
            summed = direct_reduce_scatter(conv_partial, "pair")
    first_out = (inputs + summed).astype(jnp.bfloat16)
    attn_in = norm_rows(first_out.astype(jnp.float32), gain_attn).astype(jnp.bfloat16)
    with jax.named_scope("attn_in_gather"):
        rotated = pair_count <= 4
        if rotated:
            block_in = rotated_all_gather(attn_in, "pair")
        else:
            block_in = direct_all_gather(attn_in, "pair")
    projected = jnp.dot(block_in, w_qkv, preferred_element_type=jnp.float32).astype(jnp.bfloat16)
    head_count = projected.shape[1] // (2 * KEY_SIZE + VALUE_SIZE)
    grouped = projected.reshape(local_rows, head_count, 2 * KEY_SIZE + VALUE_SIZE).transpose(1, 0, 2)
    queries = grouped[:, :, :KEY_SIZE]
    kv = grouped[:, :, KEY_SIZE:]
    scale = 1.0 / math.sqrt(KEY_SIZE)

    def attend(state, kv_block):
        running_max, running_sum, weighted = state
        key_block = kv_block[:, :, :KEY_SIZE]
        value_block = kv_block[:, :, KEY_SIZE:]
        scores = (
            jnp.einsum("hqd,hkd->hqk", queries, key_block, preferred_element_type=jnp.float32)
            * scale
        )
        new_max = jnp.maximum(running_max, jnp.max(scores, axis=-1))
        shrink = jnp.exp(running_max - new_max)
        weights = jnp.exp(scores - new_max[:, :, None])
        running_sum = running_sum * shrink + jnp.sum(weights, axis=-1)
        update = jnp.einsum(
            "hqk,hkd->hqd",
            weights.astype(jnp.bfloat16),
            value_block,
            preferred_element_type=jnp.float32,
        )
        weighted = weighted * shrink[:, :, None] + update
        return (new_max, running_sum, weighted)

    state = (
        jnp.full((head_count, local_rows), -1e30, jnp.float32),
        jnp.zeros((head_count, local_rows), jnp.float32),
        jnp.zeros((head_count, local_rows, VALUE_SIZE), jnp.float32),
    )
    with jax.named_scope("kv_ring"):
        forward = [(i, (i + 1) % seq_count) for i in range(seq_count)]
        backward = [((i + 1) % seq_count, i) for i in range(seq_count)]
        half = local_rows // 2
        going = kv[:, :half]
        coming = kv[:, half:]
        for step in range(seq_count):
            if step + 1 < seq_count:
                next_going = lax.ppermute(going, "seq", forward)
                next_coming = lax.ppermute(coming, "seq", backward)
            state = attend(state, going)
            state = attend(state, coming)
            if step + 1 < seq_count:
                going, coming = next_going, next_coming
    running_max, running_sum, weighted = state
    attended = (weighted / running_sum[:, :, None]).astype(jnp.bfloat16)
    attended = attended.transpose(1, 0, 2).reshape(local_rows, head_count * VALUE_SIZE)
    with jax.named_scope("out_projection"):
        late_w_out, unused = lax.optimization_barrier((w_out, kv))
        if rotated and seq_count % 2 == 0:
            me = lax.axis_index("pair")
            core = lax.axis_index("seq") % 2
            half = w_out.shape[1] // 2
            mine_w = lax.dynamic_slice_in_dim(late_w_out, core * half, half, 1)
            other_w = lax.dynamic_slice_in_dim(late_w_out, (1 - core) * half, half, 1)
            fetched = line_flows(mine_w, "pair")
            swapped_w = lax.ppermute(
                jnp.stack(fetched), "seq", [(i, i ^ 1) for i in range(seq_count)]
            )
            pieces = attended.reshape(pair_count, row_count, attended.shape[1])
            mixed_mine = jnp.dot(pieces[0], mine_w, preferred_element_type=jnp.float32)
            mixed_other = jnp.dot(pieces[0], other_w, preferred_element_type=jnp.float32)
            for shift in range(1, pair_count):
                incoming = lax.ppermute(
                    pieces[pair_count - shift],
                    "pair",
                    [(i, (i + shift) % pair_count) for i in range(pair_count)],
                )
                mixed_mine = mixed_mine + jnp.dot(
                    incoming, fetched[shift - 1], preferred_element_type=jnp.float32
                )
                mixed_other = mixed_other + jnp.dot(
                    incoming, swapped_w[shift - 1], preferred_element_type=jnp.float32
                )
            mixed = jnp.where(
                core == 0,
                jnp.concatenate([mixed_mine, mixed_other], 1),
                jnp.concatenate([mixed_other, mixed_mine], 1),
            )
        else:
            full_w_out = gather_weight_rows(late_w_out, "pair", "seq")
            own_heads = rows_to_heads(attended, "pair")
            mixed = jnp.dot(own_heads, full_w_out, preferred_element_type=jnp.float32)
    seq_out = (first_out.astype(jnp.float32) + mixed).astype(jnp.bfloat16)
    bin_count = row_count // POOL
    pooled = jnp.mean(seq_out.astype(jnp.float32).reshape(bin_count, POOL, channels), axis=1)
    bin_norm = norm_rows(pooled, gain_pool).astype(jnp.bfloat16)
    sides = jnp.dot(bin_norm, w_pair, preferred_element_type=jnp.float32).astype(jnp.bfloat16)
    with jax.named_scope("sides_gather"):
        if seq_count > 4:
            all_sides = doubling_all_gather(doubling_all_gather(sides, "pair"), "seq")
        else:
            all_sides = direct_all_gather(direct_all_gather(sides, "pair"), "seq")
    tile_rows = bin_count * pair_count
    tile_cols = bin_count * seq_count
    row_side = lax.dynamic_slice_in_dim(
        all_sides, lax.axis_index("seq") * tile_rows, tile_rows, 0
    )[:, :PAIR_CH]
    column_side = lax.dynamic_slice_in_dim(
        all_sides, lax.axis_index("pair") * tile_cols, tile_cols, 0
    )[:, PAIR_CH:]
    pair_tile = (
        row_side.astype(jnp.float32)[:, None, :] * column_side.astype(jnp.float32)[None, :, :]
    ).astype(jnp.bfloat16)
    flat_rows = pair_tile.reshape(tile_rows * tile_cols, PAIR_CH)
    hidden = jax.nn.relu(jnp.dot(flat_rows, w_up, preferred_element_type=jnp.float32)).astype(
        jnp.bfloat16
    )
    pair_out = flat_rows.astype(jnp.float32) + jnp.dot(
        hidden, w_down, preferred_element_type=jnp.float32
    )
    pair_map = pair_out.astype(jnp.bfloat16).reshape(tile_rows, tile_cols, PAIR_CH)
    return (seq_out, pair_map)


def solution(mesh):
    return jax.shard_map(
        shards,
        mesh=mesh,
        in_specs=(
            P(("groups", "seq", "pair"), None),
            P(),
            P(None, "pair", None),
            P(),
            P(None, "pair"),
            P("pair", None),
            P(),
            P(),
            P(),
            P(),
        ),
        out_specs=(P(("groups", "seq", "pair"), None), P(("groups", "seq"), "pair", None)),
        check_vma=False,
    )
```

```python
import math

import jax
import jax.numpy as jnp
from jax import lax
from jax.sharding import PartitionSpec as P

KEY_SIZE = 128
VALUE_SIZE = 128
DILATION = 4
POOL = 16
PAIR_CH = 128


EPS = 1e-06


def padded_2(value, sides, width):
    for axis, dim in sides:
        peers, length = (lax.axis_size(axis), value.shape[dim])
        up = [(i, (i + 1) % peers) for i in range(peers - 1)]
        down = [(j, i) for i, j in up]
        last = lax.slice_in_dim(value, length - width, length, axis=dim)
        first = lax.slice_in_dim(value, 0, width, axis=dim)
        before = lax.ppermute(last, axis, up)
        after = lax.ppermute(first, axis, down)
        value = jnp.concatenate([before, value, after], axis=dim)
    return value


def norm_rows(values, gain):
    return values * lax.rsqrt(jnp.mean(values * values, axis=-1, keepdims=True) + EPS) * gain


def conv_rows(padded, conv_weight, row_total):
    summed = jnp.zeros((row_total, conv_weight.shape[2]), jnp.float32)
    for offset in range(conv_weight.shape[0]):
        shifted = lax.dynamic_slice_in_dim(padded, offset * DILATION, row_total, 0)
        summed = summed + jnp.dot(shifted, conv_weight[offset], preferred_element_type=jnp.float32)
    return summed


def direct_reduce_scatter(partial, axis):
    n = lax.axis_size(axis)
    me = lax.axis_index(axis)
    rows = partial.shape[0] // n
    blocks = partial.reshape(n, rows, partial.shape[1])
    total = blocks[me]
    for shift in range(1, n):
        outgoing = blocks[(me + shift) % n].astype(jnp.bfloat16)
        incoming = lax.ppermute(outgoing, axis, [(i, (i + shift) % n) for i in range(n)])
        total = total + incoming.astype(jnp.float32)
    return total


def permute_all_to_all(value, axis):
    n = lax.axis_size(axis)
    me = lax.axis_index(axis)
    width = value.shape[1] // n
    pieces = value.reshape(value.shape[0], n, width)
    slots = jnp.zeros((n, value.shape[0], width), value.dtype)
    slots = lax.dynamic_update_index_in_dim(slots, pieces[:, me], me, 0)
    for shift in range(1, n):
        outgoing = pieces[:, (me + shift) % n]
        incoming = lax.ppermute(outgoing, axis, [(i, (i + shift) % n) for i in range(n)])
        slots = lax.dynamic_update_index_in_dim(slots, incoming, (me + n - shift) % n, 0)
    return slots.reshape(n * value.shape[0], width)


def line_flows(value, axis):
    n = lax.axis_size(axis)
    me = lax.axis_index(axis)
    right = [(i, i + 1) for i in range(n - 1)]
    left = [(i + 1, i) for i in range(n - 1)]
    flow_r, flow_l = value, value
    from_left, from_right = [], []
    for step in range(1, n):
        flow_r = lax.ppermute(flow_r, axis, right)
        flow_l = lax.ppermute(flow_l, axis, left)
        from_left.append(flow_r)
        from_right.append(flow_l)
    return [
        jnp.where(me >= shift, from_left[shift - 1], from_right[n - shift - 1])
        for shift in range(1, n)
    ]


def line_all_gather(value, axis):
    n = lax.axis_size(axis)
    me = lax.axis_index(axis)
    rows = value.shape[0]
    right = [(i, i + 1) for i in range(n - 1)]
    left = [(i + 1, i) for i in range(n - 1)]
    slots = jnp.zeros((n + 1, rows) + value.shape[1:], value.dtype)
    slots = lax.dynamic_update_index_in_dim(slots, value, me, 0)
    flow_r, flow_l = value, value
    for step in range(1, n):
        flow_r = lax.ppermute(flow_r, axis, right)
        flow_l = lax.ppermute(flow_l, axis, left)
        at_r = jnp.where(me - step >= 0, me - step, n)
        at_l = jnp.where(me + step < n, me + step, n)
        slots = lax.dynamic_update_index_in_dim(slots, flow_r, at_r, 0)
        slots = lax.dynamic_update_index_in_dim(slots, flow_l, at_l, 0)
    return slots[:n].reshape((n * rows,) + value.shape[1:])


def rows_to_heads(value, axis):
    n = lax.axis_size(axis)
    me = lax.axis_index(axis)
    rows = value.shape[0] // n
    pieces = value.reshape(n, rows, value.shape[1])
    slots = jnp.zeros((n, rows, value.shape[1]), value.dtype)
    slots = lax.dynamic_update_index_in_dim(slots, pieces[me], me, 0)
    for shift in range(1, n):
        outgoing = pieces[(me + shift) % n]
        incoming = lax.ppermute(outgoing, axis, [(i, (i + shift) % n) for i in range(n)])
        slots = lax.dynamic_update_index_in_dim(slots, incoming, (me + n - shift) % n, 0)
    return slots.transpose(1, 0, 2).reshape(rows, n * value.shape[1])


def gather_weight_rows(weight, axis, chip_axis):
    peers = lax.axis_size(chip_axis)
    if peers % 2:
        return line_all_gather(weight, axis)
    core = lax.axis_index(chip_axis) % 2
    half = weight.shape[1] // 2
    mine = lax.dynamic_slice_in_dim(weight, core * half, half, 1)
    gathered = line_all_gather(mine, axis)
    other = lax.ppermute(gathered, chip_axis, [(i, i ^ 1) for i in range(peers)])
    return jnp.where(
        core == 0,
        jnp.concatenate([gathered, other], 1),
        jnp.concatenate([other, gathered], 1),
    )


def rotated_all_gather(value, axis):
    n = lax.axis_size(axis)
    pieces = [value]
    for shift in range(1, n):
        pieces.append(lax.ppermute(value, axis, [(i, (i + shift) % n) for i in range(n)]))
    return jnp.concatenate(pieces, 0)


def direct_all_gather(value, axis):
    n = lax.axis_size(axis)
    if n > 4:
        return line_all_gather(value, axis)
    me = lax.axis_index(axis)
    slots = jnp.zeros((n,) + value.shape, value.dtype)
    slots = lax.dynamic_update_index_in_dim(slots, value, me, 0)
    for shift in range(1, n):
        incoming = lax.ppermute(value, axis, [(i, (i + shift) % n) for i in range(n)])
        slots = lax.dynamic_update_index_in_dim(slots, incoming, (me + n - shift) % n, 0)
    return slots.reshape((n * value.shape[0],) + value.shape[1:])


def doubling_all_gather(value, axis):
    n = lax.axis_size(axis)
    assert n & (n - 1) == 0
    me = lax.axis_index(axis)
    out = value
    k = 1
    while k < n:
        other = lax.ppermute(out, axis, [(i, i ^ k) for i in range(n)])
        low = (me & k) == 0
        out = jnp.where(low, jnp.concatenate([out, other], 0), jnp.concatenate([other, out], 0))
        k *= 2
    return out


def shards(
    sequence, gain_conv, conv_weight, gain_attn, w_qkv, w_out, gain_pool, w_pair, w_up, w_down
):
    pair_count = lax.axis_size("pair")
    seq_count = lax.axis_size("seq")
    row_count = sequence.shape[0]
    channels = sequence.shape[1]
    local_rows = row_count * pair_count
    inputs = sequence.astype(jnp.float32)
    normed = norm_rows(inputs, gain_conv).astype(jnp.bfloat16)
    swapped = permute_all_to_all(normed, "pair")
    padded = padded_2(swapped, (("seq", 0),), DILATION * (conv_weight.shape[0] - 1) // 2)
    with jax.named_scope("conv_reduce"):
        summed = direct_reduce_scatter(conv_rows(padded, conv_weight, local_rows), "pair")
    first_out = (inputs + summed).astype(jnp.bfloat16)
    attn_in = norm_rows(first_out.astype(jnp.float32), gain_attn).astype(jnp.bfloat16)
    with jax.named_scope("attn_in_gather"):
        rotated = pair_count <= 4
        if rotated:
            pieces_in = [attn_in] + [
                lax.ppermute(attn_in, "pair", [(i, (i + k) % pair_count) for i in range(pair_count)])
                for k in range(1, pair_count)
            ]
            projected = jnp.concatenate(
                [
                    jnp.dot(piece, w_qkv, preferred_element_type=jnp.float32).astype(jnp.bfloat16)
                    for piece in pieces_in
                ],
                0,
            )
        else:
            block_in = direct_all_gather(attn_in, "pair")
            projected = jnp.dot(
                block_in, w_qkv, preferred_element_type=jnp.float32
            ).astype(jnp.bfloat16)
    head_count = projected.shape[1] // (2 * KEY_SIZE + VALUE_SIZE)
    grouped = projected.reshape(local_rows, head_count, 2 * KEY_SIZE + VALUE_SIZE).transpose(1, 0, 2)
    queries = grouped[:, :, :KEY_SIZE]
    kv = grouped[:, :, KEY_SIZE:]
    scale = 1.0 / math.sqrt(KEY_SIZE)

    def attend(state, kv_block):
        running_max, running_sum, weighted = state
        key_block = kv_block[:, :, :KEY_SIZE]
        value_block = kv_block[:, :, KEY_SIZE:]
        scores = (
            jnp.einsum("hqd,hkd->hqk", queries, key_block, preferred_element_type=jnp.float32)
            * scale
        )
        new_max = jnp.maximum(running_max, jnp.max(scores, axis=-1))
        shrink = jnp.exp(running_max - new_max)
        weights = jnp.exp(scores - new_max[:, :, None])
        running_sum = running_sum * shrink + jnp.sum(weights, axis=-1)
        update = jnp.einsum(
            "hqk,hkd->hqd",
            weights.astype(jnp.bfloat16),
            value_block,
            preferred_element_type=jnp.float32,
        )
        weighted = weighted * shrink[:, :, None] + update
        return (new_max, running_sum, weighted)

    state = (
        jnp.full((head_count, local_rows), -1e30, jnp.float32),
        jnp.zeros((head_count, local_rows), jnp.float32),
        jnp.zeros((head_count, local_rows, VALUE_SIZE), jnp.float32),
    )
    with jax.named_scope("kv_ring"):
        forward = [(i, (i + 1) % seq_count) for i in range(seq_count)]
        backward = [((i + 1) % seq_count, i) for i in range(seq_count)]
        half = local_rows // 2
        going = kv[:, :half]
        coming = kv[:, half:]
        for step in range(seq_count):
            if step + 1 < seq_count:
                next_going = lax.ppermute(going, "seq", forward)
                next_coming = lax.ppermute(coming, "seq", backward)
            state = attend(state, going)
            state = attend(state, coming)
            if step + 1 < seq_count:
                going, coming = next_going, next_coming
    running_max, running_sum, weighted = state
    attended = (weighted / running_sum[:, :, None]).astype(jnp.bfloat16)
    attended = attended.transpose(1, 0, 2).reshape(local_rows, head_count * VALUE_SIZE)
    with jax.named_scope("out_projection"):
        late_w_out, unused = lax.optimization_barrier((w_out, kv))
        if rotated and seq_count % 2 == 0:
            me = lax.axis_index("pair")
            core = lax.axis_index("seq") % 2
            half = w_out.shape[1] // 2
            mine_w = lax.dynamic_slice_in_dim(late_w_out, core * half, half, 1)
            other_w = lax.dynamic_slice_in_dim(late_w_out, (1 - core) * half, half, 1)
            fetched = line_flows(mine_w, "pair")
            swapped_w = lax.ppermute(
                jnp.stack(fetched), "seq", [(i, i ^ 1) for i in range(seq_count)]
            )
            pieces = attended.reshape(pair_count, row_count, attended.shape[1])
            mixed_mine = jnp.dot(pieces[0], mine_w, preferred_element_type=jnp.float32)
            mixed_other = jnp.dot(pieces[0], other_w, preferred_element_type=jnp.float32)
            for shift in range(1, pair_count):
                incoming = lax.ppermute(
                    pieces[pair_count - shift],
                    "pair",
                    [(i, (i + shift) % pair_count) for i in range(pair_count)],
                )
                mixed_mine = mixed_mine + jnp.dot(
                    incoming, fetched[shift - 1], preferred_element_type=jnp.float32
                )
                mixed_other = mixed_other + jnp.dot(
                    incoming, swapped_w[shift - 1], preferred_element_type=jnp.float32
                )
            mixed = jnp.where(
                core == 0,
                jnp.concatenate([mixed_mine, mixed_other], 1),
                jnp.concatenate([mixed_other, mixed_mine], 1),
            )
        else:
            full_w_out = gather_weight_rows(late_w_out, "pair", "seq")
            own_heads = rows_to_heads(attended, "pair")
            mixed = jnp.dot(own_heads, full_w_out, preferred_element_type=jnp.float32)
    seq_out = (first_out.astype(jnp.float32) + mixed).astype(jnp.bfloat16)
    bin_count = row_count // POOL
    pooled = jnp.mean(seq_out.astype(jnp.float32).reshape(bin_count, POOL, channels), axis=1)
    bin_norm = norm_rows(pooled, gain_pool).astype(jnp.bfloat16)
    sides = jnp.dot(bin_norm, w_pair, preferred_element_type=jnp.float32).astype(jnp.bfloat16)
    with jax.named_scope("sides_gather"):
        if seq_count > 4:
            all_sides = doubling_all_gather(doubling_all_gather(sides, "pair"), "seq")
        else:
            all_sides = direct_all_gather(direct_all_gather(sides, "pair"), "seq")
    tile_rows = bin_count * pair_count
    tile_cols = bin_count * seq_count
    row_side = lax.dynamic_slice_in_dim(
        all_sides, lax.axis_index("seq") * tile_rows, tile_rows, 0
    )[:, :PAIR_CH]
    column_side = lax.dynamic_slice_in_dim(
        all_sides, lax.axis_index("pair") * tile_cols, tile_cols, 0
    )[:, PAIR_CH:]
    pair_tile = (
        row_side.astype(jnp.float32)[:, None, :] * column_side.astype(jnp.float32)[None, :, :]
    ).astype(jnp.bfloat16)
    flat_rows = pair_tile.reshape(tile_rows * tile_cols, PAIR_CH)
    hidden = jax.nn.relu(jnp.dot(flat_rows, w_up, preferred_element_type=jnp.float32)).astype(
        jnp.bfloat16
    )
    pair_out = flat_rows.astype(jnp.float32) + jnp.dot(
        hidden, w_down, preferred_element_type=jnp.float32
    )
    pair_map = pair_out.astype(jnp.bfloat16).reshape(tile_rows, tile_cols, PAIR_CH)
    return (seq_out, pair_map)


def solution(mesh):
    return jax.shard_map(
        shards,
        mesh=mesh,
        in_specs=(
            P(("groups", "seq", "pair"), None),
            P(),
            P(None, "pair", None),
            P(),
            P(None, "pair"),
            P("pair", None),
            P(),
            P(),
            P(),
            P(),
        ),
        out_specs=(P(("groups", "seq", "pair"), None), P(("groups", "seq"), "pair", None)),
        check_vma=False,
    )
```

```python
import math

import jax
import jax.numpy as jnp
from jax import lax
from jax.sharding import PartitionSpec as P

KEY_SIZE = 128
VALUE_SIZE = 128
DILATION = 4
POOL = 16
PAIR_CH = 128


EPS = 1e-06


def padded_2(value, sides, width):
    for axis, dim in sides:
        peers, length = (lax.axis_size(axis), value.shape[dim])
        up = [(i, (i + 1) % peers) for i in range(peers - 1)]
        down = [(j, i) for i, j in up]
        last = lax.slice_in_dim(value, length - width, length, axis=dim)
        first = lax.slice_in_dim(value, 0, width, axis=dim)
        before = lax.ppermute(last, axis, up)
        after = lax.ppermute(first, axis, down)
        value = jnp.concatenate([before, value, after], axis=dim)
    return value


def norm_rows(values, gain):
    return values * lax.rsqrt(jnp.mean(values * values, axis=-1, keepdims=True) + EPS) * gain


def conv_rows(padded, conv_weight, row_total):
    summed = jnp.zeros((row_total, conv_weight.shape[2]), jnp.float32)
    for offset in range(conv_weight.shape[0]):
        shifted = lax.dynamic_slice_in_dim(padded, offset * DILATION, row_total, 0)
        summed = summed + jnp.dot(shifted, conv_weight[offset], preferred_element_type=jnp.float32)
    return summed


def direct_reduce_scatter(partial, axis):
    n = lax.axis_size(axis)
    me = lax.axis_index(axis)
    rows = partial.shape[0] // n
    blocks = partial.reshape(n, rows, partial.shape[1])
    total = blocks[me]
    for shift in range(1, n):
        outgoing = blocks[(me + shift) % n].astype(jnp.bfloat16)
        incoming = lax.ppermute(outgoing, axis, [(i, (i + shift) % n) for i in range(n)])
        total = total + incoming.astype(jnp.float32)
    return total


def permute_all_to_all(value, axis):
    n = lax.axis_size(axis)
    me = lax.axis_index(axis)
    width = value.shape[1] // n
    pieces = value.reshape(value.shape[0], n, width)
    slots = jnp.zeros((n, value.shape[0], width), value.dtype)
    slots = lax.dynamic_update_index_in_dim(slots, pieces[:, me], me, 0)
    for shift in range(1, n):
        outgoing = pieces[:, (me + shift) % n]
        incoming = lax.ppermute(outgoing, axis, [(i, (i + shift) % n) for i in range(n)])
        slots = lax.dynamic_update_index_in_dim(slots, incoming, (me + n - shift) % n, 0)
    return slots.reshape(n * value.shape[0], width)


def line_flows(value, axis):
    n = lax.axis_size(axis)
    me = lax.axis_index(axis)
    right = [(i, i + 1) for i in range(n - 1)]
    left = [(i + 1, i) for i in range(n - 1)]
    flow_r, flow_l = value, value
    from_left, from_right = [], []
    for step in range(1, n):
        flow_r = lax.ppermute(flow_r, axis, right)
        flow_l = lax.ppermute(flow_l, axis, left)
        from_left.append(flow_r)
        from_right.append(flow_l)
    return [
        jnp.where(me >= shift, from_left[shift - 1], from_right[n - shift - 1])
        for shift in range(1, n)
    ]


def line_all_gather(value, axis):
    n = lax.axis_size(axis)
    me = lax.axis_index(axis)
    rows = value.shape[0]
    right = [(i, i + 1) for i in range(n - 1)]
    left = [(i + 1, i) for i in range(n - 1)]
    slots = jnp.zeros((n + 1, rows) + value.shape[1:], value.dtype)
    slots = lax.dynamic_update_index_in_dim(slots, value, me, 0)
    flow_r, flow_l = value, value
    for step in range(1, n):
        flow_r = lax.ppermute(flow_r, axis, right)
        flow_l = lax.ppermute(flow_l, axis, left)
        at_r = jnp.where(me - step >= 0, me - step, n)
        at_l = jnp.where(me + step < n, me + step, n)
        slots = lax.dynamic_update_index_in_dim(slots, flow_r, at_r, 0)
        slots = lax.dynamic_update_index_in_dim(slots, flow_l, at_l, 0)
    return slots[:n].reshape((n * rows,) + value.shape[1:])


def rows_to_heads(value, axis):
    n = lax.axis_size(axis)
    me = lax.axis_index(axis)
    rows = value.shape[0] // n
    pieces = value.reshape(n, rows, value.shape[1])
    slots = jnp.zeros((n, rows, value.shape[1]), value.dtype)
    slots = lax.dynamic_update_index_in_dim(slots, pieces[me], me, 0)
    for shift in range(1, n):
        outgoing = pieces[(me + shift) % n]
        incoming = lax.ppermute(outgoing, axis, [(i, (i + shift) % n) for i in range(n)])
        slots = lax.dynamic_update_index_in_dim(slots, incoming, (me + n - shift) % n, 0)
    return slots.transpose(1, 0, 2).reshape(rows, n * value.shape[1])


def gather_weight_rows(weight, axis, chip_axis):
    peers = lax.axis_size(chip_axis)
    if peers % 2:
        return line_all_gather(weight, axis)
    core = lax.axis_index(chip_axis) % 2
    half = weight.shape[1] // 2
    mine = lax.dynamic_slice_in_dim(weight, core * half, half, 1)
    gathered = line_all_gather(mine, axis)
    other = lax.ppermute(gathered, chip_axis, [(i, i ^ 1) for i in range(peers)])
    return jnp.where(
        core == 0,
        jnp.concatenate([gathered, other], 1),
        jnp.concatenate([other, gathered], 1),
    )


def rotated_all_gather(value, axis):
    n = lax.axis_size(axis)
    pieces = [value]
    for shift in range(1, n):
        pieces.append(lax.ppermute(value, axis, [(i, (i + shift) % n) for i in range(n)]))
    return jnp.concatenate(pieces, 0)


def direct_all_gather(value, axis):
    n = lax.axis_size(axis)
    if n > 4:
        return line_all_gather(value, axis)
    me = lax.axis_index(axis)
    slots = jnp.zeros((n,) + value.shape, value.dtype)
    slots = lax.dynamic_update_index_in_dim(slots, value, me, 0)
    for shift in range(1, n):
        incoming = lax.ppermute(value, axis, [(i, (i + shift) % n) for i in range(n)])
        slots = lax.dynamic_update_index_in_dim(slots, incoming, (me + n - shift) % n, 0)
    return slots.reshape((n * value.shape[0],) + value.shape[1:])


def doubling_all_gather(value, axis):
    n = lax.axis_size(axis)
    assert n & (n - 1) == 0
    me = lax.axis_index(axis)
    out = value
    k = 1
    while k < n:
        other = lax.ppermute(out, axis, [(i, i ^ k) for i in range(n)])
        low = (me & k) == 0
        out = jnp.where(low, jnp.concatenate([out, other], 0), jnp.concatenate([other, out], 0))
        k *= 2
    return out


def shards(
    sequence, gain_conv, conv_weight, gain_attn, w_qkv, w_out, gain_pool, w_pair, w_up, w_down
):
    pair_count = lax.axis_size("pair")
    seq_count = lax.axis_size("seq")
    row_count = sequence.shape[0]
    channels = sequence.shape[1]
    local_rows = row_count * pair_count
    inputs = sequence.astype(jnp.float32)
    normed = norm_rows(inputs, gain_conv).astype(jnp.bfloat16)
    swapped = permute_all_to_all(normed, "pair")
    padded = padded_2(swapped, (("seq", 0),), DILATION * (conv_weight.shape[0] - 1) // 2)
    with jax.named_scope("conv_reduce"):
        summed = direct_reduce_scatter(conv_rows(padded, conv_weight, local_rows), "pair")
    first_out = (inputs + summed).astype(jnp.bfloat16)
    attn_in = norm_rows(first_out.astype(jnp.float32), gain_attn).astype(jnp.bfloat16)
    with jax.named_scope("attn_in_gather"):
        rotated = pair_count <= 4
        if rotated:
            block_in = rotated_all_gather(attn_in, "pair")
        else:
            block_in = direct_all_gather(attn_in, "pair")
    projected = jnp.dot(block_in, w_qkv, preferred_element_type=jnp.float32).astype(jnp.bfloat16)
    head_count = projected.shape[1] // (2 * KEY_SIZE + VALUE_SIZE)
    grouped = projected.reshape(local_rows, head_count, 2 * KEY_SIZE + VALUE_SIZE).transpose(1, 0, 2)
    queries = grouped[:, :, :KEY_SIZE]
    kv = grouped[:, :, KEY_SIZE:]
    scale = 1.0 / math.sqrt(KEY_SIZE)

    def attend(state, kv_block):
        running_max, running_sum, weighted = state
        key_block = kv_block[:, :, :KEY_SIZE]
        value_block = kv_block[:, :, KEY_SIZE:]
        scores = (
            jnp.einsum("hqd,hkd->hqk", queries, key_block, preferred_element_type=jnp.float32)
            * scale
        )
        new_max = jnp.maximum(running_max, jnp.max(scores, axis=-1))
        shrink = jnp.exp(running_max - new_max)
        weights = jnp.exp(scores - new_max[:, :, None])
        running_sum = running_sum * shrink + jnp.sum(weights, axis=-1)
        update = jnp.einsum(
            "hqk,hkd->hqd",
            weights.astype(jnp.bfloat16),
            value_block,
            preferred_element_type=jnp.float32,
        )
        weighted = weighted * shrink[:, :, None] + update
        return (new_max, running_sum, weighted)

    state = (
        jnp.full((head_count, local_rows), -1e30, jnp.float32),
        jnp.zeros((head_count, local_rows), jnp.float32),
        jnp.zeros((head_count, local_rows, VALUE_SIZE), jnp.float32),
    )
    with jax.named_scope("kv_ring"):
        forward = [(i, (i + 1) % seq_count) for i in range(seq_count)]
        backward = [((i + 1) % seq_count, i) for i in range(seq_count)]
        half = local_rows // 2
        going = kv[:, :half]
        coming = kv[:, half:]
        for step in range(seq_count):
            if step + 1 < seq_count:
                next_going = lax.ppermute(going, "seq", forward)
                next_coming = lax.ppermute(coming, "seq", backward)
            state = attend(state, going)
            state = attend(state, coming)
            if step + 1 < seq_count:
                going, coming = next_going, next_coming
    running_max, running_sum, weighted = state
    attended = (weighted / running_sum[:, :, None]).astype(jnp.bfloat16)
    attended = attended.transpose(1, 0, 2).reshape(local_rows, head_count * VALUE_SIZE)
    with jax.named_scope("out_projection"):
        late_w_out, unused = lax.optimization_barrier((w_out, kv))
        if rotated and seq_count % 2 == 0:
            me = lax.axis_index("pair")
            core = lax.axis_index("seq") % 2
            ways = []
            for s_i in range(seq_count):
                for p_i in range(pair_count):
                    src = s_i * pair_count + p_i
                    if s_i % 2 == 0 and p_i + 1 < pair_count:
                        ways.append((src, src + 1))
                    if s_i % 2 == 1 and p_i > 0:
                        ways.append((src, src - 1))
            flow = late_w_out
            received = []
            for step in range(1, pair_count):
                flow = lax.ppermute(flow, ("seq", "pair"), ways)
                received.append(flow)
            received = jnp.stack(received)
            swapped_w = lax.ppermute(received, "seq", [(i, i ^ 1) for i in range(seq_count)])
            from_left = jnp.where(core == 0, received, swapped_w)
            from_right = jnp.where(core == 0, swapped_w, received)
            pieces = attended.reshape(pair_count, row_count, attended.shape[1])
            mixed = jnp.dot(pieces[0], late_w_out, preferred_element_type=jnp.float32)
            for shift in range(1, pair_count):
                incoming = lax.ppermute(
                    pieces[pair_count - shift],
                    "pair",
                    [(i, (i + shift) % pair_count) for i in range(pair_count)],
                )
                block = jnp.where(
                    me >= shift, from_left[shift - 1], from_right[pair_count - shift - 1]
                )
                mixed = mixed + jnp.dot(incoming, block, preferred_element_type=jnp.float32)
        else:
            full_w_out = gather_weight_rows(late_w_out, "pair", "seq")
            own_heads = rows_to_heads(attended, "pair")
            mixed = jnp.dot(own_heads, full_w_out, preferred_element_type=jnp.float32)
    seq_out = (first_out.astype(jnp.float32) + mixed).astype(jnp.bfloat16)
    bin_count = row_count // POOL
    pooled = jnp.mean(seq_out.astype(jnp.float32).reshape(bin_count, POOL, channels), axis=1)
    bin_norm = norm_rows(pooled, gain_pool).astype(jnp.bfloat16)
    sides = jnp.dot(bin_norm, w_pair, preferred_element_type=jnp.float32).astype(jnp.bfloat16)
    with jax.named_scope("sides_gather"):
        if seq_count > 4:
            all_sides = doubling_all_gather(doubling_all_gather(sides, "pair"), "seq")
        else:
            all_sides = direct_all_gather(direct_all_gather(sides, "pair"), "seq")
    tile_rows = bin_count * pair_count
    tile_cols = bin_count * seq_count
    row_side = lax.dynamic_slice_in_dim(
        all_sides, lax.axis_index("seq") * tile_rows, tile_rows, 0
    )[:, :PAIR_CH]
    column_side = lax.dynamic_slice_in_dim(
        all_sides, lax.axis_index("pair") * tile_cols, tile_cols, 0
    )[:, PAIR_CH:]
    pair_tile = (
        row_side.astype(jnp.float32)[:, None, :] * column_side.astype(jnp.float32)[None, :, :]
    ).astype(jnp.bfloat16)
    flat_rows = pair_tile.reshape(tile_rows * tile_cols, PAIR_CH)
    hidden = jax.nn.relu(jnp.dot(flat_rows, w_up, preferred_element_type=jnp.float32)).astype(
        jnp.bfloat16
    )
    pair_out = flat_rows.astype(jnp.float32) + jnp.dot(
        hidden, w_down, preferred_element_type=jnp.float32
    )
    pair_map = pair_out.astype(jnp.bfloat16).reshape(tile_rows, tile_cols, PAIR_CH)
    return (seq_out, pair_map)


def solution(mesh):
    return jax.shard_map(
        shards,
        mesh=mesh,
        in_specs=(
            P(("groups", "seq", "pair"), None),
            P(),
            P(None, "pair", None),
            P(),
            P(None, "pair"),
            P("pair", None),
            P(),
            P(),
            P(),
            P(),
        ),
        out_specs=(P(("groups", "seq", "pair"), None), P(("groups", "seq"), "pair", None)),
        check_vma=False,
    )
```

```python
import math

import jax
import jax.numpy as jnp
from jax import lax
from jax.sharding import PartitionSpec as P

KEY_SIZE = 128
VALUE_SIZE = 128
DILATION = 4
POOL = 16
PAIR_CH = 128


EPS = 1e-06


def padded_2(value, sides, width):
    for axis, dim in sides:
        peers, length = (lax.axis_size(axis), value.shape[dim])
        up = [(i, (i + 1) % peers) for i in range(peers - 1)]
        down = [(j, i) for i, j in up]
        last = lax.slice_in_dim(value, length - width, length, axis=dim)
        first = lax.slice_in_dim(value, 0, width, axis=dim)
        before = lax.ppermute(last, axis, up)
        after = lax.ppermute(first, axis, down)
        value = jnp.concatenate([before, value, after], axis=dim)
    return value


def norm_rows(values, gain):
    return values * lax.rsqrt(jnp.mean(values * values, axis=-1, keepdims=True) + EPS) * gain


def conv_rows(padded, conv_weight, row_total):
    summed = jnp.zeros((row_total, conv_weight.shape[2]), jnp.float32)
    for offset in range(conv_weight.shape[0]):
        shifted = lax.dynamic_slice_in_dim(padded, offset * DILATION, row_total, 0)
        summed = summed + jnp.dot(shifted, conv_weight[offset], preferred_element_type=jnp.float32)
    return summed


def direct_reduce_scatter(partial, axis):
    n = lax.axis_size(axis)
    me = lax.axis_index(axis)
    rows = partial.shape[0] // n
    blocks = partial.reshape(n, rows, partial.shape[1])
    total = blocks[me]
    for shift in range(1, n):
        outgoing = blocks[(me + shift) % n].astype(jnp.bfloat16)
        incoming = lax.ppermute(outgoing, axis, [(i, (i + shift) % n) for i in range(n)])
        total = total + incoming.astype(jnp.float32)
    return total


def permute_all_to_all(value, axis):
    n = lax.axis_size(axis)
    me = lax.axis_index(axis)
    width = value.shape[1] // n
    pieces = value.reshape(value.shape[0], n, width)
    slots = jnp.zeros((n, value.shape[0], width), value.dtype)
    slots = lax.dynamic_update_index_in_dim(slots, pieces[:, me], me, 0)
    for shift in range(1, n):
        outgoing = pieces[:, (me + shift) % n]
        incoming = lax.ppermute(outgoing, axis, [(i, (i + shift) % n) for i in range(n)])
        slots = lax.dynamic_update_index_in_dim(slots, incoming, (me + n - shift) % n, 0)
    return slots.reshape(n * value.shape[0], width)


def line_flows(value, axis):
    n = lax.axis_size(axis)
    me = lax.axis_index(axis)
    right = [(i, i + 1) for i in range(n - 1)]
    left = [(i + 1, i) for i in range(n - 1)]
    flow_r, flow_l = value, value
    from_left, from_right = [], []
    for step in range(1, n):
        flow_r = lax.ppermute(flow_r, axis, right)
        flow_l = lax.ppermute(flow_l, axis, left)
        from_left.append(flow_r)
        from_right.append(flow_l)
    return [
        jnp.where(me >= shift, from_left[shift - 1], from_right[n - shift - 1])
        for shift in range(1, n)
    ]


def line_all_gather(value, axis):
    n = lax.axis_size(axis)
    me = lax.axis_index(axis)
    rows = value.shape[0]
    right = [(i, i + 1) for i in range(n - 1)]
    left = [(i + 1, i) for i in range(n - 1)]
    slots = jnp.zeros((n + 1, rows) + value.shape[1:], value.dtype)
    slots = lax.dynamic_update_index_in_dim(slots, value, me, 0)
    flow_r, flow_l = value, value
    for step in range(1, n):
        flow_r = lax.ppermute(flow_r, axis, right)
        flow_l = lax.ppermute(flow_l, axis, left)
        at_r = jnp.where(me - step >= 0, me - step, n)
        at_l = jnp.where(me + step < n, me + step, n)
        slots = lax.dynamic_update_index_in_dim(slots, flow_r, at_r, 0)
        slots = lax.dynamic_update_index_in_dim(slots, flow_l, at_l, 0)
    return slots[:n].reshape((n * rows,) + value.shape[1:])


def rows_to_heads(value, axis):
    n = lax.axis_size(axis)
    me = lax.axis_index(axis)
    rows = value.shape[0] // n
    pieces = value.reshape(n, rows, value.shape[1])
    slots = jnp.zeros((n, rows, value.shape[1]), value.dtype)
    slots = lax.dynamic_update_index_in_dim(slots, pieces[me], me, 0)
    for shift in range(1, n):
        outgoing = pieces[(me + shift) % n]
        incoming = lax.ppermute(outgoing, axis, [(i, (i + shift) % n) for i in range(n)])
        slots = lax.dynamic_update_index_in_dim(slots, incoming, (me + n - shift) % n, 0)
    return slots.transpose(1, 0, 2).reshape(rows, n * value.shape[1])


def gather_weight_rows(weight, axis, chip_axis):
    peers = lax.axis_size(chip_axis)
    if peers % 2:
        return line_all_gather(weight, axis)
    core = lax.axis_index(chip_axis) % 2
    half = weight.shape[1] // 2
    mine = lax.dynamic_slice_in_dim(weight, core * half, half, 1)
    gathered = line_all_gather(mine, axis)
    other = lax.ppermute(gathered, chip_axis, [(i, i ^ 1) for i in range(peers)])
    return jnp.where(
        core == 0,
        jnp.concatenate([gathered, other], 1),
        jnp.concatenate([other, gathered], 1),
    )


def rotated_all_gather(value, axis):
    n = lax.axis_size(axis)
    pieces = [value]
    for shift in range(1, n):
        pieces.append(lax.ppermute(value, axis, [(i, (i + shift) % n) for i in range(n)]))
    return jnp.concatenate(pieces, 0)


def direct_all_gather(value, axis):
    n = lax.axis_size(axis)
    if n > 4:
        return line_all_gather(value, axis)
    me = lax.axis_index(axis)
    slots = jnp.zeros((n,) + value.shape, value.dtype)
    slots = lax.dynamic_update_index_in_dim(slots, value, me, 0)
    for shift in range(1, n):
        incoming = lax.ppermute(value, axis, [(i, (i + shift) % n) for i in range(n)])
        slots = lax.dynamic_update_index_in_dim(slots, incoming, (me + n - shift) % n, 0)
    return slots.reshape((n * value.shape[0],) + value.shape[1:])


def doubling_all_gather(value, axis):
    n = lax.axis_size(axis)
    assert n & (n - 1) == 0
    me = lax.axis_index(axis)
    out = value
    k = 1
    while k < n:
        other = lax.ppermute(out, axis, [(i, i ^ k) for i in range(n)])
        low = (me & k) == 0
        out = jnp.where(low, jnp.concatenate([out, other], 0), jnp.concatenate([other, out], 0))
        k *= 2
    return out


def shards(
    sequence, gain_conv, conv_weight, gain_attn, w_qkv, w_out, gain_pool, w_pair, w_up, w_down
):
    pair_count = lax.axis_size("pair")
    seq_count = lax.axis_size("seq")
    row_count = sequence.shape[0]
    channels = sequence.shape[1]
    local_rows = row_count * pair_count
    inputs = sequence.astype(jnp.float32)
    normed = norm_rows(inputs, gain_conv).astype(jnp.bfloat16)
    swapped = permute_all_to_all(normed, "pair")
    padded = padded_2(swapped, (("seq", 0),), DILATION * (conv_weight.shape[0] - 1) // 2)
    with jax.named_scope("conv_reduce"):
        summed = direct_reduce_scatter(conv_rows(padded, conv_weight, local_rows), "pair")
    first_out = (inputs + summed).astype(jnp.bfloat16)
    attn_in = norm_rows(first_out.astype(jnp.float32), gain_attn).astype(jnp.bfloat16)
    with jax.named_scope("attn_in_gather"):
        rotated = pair_count <= 4
        if rotated:
            block_in = rotated_all_gather(attn_in, "pair")
        else:
            block_in = direct_all_gather(attn_in, "pair")
    projected = jnp.dot(block_in, w_qkv, preferred_element_type=jnp.float32).astype(jnp.bfloat16)
    head_count = projected.shape[1] // (2 * KEY_SIZE + VALUE_SIZE)
    grouped = projected.reshape(local_rows, head_count, 2 * KEY_SIZE + VALUE_SIZE).transpose(1, 0, 2)
    queries = grouped[:, :, :KEY_SIZE]
    kv = grouped[:, :, KEY_SIZE:]
    scale = 1.0 / math.sqrt(KEY_SIZE)

    def attend(state, kv_block):
        running_max, running_sum, weighted = state
        key_block = kv_block[:, :, :KEY_SIZE]
        value_block = kv_block[:, :, KEY_SIZE:]
        scores = (
            jnp.einsum("hqd,hkd->hqk", queries, key_block, preferred_element_type=jnp.float32)
            * scale
        )
        new_max = jnp.maximum(running_max, jnp.max(scores, axis=-1))
        shrink = jnp.exp(running_max - new_max)
        weights = jnp.exp(scores - new_max[:, :, None])
        running_sum = running_sum * shrink + jnp.sum(weights, axis=-1)
        update = jnp.einsum(
            "hqk,hkd->hqd",
            weights.astype(jnp.bfloat16),
            value_block,
            preferred_element_type=jnp.float32,
        )
        weighted = weighted * shrink[:, :, None] + update
        return (new_max, running_sum, weighted)

    state = (
        jnp.full((head_count, local_rows), -1e30, jnp.float32),
        jnp.zeros((head_count, local_rows), jnp.float32),
        jnp.zeros((head_count, local_rows, VALUE_SIZE), jnp.float32),
    )
    with jax.named_scope("kv_ring"):
        forward = [(i, (i + 1) % seq_count) for i in range(seq_count)]
        backward = [((i + 1) % seq_count, i) for i in range(seq_count)]
        forward_steps = seq_count // 2
        backward_steps = seq_count - 1 - forward_steps
        if seq_count <= 4:
            going = kv
            coming = kv
            state = attend(state, kv)
            for step in range(forward_steps):
                going = lax.ppermute(going, "seq", forward)
                if step < backward_steps:
                    coming = lax.ppermute(coming, "seq", backward)
                state = attend(state, going)
                if step < backward_steps:
                    state = attend(state, coming)
        else:
            half = local_rows // 2
            going = kv[:, :half]
            coming = kv[:, half:]
            for step in range(seq_count):
                if step + 1 < seq_count:
                    next_going = lax.ppermute(going, "seq", forward)
                    next_coming = lax.ppermute(coming, "seq", backward)
                state = attend(state, going)
                state = attend(state, coming)
                if step + 1 < seq_count:
                    going, coming = next_going, next_coming
    running_max, running_sum, weighted = state
    attended = (weighted / running_sum[:, :, None]).astype(jnp.bfloat16)
    attended = attended.transpose(1, 0, 2).reshape(local_rows, head_count * VALUE_SIZE)
    with jax.named_scope("out_projection"):
        late_w_out, unused = lax.optimization_barrier((w_out, kv))
        if rotated and seq_count % 2 == 0:
            me = lax.axis_index("pair")
            core = lax.axis_index("seq") % 2
            ways = []
            for s_i in range(seq_count):
                for p_i in range(pair_count):
                    src = s_i * pair_count + p_i
                    if s_i % 2 == 0 and p_i + 1 < pair_count:
                        ways.append((src, src + 1))
                    if s_i % 2 == 1 and p_i > 0:
                        ways.append((src, src - 1))
            flow = late_w_out
            received = []
            for step in range(1, pair_count):
                flow = lax.ppermute(flow, ("seq", "pair"), ways)
                received.append(flow)
            received = jnp.stack(received)
            swapped_w = lax.ppermute(received, "seq", [(i, i ^ 1) for i in range(seq_count)])
            from_left = jnp.where(core == 0, received, swapped_w)
            from_right = jnp.where(core == 0, swapped_w, received)
            pieces = attended.reshape(pair_count, row_count, attended.shape[1])
            mixed = jnp.dot(pieces[0], late_w_out, preferred_element_type=jnp.float32)
            for shift in range(1, pair_count):
                incoming = lax.ppermute(
                    pieces[pair_count - shift],
                    "pair",
                    [(i, (i + shift) % pair_count) for i in range(pair_count)],
                )
                block = jnp.where(
                    me >= shift, from_left[shift - 1], from_right[pair_count - shift - 1]
                )
                mixed = mixed + jnp.dot(incoming, block, preferred_element_type=jnp.float32)
        else:
            full_w_out = gather_weight_rows(late_w_out, "pair", "seq")
            own_heads = rows_to_heads(attended, "pair")
            mixed = jnp.dot(own_heads, full_w_out, preferred_element_type=jnp.float32)
    seq_out = (first_out.astype(jnp.float32) + mixed).astype(jnp.bfloat16)
    bin_count = row_count // POOL
    pooled = jnp.mean(seq_out.astype(jnp.float32).reshape(bin_count, POOL, channels), axis=1)
    bin_norm = norm_rows(pooled, gain_pool).astype(jnp.bfloat16)
    sides = jnp.dot(bin_norm, w_pair, preferred_element_type=jnp.float32).astype(jnp.bfloat16)
    with jax.named_scope("sides_gather"):
        if seq_count > 4:
            all_sides = doubling_all_gather(doubling_all_gather(sides, "pair"), "seq")
        else:
            all_sides = direct_all_gather(direct_all_gather(sides, "pair"), "seq")
    tile_rows = bin_count * pair_count
    tile_cols = bin_count * seq_count
    row_side = lax.dynamic_slice_in_dim(
        all_sides, lax.axis_index("seq") * tile_rows, tile_rows, 0
    )[:, :PAIR_CH]
    column_side = lax.dynamic_slice_in_dim(
        all_sides, lax.axis_index("pair") * tile_cols, tile_cols, 0
    )[:, PAIR_CH:]
    pair_tile = (
        row_side.astype(jnp.float32)[:, None, :] * column_side.astype(jnp.float32)[None, :, :]
    ).astype(jnp.bfloat16)
    flat_rows = pair_tile.reshape(tile_rows * tile_cols, PAIR_CH)
    hidden = jax.nn.relu(jnp.dot(flat_rows, w_up, preferred_element_type=jnp.float32)).astype(
        jnp.bfloat16
    )
    pair_out = flat_rows.astype(jnp.float32) + jnp.dot(
        hidden, w_down, preferred_element_type=jnp.float32
    )
    pair_map = pair_out.astype(jnp.bfloat16).reshape(tile_rows, tile_cols, PAIR_CH)
    return (seq_out, pair_map)


def solution(mesh):
    return jax.shard_map(
        shards,
        mesh=mesh,
        in_specs=(
            P(("groups", "seq", "pair"), None),
            P(),
            P(None, "pair", None),
            P(),
            P(None, "pair"),
            P("pair", None),
            P(),
            P(),
            P(),
            P(),
        ),
        out_specs=(P(("groups", "seq", "pair"), None), P(("groups", "seq"), "pair", None)),
        check_vma=False,
    )
```

```python
import math

import jax
import jax.numpy as jnp
from jax import lax
from jax.sharding import PartitionSpec as P

KEY_SIZE = 128
VALUE_SIZE = 128
DILATION = 4
POOL = 16
PAIR_CH = 128


EPS = 1e-06


def padded_2(value, sides, width):
    for axis, dim in sides:
        peers, length = (lax.axis_size(axis), value.shape[dim])
        up = [(i, (i + 1) % peers) for i in range(peers - 1)]
        down = [(j, i) for i, j in up]
        last = lax.slice_in_dim(value, length - width, length, axis=dim)
        first = lax.slice_in_dim(value, 0, width, axis=dim)
        before = lax.ppermute(last, axis, up)
        after = lax.ppermute(first, axis, down)
        value = jnp.concatenate([before, value, after], axis=dim)
    return value


def norm_rows(values, gain):
    return values * lax.rsqrt(jnp.mean(values * values, axis=-1, keepdims=True) + EPS) * gain


def conv_rows(padded, conv_weight, row_total):
    summed = jnp.zeros((row_total, conv_weight.shape[2]), jnp.float32)
    for offset in range(conv_weight.shape[0]):
        shifted = lax.dynamic_slice_in_dim(padded, offset * DILATION, row_total, 0)
        summed = summed + jnp.dot(shifted, conv_weight[offset], preferred_element_type=jnp.float32)
    return summed


def direct_reduce_scatter(partial, axis):
    n = lax.axis_size(axis)
    me = lax.axis_index(axis)
    rows = partial.shape[0] // n
    blocks = partial.reshape(n, rows, partial.shape[1])
    total = blocks[me]
    for shift in range(1, n):
        outgoing = blocks[(me + shift) % n].astype(jnp.bfloat16)
        incoming = lax.ppermute(outgoing, axis, [(i, (i + shift) % n) for i in range(n)])
        total = total + incoming.astype(jnp.float32)
    return total


def permute_all_to_all(value, axis):
    n = lax.axis_size(axis)
    me = lax.axis_index(axis)
    width = value.shape[1] // n
    pieces = value.reshape(value.shape[0], n, width)
    slots = jnp.zeros((n, value.shape[0], width), value.dtype)
    slots = lax.dynamic_update_index_in_dim(slots, pieces[:, me], me, 0)
    for shift in range(1, n):
        outgoing = pieces[:, (me + shift) % n]
        incoming = lax.ppermute(outgoing, axis, [(i, (i + shift) % n) for i in range(n)])
        slots = lax.dynamic_update_index_in_dim(slots, incoming, (me + n - shift) % n, 0)
    return slots.reshape(n * value.shape[0], width)


def line_flows(value, axis):
    n = lax.axis_size(axis)
    me = lax.axis_index(axis)
    right = [(i, i + 1) for i in range(n - 1)]
    left = [(i + 1, i) for i in range(n - 1)]
    flow_r, flow_l = value, value
    from_left, from_right = [], []
    for step in range(1, n):
        flow_r = lax.ppermute(flow_r, axis, right)
        flow_l = lax.ppermute(flow_l, axis, left)
        from_left.append(flow_r)
        from_right.append(flow_l)
    return [
        jnp.where(me >= shift, from_left[shift - 1], from_right[n - shift - 1])
        for shift in range(1, n)
    ]


def line_all_gather(value, axis):
    n = lax.axis_size(axis)
    me = lax.axis_index(axis)
    rows = value.shape[0]
    right = [(i, i + 1) for i in range(n - 1)]
    left = [(i + 1, i) for i in range(n - 1)]
    slots = jnp.zeros((n + 1, rows) + value.shape[1:], value.dtype)
    slots = lax.dynamic_update_index_in_dim(slots, value, me, 0)
    flow_r, flow_l = value, value
    for step in range(1, n):
        flow_r = lax.ppermute(flow_r, axis, right)
        flow_l = lax.ppermute(flow_l, axis, left)
        at_r = jnp.where(me - step >= 0, me - step, n)
        at_l = jnp.where(me + step < n, me + step, n)
        slots = lax.dynamic_update_index_in_dim(slots, flow_r, at_r, 0)
        slots = lax.dynamic_update_index_in_dim(slots, flow_l, at_l, 0)
    return slots[:n].reshape((n * rows,) + value.shape[1:])


def rows_to_heads(value, axis):
    n = lax.axis_size(axis)
    me = lax.axis_index(axis)
    rows = value.shape[0] // n
    pieces = value.reshape(n, rows, value.shape[1])
    slots = jnp.zeros((n, rows, value.shape[1]), value.dtype)
    slots = lax.dynamic_update_index_in_dim(slots, pieces[me], me, 0)
    for shift in range(1, n):
        outgoing = pieces[(me + shift) % n]
        incoming = lax.ppermute(outgoing, axis, [(i, (i + shift) % n) for i in range(n)])
        slots = lax.dynamic_update_index_in_dim(slots, incoming, (me + n - shift) % n, 0)
    return slots.transpose(1, 0, 2).reshape(rows, n * value.shape[1])


def gather_weight_rows(weight, axis, chip_axis):
    peers = lax.axis_size(chip_axis)
    if peers % 2:
        return line_all_gather(weight, axis)
    core = lax.axis_index(chip_axis) % 2
    half = weight.shape[1] // 2
    mine = lax.dynamic_slice_in_dim(weight, core * half, half, 1)
    gathered = line_all_gather(mine, axis)
    other = lax.ppermute(gathered, chip_axis, [(i, i ^ 1) for i in range(peers)])
    return jnp.where(
        core == 0,
        jnp.concatenate([gathered, other], 1),
        jnp.concatenate([other, gathered], 1),
    )


def rotated_all_gather(value, axis):
    n = lax.axis_size(axis)
    pieces = [value]
    for shift in range(1, n):
        pieces.append(lax.ppermute(value, axis, [(i, (i + shift) % n) for i in range(n)]))
    return jnp.concatenate(pieces, 0)


def direct_all_gather(value, axis):
    n = lax.axis_size(axis)
    if n > 4:
        return line_all_gather(value, axis)
    me = lax.axis_index(axis)
    slots = jnp.zeros((n,) + value.shape, value.dtype)
    slots = lax.dynamic_update_index_in_dim(slots, value, me, 0)
    for shift in range(1, n):
        incoming = lax.ppermute(value, axis, [(i, (i + shift) % n) for i in range(n)])
        slots = lax.dynamic_update_index_in_dim(slots, incoming, (me + n - shift) % n, 0)
    return slots.reshape((n * value.shape[0],) + value.shape[1:])


def doubling_all_gather(value, axis):
    n = lax.axis_size(axis)
    assert n & (n - 1) == 0
    me = lax.axis_index(axis)
    out = value
    k = 1
    while k < n:
        other = lax.ppermute(out, axis, [(i, i ^ k) for i in range(n)])
        low = (me & k) == 0
        out = jnp.where(low, jnp.concatenate([out, other], 0), jnp.concatenate([other, out], 0))
        k *= 2
    return out


def shards(
    sequence, gain_conv, conv_weight, gain_attn, w_qkv, w_out, gain_pool, w_pair, w_up, w_down
):
    pair_count = lax.axis_size("pair")
    seq_count = lax.axis_size("seq")
    row_count = sequence.shape[0]
    channels = sequence.shape[1]
    local_rows = row_count * pair_count
    inputs = sequence.astype(jnp.float32)
    normed = norm_rows(inputs, gain_conv).astype(jnp.bfloat16)
    swapped = permute_all_to_all(normed, "pair")
    padded = padded_2(swapped, (("seq", 0),), DILATION * (conv_weight.shape[0] - 1) // 2)
    with jax.named_scope("conv_reduce"):
        summed = direct_reduce_scatter(conv_rows(padded, conv_weight, local_rows), "pair")
    first_out = (inputs + summed).astype(jnp.bfloat16)
    attn_in = norm_rows(first_out.astype(jnp.float32), gain_attn).astype(jnp.bfloat16)
    with jax.named_scope("attn_in_gather"):
        rotated = pair_count <= 4
        if rotated:
            block_in = rotated_all_gather(attn_in, "pair")
        else:
            block_in = direct_all_gather(attn_in, "pair")
    projected = jnp.dot(block_in, w_qkv, preferred_element_type=jnp.float32).astype(jnp.bfloat16)
    head_count = projected.shape[1] // (2 * KEY_SIZE + VALUE_SIZE)
    grouped = projected.reshape(local_rows, head_count, 2 * KEY_SIZE + VALUE_SIZE).transpose(1, 0, 2)
    queries = grouped[:, :, :KEY_SIZE]
    kv = grouped[:, :, KEY_SIZE:]
    if rotated and seq_count % 2 == 0:
        late_w_out, kv = lax.optimization_barrier((w_out, kv))
    scale = 1.0 / math.sqrt(KEY_SIZE)

    def attend(state, kv_block):
        running_max, running_sum, weighted = state
        key_block = kv_block[:, :, :KEY_SIZE]
        value_block = kv_block[:, :, KEY_SIZE:]
        scores = (
            jnp.einsum("hqd,hkd->hqk", queries, key_block, preferred_element_type=jnp.float32)
            * scale
        )
        new_max = jnp.maximum(running_max, jnp.max(scores, axis=-1))
        shrink = jnp.exp(running_max - new_max)
        weights = jnp.exp(scores - new_max[:, :, None])
        running_sum = running_sum * shrink + jnp.sum(weights, axis=-1)
        update = jnp.einsum(
            "hqk,hkd->hqd",
            weights.astype(jnp.bfloat16),
            value_block,
            preferred_element_type=jnp.float32,
        )
        weighted = weighted * shrink[:, :, None] + update
        return (new_max, running_sum, weighted)

    state = (
        jnp.full((head_count, local_rows), -1e30, jnp.float32),
        jnp.zeros((head_count, local_rows), jnp.float32),
        jnp.zeros((head_count, local_rows, VALUE_SIZE), jnp.float32),
    )
    with jax.named_scope("kv_ring"):
        forward = [(i, (i + 1) % seq_count) for i in range(seq_count)]
        backward = [((i + 1) % seq_count, i) for i in range(seq_count)]
        half = local_rows // 2
        going = kv[:, :half]
        coming = kv[:, half:]
        for step in range(seq_count):
            if step + 1 < seq_count:
                next_going = lax.ppermute(going, "seq", forward)
                next_coming = lax.ppermute(coming, "seq", backward)
            state = attend(state, going)
            state = attend(state, coming)
            if step + 1 < seq_count:
                going, coming = next_going, next_coming
    running_max, running_sum, weighted = state
    attended = (weighted / running_sum[:, :, None]).astype(jnp.bfloat16)
    attended = attended.transpose(1, 0, 2).reshape(local_rows, head_count * VALUE_SIZE)
    with jax.named_scope("out_projection"):
        if rotated and seq_count % 2 == 0:
            me = lax.axis_index("pair")
            core = lax.axis_index("seq") % 2
            ways = []
            for s_i in range(seq_count):
                for p_i in range(pair_count):
                    src = s_i * pair_count + p_i
                    if s_i % 2 == 0 and p_i + 1 < pair_count:
                        ways.append((src, src + 1))
                    if s_i % 2 == 1 and p_i > 0:
                        ways.append((src, src - 1))
            flow = late_w_out
            received = []
            for step in range(1, pair_count):
                flow = lax.ppermute(flow, ("seq", "pair"), ways)
                received.append(flow)
            received = jnp.stack(received)
            swapped_w = lax.ppermute(received, "seq", [(i, i ^ 1) for i in range(seq_count)])
            from_left = jnp.where(core == 0, received, swapped_w)
            from_right = jnp.where(core == 0, swapped_w, received)
            pieces = attended.reshape(pair_count, row_count, attended.shape[1])
            mixed = jnp.dot(pieces[0], late_w_out, preferred_element_type=jnp.float32)
            for shift in range(1, pair_count):
                incoming = lax.ppermute(
                    pieces[pair_count - shift],
                    "pair",
                    [(i, (i + shift) % pair_count) for i in range(pair_count)],
                )
                block = jnp.where(
                    me >= shift, from_left[shift - 1], from_right[pair_count - shift - 1]
                )
                mixed = mixed + jnp.dot(incoming, block, preferred_element_type=jnp.float32)
        else:
            late_w_out, unused = lax.optimization_barrier((w_out, kv))
            full_w_out = gather_weight_rows(late_w_out, "pair", "seq")
            own_heads = rows_to_heads(attended, "pair")
            mixed = jnp.dot(own_heads, full_w_out, preferred_element_type=jnp.float32)
    seq_out = (first_out.astype(jnp.float32) + mixed).astype(jnp.bfloat16)
    bin_count = row_count // POOL
    pooled = jnp.mean(seq_out.astype(jnp.float32).reshape(bin_count, POOL, channels), axis=1)
    bin_norm = norm_rows(pooled, gain_pool).astype(jnp.bfloat16)
    sides = jnp.dot(bin_norm, w_pair, preferred_element_type=jnp.float32).astype(jnp.bfloat16)
    with jax.named_scope("sides_gather"):
        if seq_count > 4:
            all_sides = doubling_all_gather(doubling_all_gather(sides, "pair"), "seq")
        else:
            all_sides = direct_all_gather(direct_all_gather(sides, "pair"), "seq")
    tile_rows = bin_count * pair_count
    tile_cols = bin_count * seq_count
    row_side = lax.dynamic_slice_in_dim(
        all_sides, lax.axis_index("seq") * tile_rows, tile_rows, 0
    )[:, :PAIR_CH]
    column_side = lax.dynamic_slice_in_dim(
        all_sides, lax.axis_index("pair") * tile_cols, tile_cols, 0
    )[:, PAIR_CH:]
    pair_tile = (
        row_side.astype(jnp.float32)[:, None, :] * column_side.astype(jnp.float32)[None, :, :]
    ).astype(jnp.bfloat16)
    flat_rows = pair_tile.reshape(tile_rows * tile_cols, PAIR_CH)
    hidden = jax.nn.relu(jnp.dot(flat_rows, w_up, preferred_element_type=jnp.float32)).astype(
        jnp.bfloat16
    )
    pair_out = flat_rows.astype(jnp.float32) + jnp.dot(
        hidden, w_down, preferred_element_type=jnp.float32
    )
    pair_map = pair_out.astype(jnp.bfloat16).reshape(tile_rows, tile_cols, PAIR_CH)
    return (seq_out, pair_map)


def solution(mesh):
    return jax.shard_map(
        shards,
        mesh=mesh,
        in_specs=(
            P(("groups", "seq", "pair"), None),
            P(),
            P(None, "pair", None),
            P(),
            P(None, "pair"),
            P("pair", None),
            P(),
            P(),
            P(),
            P(),
        ),
        out_specs=(P(("groups", "seq", "pair"), None), P(("groups", "seq"), "pair", None)),
        check_vma=False,
    )
```

```python
import math

import jax
import jax.numpy as jnp
from jax import lax
from jax.sharding import PartitionSpec as P

KEY_SIZE = 128
VALUE_SIZE = 128
DILATION = 4
POOL = 16
PAIR_CH = 128


EPS = 1e-06


def padded_2(value, sides, width):
    for axis, dim in sides:
        peers, length = (lax.axis_size(axis), value.shape[dim])
        up = [(i, (i + 1) % peers) for i in range(peers - 1)]
        down = [(j, i) for i, j in up]
        last = lax.slice_in_dim(value, length - width, length, axis=dim)
        first = lax.slice_in_dim(value, 0, width, axis=dim)
        before = lax.ppermute(last, axis, up)
        after = lax.ppermute(first, axis, down)
        value = jnp.concatenate([before, value, after], axis=dim)
    return value


def norm_rows(values, gain):
    return values * lax.rsqrt(jnp.mean(values * values, axis=-1, keepdims=True) + EPS) * gain


def conv_rows(padded, conv_weight, row_total):
    summed = jnp.zeros((row_total, conv_weight.shape[2]), jnp.float32)
    for offset in range(conv_weight.shape[0]):
        shifted = lax.dynamic_slice_in_dim(padded, offset * DILATION, row_total, 0)
        summed = summed + jnp.dot(shifted, conv_weight[offset], preferred_element_type=jnp.float32)
    return summed


def direct_reduce_scatter(partial, axis):
    n = lax.axis_size(axis)
    me = lax.axis_index(axis)
    rows = partial.shape[0] // n
    blocks = partial.reshape(n, rows, partial.shape[1])
    total = blocks[me]
    for shift in range(1, n):
        outgoing = blocks[(me + shift) % n].astype(jnp.bfloat16)
        incoming = lax.ppermute(outgoing, axis, [(i, (i + shift) % n) for i in range(n)])
        total = total + incoming.astype(jnp.float32)
    return total


def permute_all_to_all(value, axis):
    n = lax.axis_size(axis)
    me = lax.axis_index(axis)
    width = value.shape[1] // n
    pieces = value.reshape(value.shape[0], n, width)
    slots = jnp.zeros((n, value.shape[0], width), value.dtype)
    slots = lax.dynamic_update_index_in_dim(slots, pieces[:, me], me, 0)
    for shift in range(1, n):
        outgoing = pieces[:, (me + shift) % n]
        incoming = lax.ppermute(outgoing, axis, [(i, (i + shift) % n) for i in range(n)])
        slots = lax.dynamic_update_index_in_dim(slots, incoming, (me + n - shift) % n, 0)
    return slots.reshape(n * value.shape[0], width)


def line_flows(value, axis):
    n = lax.axis_size(axis)
    me = lax.axis_index(axis)
    right = [(i, i + 1) for i in range(n - 1)]
    left = [(i + 1, i) for i in range(n - 1)]
    flow_r, flow_l = value, value
    from_left, from_right = [], []
    for step in range(1, n):
        flow_r = lax.ppermute(flow_r, axis, right)
        flow_l = lax.ppermute(flow_l, axis, left)
        from_left.append(flow_r)
        from_right.append(flow_l)
    return [
        jnp.where(me >= shift, from_left[shift - 1], from_right[n - shift - 1])
        for shift in range(1, n)
    ]


def line_all_gather(value, axis):
    n = lax.axis_size(axis)
    me = lax.axis_index(axis)
    rows = value.shape[0]
    right = [(i, i + 1) for i in range(n - 1)]
    left = [(i + 1, i) for i in range(n - 1)]
    slots = jnp.zeros((n + 1, rows) + value.shape[1:], value.dtype)
    slots = lax.dynamic_update_index_in_dim(slots, value, me, 0)
    flow_r, flow_l = value, value
    for step in range(1, n):
        flow_r = lax.ppermute(flow_r, axis, right)
        flow_l = lax.ppermute(flow_l, axis, left)
        at_r = jnp.where(me - step >= 0, me - step, n)
        at_l = jnp.where(me + step < n, me + step, n)
        slots = lax.dynamic_update_index_in_dim(slots, flow_r, at_r, 0)
        slots = lax.dynamic_update_index_in_dim(slots, flow_l, at_l, 0)
    return slots[:n].reshape((n * rows,) + value.shape[1:])


def rows_to_heads(value, axis):
    n = lax.axis_size(axis)
    me = lax.axis_index(axis)
    rows = value.shape[0] // n
    pieces = value.reshape(n, rows, value.shape[1])
    slots = jnp.zeros((n, rows, value.shape[1]), value.dtype)
    slots = lax.dynamic_update_index_in_dim(slots, pieces[me], me, 0)
    for shift in range(1, n):
        outgoing = pieces[(me + shift) % n]
        incoming = lax.ppermute(outgoing, axis, [(i, (i + shift) % n) for i in range(n)])
        slots = lax.dynamic_update_index_in_dim(slots, incoming, (me + n - shift) % n, 0)
    return slots.transpose(1, 0, 2).reshape(rows, n * value.shape[1])


def gather_weight_rows(weight, axis, chip_axis):
    peers = lax.axis_size(chip_axis)
    if peers % 2:
        return line_all_gather(weight, axis)
    core = lax.axis_index(chip_axis) % 2
    half = weight.shape[1] // 2
    mine = lax.dynamic_slice_in_dim(weight, core * half, half, 1)
    gathered = line_all_gather(mine, axis)
    other = lax.ppermute(gathered, chip_axis, [(i, i ^ 1) for i in range(peers)])
    return jnp.where(
        core == 0,
        jnp.concatenate([gathered, other], 1),
        jnp.concatenate([other, gathered], 1),
    )


def rotated_all_gather(value, axis):
    n = lax.axis_size(axis)
    pieces = [value]
    for shift in range(1, n):
        pieces.append(lax.ppermute(value, axis, [(i, (i + shift) % n) for i in range(n)]))
    return jnp.concatenate(pieces, 0)


def direct_all_gather(value, axis):
    n = lax.axis_size(axis)
    if n > 4:
        return line_all_gather(value, axis)
    me = lax.axis_index(axis)
    slots = jnp.zeros((n,) + value.shape, value.dtype)
    slots = lax.dynamic_update_index_in_dim(slots, value, me, 0)
    for shift in range(1, n):
        incoming = lax.ppermute(value, axis, [(i, (i + shift) % n) for i in range(n)])
        slots = lax.dynamic_update_index_in_dim(slots, incoming, (me + n - shift) % n, 0)
    return slots.reshape((n * value.shape[0],) + value.shape[1:])


def doubling_all_gather(value, axis):
    n = lax.axis_size(axis)
    assert n & (n - 1) == 0
    me = lax.axis_index(axis)
    out = value
    k = 1
    while k < n:
        other = lax.ppermute(out, axis, [(i, i ^ k) for i in range(n)])
        low = (me & k) == 0
        out = jnp.where(low, jnp.concatenate([out, other], 0), jnp.concatenate([other, out], 0))
        k *= 2
    return out


def shards(
    sequence, gain_conv, conv_weight, gain_attn, w_qkv, w_out, gain_pool, w_pair, w_up, w_down
):
    pair_count = lax.axis_size("pair")
    seq_count = lax.axis_size("seq")
    row_count = sequence.shape[0]
    channels = sequence.shape[1]
    local_rows = row_count * pair_count
    inputs = sequence.astype(jnp.float32)
    normed = norm_rows(inputs, gain_conv).astype(jnp.bfloat16)
    swapped = permute_all_to_all(normed, "pair")
    padded = padded_2(swapped, (("seq", 0),), DILATION * (conv_weight.shape[0] - 1) // 2)
    with jax.named_scope("conv_reduce"):
        summed = direct_reduce_scatter(conv_rows(padded, conv_weight, local_rows), "pair")
    first_out = (inputs + summed).astype(jnp.bfloat16)
    attn_in = norm_rows(first_out.astype(jnp.float32), gain_attn).astype(jnp.bfloat16)
    with jax.named_scope("attn_in_gather"):
        rotated = pair_count <= 4
        if rotated:
            block_in = rotated_all_gather(attn_in, "pair")
        else:
            block_in = direct_all_gather(attn_in, "pair")
    projected = jnp.dot(block_in, w_qkv, preferred_element_type=jnp.float32).astype(jnp.bfloat16)
    head_count = projected.shape[1] // (2 * KEY_SIZE + VALUE_SIZE)
    grouped = projected.reshape(local_rows, head_count, 2 * KEY_SIZE + VALUE_SIZE).transpose(1, 0, 2)
    queries = grouped[:, :, :KEY_SIZE]
    kv = grouped[:, :, KEY_SIZE:]
    scale = 1.0 / math.sqrt(KEY_SIZE)

    def attend(state, kv_block):
        running_max, running_sum, weighted = state
        key_block = kv_block[:, :, :KEY_SIZE]
        value_block = kv_block[:, :, KEY_SIZE:]
        scores = (
            jnp.einsum("hqd,hkd->hqk", queries, key_block, preferred_element_type=jnp.float32)
            * scale
        )
        new_max = jnp.maximum(running_max, jnp.max(scores, axis=-1))
        shrink = jnp.exp(running_max - new_max)
        weights = jnp.exp(scores - new_max[:, :, None])
        running_sum = running_sum * shrink + jnp.sum(weights, axis=-1)
        update = jnp.einsum(
            "hqk,hkd->hqd",
            weights.astype(jnp.bfloat16),
            value_block,
            preferred_element_type=jnp.float32,
        )
        weighted = weighted * shrink[:, :, None] + update
        return (new_max, running_sum, weighted)

    state = (
        jnp.full((head_count, local_rows), -1e30, jnp.float32),
        jnp.zeros((head_count, local_rows), jnp.float32),
        jnp.zeros((head_count, local_rows, VALUE_SIZE), jnp.float32),
    )
    with jax.named_scope("kv_ring"):
        forward = [(i, (i + 1) % seq_count) for i in range(seq_count)]
        backward = [((i + 1) % seq_count, i) for i in range(seq_count)]
        half = local_rows // 2
        going = kv[:, :half]
        coming = kv[:, half:]
        for step in range(seq_count):
            if step + 1 < seq_count:
                next_going = lax.ppermute(going, "seq", forward)
                next_coming = lax.ppermute(coming, "seq", backward)
            state = attend(state, going)
            state = attend(state, coming)
            if step + 1 < seq_count:
                going, coming = next_going, next_coming
    running_max, running_sum, weighted = state
    attended = (weighted / running_sum[:, :, None]).astype(jnp.bfloat16)
    attended = attended.transpose(1, 0, 2).reshape(local_rows, head_count * VALUE_SIZE)
    with jax.named_scope("out_projection"):
        late_w_out, unused = lax.optimization_barrier((w_out, kv))
        if rotated and seq_count % 2 == 0:
            me = lax.axis_index("pair")
            core = lax.axis_index("seq") % 2
            ways = []
            for s_i in range(seq_count):
                for p_i in range(pair_count):
                    src = s_i * pair_count + p_i
                    if s_i % 2 == 0 and p_i + 1 < pair_count:
                        ways.append((src, src + 1))
                    if s_i % 2 == 1 and p_i > 0:
                        ways.append((src, src - 1))
            flow = late_w_out
            received = []
            for step in range(1, pair_count):
                flow = lax.ppermute(flow, ("seq", "pair"), ways)
                received.append(flow)
            received = jnp.stack(received)
            swapped_w = lax.ppermute(received, "seq", [(i, i ^ 1) for i in range(seq_count)])
            pieces = attended.reshape(pair_count, row_count, attended.shape[1])
            mixed = jnp.dot(pieces[0], late_w_out, preferred_element_type=jnp.float32)
            for shift in range(1, pair_count):
                incoming = lax.ppermute(
                    pieces[pair_count - shift],
                    "pair",
                    [(i, (i + shift) % pair_count) for i in range(pair_count)],
                )
                near = shift - 1
                far = pair_count - shift - 1
                block = jnp.where(
                    me >= shift,
                    jnp.where(core == 0, received[near], swapped_w[near]),
                    jnp.where(core == 0, swapped_w[far], received[far]),
                )
                mixed = mixed + jnp.dot(incoming, block, preferred_element_type=jnp.float32)
        else:
            full_w_out = gather_weight_rows(late_w_out, "pair", "seq")
            own_heads = rows_to_heads(attended, "pair")
            mixed = jnp.dot(own_heads, full_w_out, preferred_element_type=jnp.float32)
    seq_out = (first_out.astype(jnp.float32) + mixed).astype(jnp.bfloat16)
    bin_count = row_count // POOL
    pooled = jnp.mean(seq_out.astype(jnp.float32).reshape(bin_count, POOL, channels), axis=1)
    bin_norm = norm_rows(pooled, gain_pool).astype(jnp.bfloat16)
    sides = jnp.dot(bin_norm, w_pair, preferred_element_type=jnp.float32).astype(jnp.bfloat16)
    with jax.named_scope("sides_gather"):
        if seq_count > 4:
            all_sides = doubling_all_gather(doubling_all_gather(sides, "pair"), "seq")
        else:
            all_sides = direct_all_gather(direct_all_gather(sides, "pair"), "seq")
    tile_rows = bin_count * pair_count
    tile_cols = bin_count * seq_count
    row_side = lax.dynamic_slice_in_dim(
        all_sides, lax.axis_index("seq") * tile_rows, tile_rows, 0
    )[:, :PAIR_CH]
    column_side = lax.dynamic_slice_in_dim(
        all_sides, lax.axis_index("pair") * tile_cols, tile_cols, 0
    )[:, PAIR_CH:]
    pair_tile = (
        row_side.astype(jnp.float32)[:, None, :] * column_side.astype(jnp.float32)[None, :, :]
    ).astype(jnp.bfloat16)
    flat_rows = pair_tile.reshape(tile_rows * tile_cols, PAIR_CH)
    hidden = jax.nn.relu(jnp.dot(flat_rows, w_up, preferred_element_type=jnp.float32)).astype(
        jnp.bfloat16
    )
    pair_out = flat_rows.astype(jnp.float32) + jnp.dot(
        hidden, w_down, preferred_element_type=jnp.float32
    )
    pair_map = pair_out.astype(jnp.bfloat16).reshape(tile_rows, tile_cols, PAIR_CH)
    return (seq_out, pair_map)


def solution(mesh):
    return jax.shard_map(
        shards,
        mesh=mesh,
        in_specs=(
            P(("groups", "seq", "pair"), None),
            P(),
            P(None, "pair", None),
            P(),
            P(None, "pair"),
            P("pair", None),
            P(),
            P(),
            P(),
            P(),
        ),
        out_specs=(P(("groups", "seq", "pair"), None), P(("groups", "seq"), "pair", None)),
        check_vma=False,
    )
```
